256 devices in a mesh: chord: 4 (over y), span: 16 (over z, x_lo), wall: 4 (over x_hi, core).
Axes of the slice: x: 4 (x_hi: 2, x_lo: 2; x = x_hi * 2 + x_lo), y: 4, z: 8, core: 2. Of those that a mesh axis runs over, the one named last changes fastest.
Arguments:
- sensitivity: float32 [6, 32, 256, 512], P(None, 'chord', 'span', 'wall'), may hold values from -6 to 6
- diagonal: float32 [6, 32, 256, 512], P(None, 'chord', 'span', 'wall'), may hold values from 10 to 20
- face_coef: float32 [3, 32, 256, 512], P(None, 'chord', 'span', 'wall'), may hold values from 0.3 to 1.5
- upper_blocks: float32 [3, 6, 6], replicated, may hold values from -2.5 to 2.5
- lower_blocks: float32 [3, 6, 6], replicated, may hold values from -2.5 to 2.5
- iface_blocks: float32 [2, 6, 6], replicated, may hold values from -2.5 to 2.5
- production: float32 [32, 256, 512], P('chord', 'span', 'wall'), may hold values from -6 to 6
- send_cell: int32 [4, 16, 4, 16, 64], P('chord', 'span', 'wall'), may hold values from 0 to 16383
- target_cell: int32 [4, 16, 4, 16, 64], P('chord', 'span', 'wall'), may hold values from 0 to 16383
- orient: int32 [4, 16, 4, 16, 64], P('chord', 'span', 'wall'), may hold values from 0 to 1
- iface_weight: float32 [4, 16, 4, 16, 64], P('chord', 'span', 'wall'), may hold values from 0.5 to 2
Outputs:
- adjoint: float32 [6, 32, 256, 512], P(None, 'chord', 'span', 'wall')
- gradient: float32 [32, 256, 512], P('chord', 'span', 'wall')
The draws below stay inside these ranges and needn't reach their ends.
All inputs are finite; a program needn't handle non-finite values.
Results may differ from the reference program's by a relative error of at most 0.0001.
Values sent between devices are 32-bit elements; how exact they have to be, the bound alone decides.
No kernel may reach another device: no remote copies, remote signals or barrier semaphores. Data moves between devices by JAX's collectives and lax.ppermute only.
A program may use at most 64 MiB of HBM per device.

```python
import math
import jax
import jax.numpy as jnp
from jax import lax

NV = 6
CX = 8
CY = 16
CZ = 128
CAP = 64
SWEEPS = 3
NX = 32
NY = 256
NZ = 512
CELLS = 16384
N_CHORD = 4
N_SPAN = 16
N_WALL = 4


def set_ends(values, stream_key, least, largest):
    shape = values.shape
    place = [jax.random.randint(jax.random.fold_in(stream_key, axis), (), 0, shape[axis]) for axis in range(len(shape))]
    values = values.at[tuple(place)].set(least)
    longest = shape.index(max(shape))
    place[longest] = (place[longest] + 1) % shape[longest]
    return values.at[tuple(place)].set(largest)


def level_of(rng, dims, shards, low, top_value):
    def one(position, shards_of):
        draws = jax.random.uniform(jax.random.fold_in(jax.random.fold_in(rng, 6), position), (shards_of,), jnp.float32, low / len(shards), top_value / len(shards))
        return jnp.repeat(jnp.exp(draws), dims[position] // shards_of).reshape((-1,) + (1,) * (len(dims) - position - 1))

    level = one(*shards[0])
    for cut in shards[1:]:
        level = level * one(*cut)
    return level


def gaussian(own_key, shape, deviation, limit, cuts=(), held_as=jnp.bfloat16):
    loudness = level_of(own_key, shape, cuts, -0.22, 0.18) if cuts else 1.0
    values = jax.random.normal(own_key, shape, jnp.float32) * deviation * loudness
    return jnp.minimum(jnp.maximum(values, -limit), limit).astype(held_as)


def setup_inputs(seed: int = 0) -> dict:
    key_of = jax.random.split(jax.random.key(seed), 12)
    sensitivity = gaussian(key_of[0], (NV, NX, NY, NZ), 1.0, 6.0, ((1, 4), (2, 16), (3, 4)), jnp.float32)
    diagonal = jnp.clip(jnp.exp(math.log(20.0) - 0.6931472 * jax.random.uniform(key_of[1], (NV, NX, NY, NZ), jnp.float32) ** level_of(key_of[1], (NV, NX, NY, NZ), ((1, 4), (2, 16), (3, 4)), -0.2, 0.2)), 10.0, 20.0)
    face_coef = jnp.clip(0.3 + 1.2 * jax.random.uniform(key_of[2], (3, NX, NY, NZ), jnp.float32) ** level_of(key_of[2], (3, NX, NY, NZ), ((1, 4), (2, 16), (3, 4)), -0.2, 0.2), 0.3, 1.5)
    upper_blocks = gaussian(key_of[3], (3, NV, NV), NV ** -0.5, 2.5, (), jnp.float32)
    lower_blocks = gaussian(key_of[4], (3, NV, NV), NV ** -0.5, 2.5, (), jnp.float32)
    iface_blocks = gaussian(key_of[5], (2, NV, NV), NV ** -0.5, 2.5, (), jnp.float32)
    production = gaussian(key_of[6], (NX, NY, NZ), 1.0, 6.0, ((0, 4), (1, 16), (2, 4)), jnp.float32)
    send_cell = set_ends(jax.random.randint(key_of[7], (N_CHORD, N_SPAN, N_WALL, N_SPAN, CAP), 0, CELLS), jax.random.fold_in(key_of[7], 1), 0, CELLS - 1).astype(jnp.int32)
    target_cell = set_ends(jax.random.randint(key_of[8], (N_CHORD, N_SPAN, N_WALL, N_SPAN, CAP), 0, CELLS), jax.random.fold_in(key_of[8], 1), 0, CELLS - 1).astype(jnp.int32)
    orient = set_ends(jax.random.randint(key_of[9], (N_CHORD, N_SPAN, N_WALL, N_SPAN, CAP), 0, 2), jax.random.fold_in(key_of[9], 1), 0, 1).astype(jnp.int32)
    iface_weight = jnp.clip(jnp.exp(math.log(2.0) - 1.3862944 * jax.random.uniform(key_of[10], (N_CHORD, N_SPAN, N_WALL, N_SPAN, CAP), jnp.float32) ** level_of(key_of[10], (N_CHORD, N_SPAN, N_WALL, N_SPAN, CAP), ((0, 4), (1, 16), (2, 4)), -0.2, 0.2)), 0.5, 2.0)
    return dict(sensitivity=sensitivity, diagonal=diagonal, face_coef=face_coef, upper_blocks=upper_blocks, lower_blocks=lower_blocks, iface_blocks=iface_blocks, production=production, send_cell=send_cell, target_cell=target_cell, orient=orient, iface_weight=iface_weight)


def couple(block, field):
    return jnp.einsum('ji,jxyz->ixyz', block, field, precision=lax.Precision.HIGHEST)


def local_part(adjoint, diagonal, face_coef, upper_blocks, lower_blocks):
    padded = jnp.pad(adjoint, ((0, 0), (1, 1), (1, 1), (1, 1)))
    pairs = [(padded[:, 2:, 1:-1, 1:-1], padded[:, :-2, 1:-1, 1:-1]),
             (padded[:, 1:-1, 2:, 1:-1], padded[:, 1:-1, :-2, 1:-1]),
             (padded[:, 1:-1, 1:-1, 2:], padded[:, 1:-1, 1:-1, :-2])]
    result = diagonal * adjoint
    for axis_num in range(3):
        upper, lower = pairs[axis_num]
        result = result + face_coef[axis_num][None] * (couple(upper_blocks[axis_num], upper) + couple(lower_blocks[axis_num], lower))
    return result


def iface_part(adjoint, send_cell, target_cell, orient, iface_weight, iface_blocks):
    n_c, n_s, n_w = N_CHORD, N_SPAN, N_WALL
    cells = CX * CY * CZ
    blocks = adjoint.reshape(NV, n_c, CX, n_s, CY, n_w, CZ).transpose(0, 1, 3, 5, 2, 4, 6).reshape(NV, n_c, n_s, n_w, cells)
    source = jnp.take_along_axis(blocks, send_cell.reshape(1, n_c, n_s, n_w, n_s * CAP), axis=4).reshape(NV, n_c, n_s, n_w, n_s, CAP)
    first = jnp.einsum('ji,jabcdk->iabcdk', iface_blocks[0], source, precision=lax.Precision.HIGHEST)
    second = jnp.einsum('ji,jabcdk->iabcdk', iface_blocks[1], source, precision=lax.Precision.HIGHEST)
    values = jnp.where(orient[None] == 1, second, first) * iface_weight[None]
    shape = (n_c, n_s, n_w, n_s, CAP)
    chord_idx = lax.broadcasted_iota(jnp.int32, shape, 0)
    dest_idx = lax.broadcasted_iota(jnp.int32, shape, 3)
    wall_idx = lax.broadcasted_iota(jnp.int32, shape, 2)
    total = jnp.zeros((NV, n_c, n_s, n_w, cells), jnp.float32)
    total = total.at[:, chord_idx, dest_idx, wall_idx, target_cell.astype(jnp.int32)].add(values)
    return total.reshape(NV, n_c, n_s, n_w, CX, CY, CZ).transpose(0, 1, 4, 2, 5, 3, 6).reshape(NV, n_c * CX, n_s * CY, n_w * CZ)


def reference(sensitivity, diagonal, face_coef, upper_blocks, lower_blocks, iface_blocks, production, send_cell, target_cell, orient, iface_weight):
    adjoint = sensitivity / diagonal
    for sweep in range(SWEEPS):
        applied = local_part(adjoint, diagonal, face_coef, upper_blocks, lower_blocks) + iface_part(adjoint, send_cell, target_cell, orient, iface_weight, iface_blocks)
        adjoint = adjoint + (sensitivity - applied) / diagonal
    gradient = production * adjoint[NV - 1]
    return adjoint, gradient
```

```python
import jax
import jax.numpy as jnp
from jax import lax
from jax.experimental import pallas as pl
from jax.experimental.pallas import tpu as pltpu
from jax.sharding import PartitionSpec as P

SWEEPS = 3
F32 = jnp.float32
BF16 = jnp.bfloat16


def split3(x):
    p1 = x.astype(BF16)
    r1 = x - p1.astype(F32)
    p2 = r1.astype(BF16)
    p3 = (r1 - p2.astype(F32)).astype(BF16)
    return p1, p2, p3


def gather_rows(adj, send_ref, orient_ref, weight_ref, blk, n_var, lanes):
    rows = adj.shape[1] * adj.shape[2]
    n_rows = send_ref.shape[1]
    cell = send_ref[...]
    row_of = cell // lanes
    lane_of = cell % lanes
    lane_hot = (lax.broadcasted_iota(jnp.int32, (lanes, n_rows), 0) == lane_of).astype(BF16)
    row_hot = (lax.broadcasted_iota(jnp.int32, (rows, n_rows), 0) == row_of).astype(F32)
    flat = adj.reshape(n_var * rows, lanes)
    picked = None
    for part in split3(flat):
        term = jnp.dot(part, lane_hot, preferred_element_type=F32)
        picked = term if picked is None else picked + term
    src = jnp.sum(picked.reshape(n_var, rows, n_rows) * row_hot[None], axis=1)
    orient = orient_ref[...]
    weight = weight_ref[...]
    out = []
    for i in range(n_var):
        first = None
        second = None
        for j in range(n_var):
            a = blk[216 + j * n_var + i] * src[j:j + 1]
            b = blk[216 + 36 + j * n_var + i] * src[j:j + 1]
            first = a if first is None else first + a
            second = b if second is None else second + b
        out.append(jnp.where(orient == 1, second, first) * weight)
    return jnp.concatenate(out, axis=0)


def write_faces(adj, faces):
    c_lo, c_hi, s_lo, s_hi, w_lo, w_hi = faces
    nx, ny, nz = adj.shape[1], adj.shape[2], adj.shape[3]
    c_lo[...] = adj[:, 0:1]
    c_hi[...] = adj[:, nx - 1:nx]
    s_lo[...] = adj[:, :, 0:1]
    s_hi[...] = adj[:, :, ny - 1:ny]
    w_lo[...] = adj[:, :, :, 0:1]
    w_hi[...] = adj[:, :, :, nz - 1:nz]


def init_kernel(blk_ref, sens_ref, diag_ref, send_ref, orient_ref, weight_ref,
                adj_ref, rows_ref, c_lo, c_hi, s_lo, s_hi, w_lo, w_hi):
    n_var = sens_ref.shape[0]
    lanes = sens_ref.shape[3]
    adj = sens_ref[...] / diag_ref[...]
    adj_ref[...] = adj
    write_faces(adj, (c_lo, c_hi, s_lo, s_hi, w_lo, w_hi))
    rows_ref[...] = gather_rows(adj, send_ref, orient_ref, weight_ref, blk_ref, n_var, lanes)


def sweep_body(blk, adj, sens, diag, face, halos, incoming, target_ref):
    n_var, nx, ny, nz = adj.shape
    rows = nx * ny
    h_c_lo, h_c_hi, h_s_lo, h_s_hi, h_w_lo, h_w_hi = halos
    j_idx = lax.broadcasted_iota(jnp.int32, adj.shape, 2)
    k_idx = lax.broadcasted_iota(jnp.int32, adj.shape, 3)
    up = [
        jnp.concatenate([adj[:, 1:], h_c_hi], axis=1),
        jnp.where(j_idx == ny - 1, h_s_hi, pltpu.roll(adj, ny - 1, 2)),
        jnp.where(k_idx == nz - 1, h_w_hi, pltpu.roll(adj, nz - 1, 3)),
    ]
    lo = [
        jnp.concatenate([h_c_lo, adj[:, :-1]], axis=1),
        jnp.where(j_idx == 0, h_s_lo, pltpu.roll(adj, 1, 2)),
        jnp.where(k_idx == 0, h_w_lo, pltpu.roll(adj, 1, 3)),
    ]
    n_rows = incoming.shape[1]
    cell = target_ref[...]
    row_of = cell // nz
    lane_of = cell % nz
    row_hot = (lax.broadcasted_iota(jnp.int32, (rows, n_rows), 0) == row_of).astype(F32)
    lane_hot = (lax.broadcasted_iota(jnp.int32, (nz, n_rows), 0) == lane_of).astype(BF16)
    coupled = None
    for part in split3(incoming):
        lhs = (row_hot[None] * part.astype(F32)[:, None, :]).astype(BF16).reshape(n_var * rows, n_rows)
        term = lax.dot_general(lhs, lane_hot, (((1,), (1,)), ((), ())), preferred_element_type=F32)
        coupled = term if coupled is None else coupled + term
    coupled = coupled.reshape(n_var, nx, ny, nz)
    new = []
    for i in range(n_var):
        applied = diag[i] * adj[i] + coupled[i]
        for d in range(3):
            acc = None
            for j in range(n_var):
                t = blk[d * 36 + j * n_var + i] * up[d][j] + blk[108 + d * 36 + j * n_var + i] * lo[d][j]
                acc = t if acc is None else acc + t
            applied = applied + face[d] * acc
        new.append(adj[i] + (sens[i] - applied) / diag[i])
    return jnp.stack(new, axis=0)


def sweep_kernel(blk_ref, adj_ref, sens_ref, diag_ref, face_ref, hcl, hch, hsl, hsh, hwl, hwh,
                 inc_ref, tgt_ref, send_ref, orient_ref, weight_ref,
                 out_ref, rows_ref, c_lo, c_hi, s_lo, s_hi, w_lo, w_hi):
    n_var = adj_ref.shape[0]
    lanes = adj_ref.shape[3]
    halos = (hcl[...], hch[...], hsl[...], hsh[...], hwl[...], hwh[...])
    new = sweep_body(blk_ref, adj_ref[...], sens_ref[...], diag_ref[...], face_ref[...], halos,
                     inc_ref[...], tgt_ref)
    out_ref[...] = new
    write_faces(new, (c_lo, c_hi, s_lo, s_hi, w_lo, w_hi))
    rows_ref[...] = gather_rows(new, send_ref, orient_ref, weight_ref, blk_ref, n_var, lanes)


def last_kernel(blk_ref, adj_ref, sens_ref, diag_ref, face_ref, hcl, hch, hsl, hsh, hwl, hwh,
                inc_ref, tgt_ref, prod_ref, out_ref, grad_ref):
    n_var = adj_ref.shape[0]
    halos = (hcl[...], hch[...], hsl[...], hsh[...], hwl[...], hwh[...])
    new = sweep_body(blk_ref, adj_ref[...], sens_ref[...], diag_ref[...], face_ref[...], halos,
                     inc_ref[...], tgt_ref)
    out_ref[...] = new
    grad_ref[...] = prod_ref[...] * new[n_var - 1]


def face_shapes(shape):
    n_var, nx, ny, nz = shape
    c = jax.ShapeDtypeStruct((n_var, 1, ny, nz), F32)
    s = jax.ShapeDtypeStruct((n_var, nx, 1, nz), F32)
    w = jax.ShapeDtypeStruct((n_var, nx, ny, 1), F32)
    return [c, c, s, s, w, w]


def exchange(faces):
    c_lo, c_hi, s_lo, s_hi, w_lo, w_hi = faces
    out = []
    for axis, lo_face, hi_face in (("chord", c_lo, c_hi), ("span", s_lo, s_hi), ("wall", w_lo, w_hi)):
        count = lax.axis_size(axis)
        forward = [(i, i + 1) for i in range(count - 1)]
        backward = [(i + 1, i) for i in range(count - 1)]
        out.append(lax.ppermute(hi_face, axis, forward))
        out.append(lax.ppermute(lo_face, axis, backward))
    return out


def local(sensitivity, diagonal, face_coef, upper_blocks, lower_blocks, iface_blocks, production,
          send_cell, target_cell, orient, iface_weight):
    n_span = lax.axis_size("span")
    n_var = sensitivity.shape[0]
    slots = send_cell.shape[-1]
    n_rows = n_span * slots
    shape = sensitivity.shape
    blk = jnp.concatenate([upper_blocks.reshape(-1), lower_blocks.reshape(-1), iface_blocks.reshape(-1)])
    send_row = send_cell.reshape(1, n_rows)
    orient_row = orient.reshape(1, n_rows)
    weight_row = iface_weight.reshape(1, n_rows)
    target_row = lax.all_to_all(
        target_cell.reshape(n_span, slots), "span", split_axis=0, concat_axis=0, tiled=True
    ).reshape(1, n_rows)

    vmem = pl.BlockSpec(memory_space=pltpu.VMEM)
    smem = pl.BlockSpec(memory_space=pltpu.SMEM)
    adj_sds = jax.ShapeDtypeStruct(shape, F32)
    rows_sds = jax.ShapeDtypeStruct((n_var, n_rows), F32)

    init = pl.pallas_call(
        init_kernel,
        out_shape=[adj_sds, rows_sds] + face_shapes(shape),
        in_specs=[smem] + [vmem] * 5,
        out_specs=[vmem] * 8,
    )
    adj, rows, *faces = init(blk, sensitivity, diagonal, send_row, orient_row, weight_row)

    step = pl.pallas_call(
        sweep_kernel,
        out_shape=[adj_sds, rows_sds] + face_shapes(shape),
        in_specs=[smem] + [vmem] * 15,
        out_specs=[vmem] * 8,
    )
    last = pl.pallas_call(
        last_kernel,
        out_shape=[adj_sds, jax.ShapeDtypeStruct(production.shape, F32)],
        in_specs=[smem] + [vmem] * 13,
        out_specs=[vmem] * 2,
    )
    for sweep in range(SWEEPS):
        halos = exchange(faces)
        incoming = lax.all_to_all(
            rows.reshape(n_var, n_span, slots), "span", split_axis=1, concat_axis=1, tiled=True
        ).reshape(n_var, n_rows)
        if sweep < SWEEPS - 1:
            adj, rows, *faces = step(blk, adj, sensitivity, diagonal, face_coef, *halos, incoming,
                                     target_row, send_row, orient_row, weight_row)
        else:
            adj, gradient = last(blk, adj, sensitivity, diagonal, face_coef, *halos, incoming,
                                 target_row, production)
    return (adj, gradient)


def solution(mesh):
    placed = (
        P(None, "chord", "span", "wall"),
        P(None, "chord", "span", "wall"),
        P(None, "chord", "span", "wall"),
        P(),
        P(),
        P(),
        P("chord", "span", "wall"),
        P("chord", "span", "wall", None, None),
        P("chord", "span", "wall", None, None),
        P("chord", "span", "wall", None, None),
        P("chord", "span", "wall", None, None),
    )
    return jax.shard_map(
        local,
        mesh=mesh,
        in_specs=placed,
        out_specs=(P(None, "chord", "span", "wall"), P("chord", "span", "wall")),
        check_vma=False,
    )
```

```python
import jax
import jax.numpy as jnp
from jax import lax
from jax.experimental import pallas as pl
from jax.experimental.pallas import tpu as pltpu
from jax.sharding import PartitionSpec as P

SWEEPS = 3
F32 = jnp.float32
BF16 = jnp.bfloat16


def split3(x):
    p1 = x.astype(BF16)
    r1 = x - p1.astype(F32)
    p2 = r1.astype(BF16)
    p3 = (r1 - p2.astype(F32)).astype(BF16)
    return p1, p2, p3


def gather_rows(adj, send_ref, orient_ref, weight_ref, blk, n_var, lanes):
    rows = adj.shape[1] * adj.shape[2]
    n_rows = send_ref.shape[1]
    cell = send_ref[...]
    row_of = cell // lanes
    lane_of = cell % lanes
    lane_hot = (lax.broadcasted_iota(jnp.int32, (lanes, n_rows), 0) == lane_of).astype(BF16)
    row_hot = (lax.broadcasted_iota(jnp.int32, (rows, n_rows), 0) == row_of).astype(F32)
    flat = adj.reshape(n_var * rows, lanes)
    picked = None
    for part in split3(flat):
        term = jnp.dot(part, lane_hot, preferred_element_type=F32)
        picked = term if picked is None else picked + term
    src = jnp.sum(picked.reshape(n_var, rows, n_rows) * row_hot[None], axis=1)
    orient = orient_ref[...]
    weight = weight_ref[...]
    out = []
    for i in range(n_var):
        first = None
        second = None
        for j in range(n_var):
            a = blk[216 + j * n_var + i] * src[j:j + 1]
            b = blk[216 + 36 + j * n_var + i] * src[j:j + 1]
            first = a if first is None else first + a
            second = b if second is None else second + b
        out.append(jnp.where(orient == 1, second, first) * weight)
    return jnp.concatenate(out, axis=0)


def wall_columns(adj):
    n_var, nx, ny, nz = adj.shape
    lo, hi = [], []
    for v in range(n_var):
        t = adj[v].reshape(nx * ny, nz).T
        lo.append(t[0:1])
        hi.append(t[nz - 1:nz])
    return jnp.concatenate(lo, axis=0), jnp.concatenate(hi, axis=0)


def write_faces(adj, faces):
    c_lo, c_hi, s_lo, s_hi, w_lo, w_hi = faces
    nx, ny, nz = adj.shape[1], adj.shape[2], adj.shape[3]
    j_idx = lax.broadcasted_iota(jnp.int32, adj.shape, 2)
    c_lo[...] = adj[:, 0:1]
    c_hi[...] = adj[:, nx - 1:nx]
    s_lo[...] = jnp.sum(jnp.where(j_idx == 0, adj, 0.0), axis=2)
    s_hi[...] = jnp.sum(jnp.where(j_idx == ny - 1, adj, 0.0), axis=2)
    lo, hi = wall_columns(adj)
    w_lo[...] = lo
    w_hi[...] = hi


def init_kernel(blk_ref, sens_ref, diag_ref, send_ref, orient_ref, weight_ref,
                adj_ref, rows_ref, c_lo, c_hi, s_lo, s_hi, w_lo, w_hi):
    n_var = sens_ref.shape[0]
    lanes = sens_ref.shape[3]
    adj = sens_ref[...] / diag_ref[...]
    adj_ref[...] = adj
    write_faces(adj, (c_lo, c_hi, s_lo, s_hi, w_lo, w_hi))
    rows_ref[...] = gather_rows(adj, send_ref, orient_ref, weight_ref, blk_ref, n_var, lanes)


def sweep_body(blk, adj, sens, diag, face, halos, incoming, target_ref):
    n_var, nx, ny, nz = adj.shape
    rows = nx * ny
    h_c_lo, h_c_hi, h_s_lo, h_s_hi, h_w_lo, h_w_hi = halos
    j_idx = lax.broadcasted_iota(jnp.int32, adj.shape, 2)
    k_idx = lax.broadcasted_iota(jnp.int32, adj.shape, 3)
    kk = lax.broadcasted_iota(jnp.int32, (nz, rows), 0)
    wall = []
    for v in range(n_var):
        z = jnp.where(kk == 0, h_w_lo[v:v + 1], jnp.where(kk == nz - 1, h_w_hi[v:v + 1], 0.0))
        wall.append(z.T.reshape(nx, ny, nz))
    wall = jnp.stack(wall, axis=0)
    up = [
        jnp.concatenate([adj[:, 1:], h_c_hi], axis=1),
        jnp.where(j_idx == ny - 1, h_s_hi[:, :, None, :], pltpu.roll(adj, ny - 1, 2)),
        jnp.where(k_idx == nz - 1, wall, pltpu.roll(adj, nz - 1, 3)),
    ]
    lo = [
        jnp.concatenate([h_c_lo, adj[:, :-1]], axis=1),
        jnp.where(j_idx == 0, h_s_lo[:, :, None, :], pltpu.roll(adj, 1, 2)),
        jnp.where(k_idx == 0, wall, pltpu.roll(adj, 1, 3)),
    ]
    n_rows = incoming.shape[1]
    cell = target_ref[...]
    row_of = cell // nz
    lane_of = cell % nz
    row_hot = (lax.broadcasted_iota(jnp.int32, (rows, n_rows), 0) == row_of).astype(F32)
    lane_hot = (lax.broadcasted_iota(jnp.int32, (nz, n_rows), 0) == lane_of).astype(BF16)
    coupled = None
    for part in split3(incoming):
        lhs = (row_hot[None] * part.astype(F32)[:, None, :]).astype(BF16).reshape(n_var * rows, n_rows)
        term = lax.dot_general(lhs, lane_hot, (((1,), (1,)), ((), ())), preferred_element_type=F32)
        coupled = term if coupled is None else coupled + term
    coupled = coupled.reshape(n_var, nx, ny, nz)
    new = []
    for i in range(n_var):
        applied = diag[i] * adj[i] + coupled[i]
        for d in range(3):
            acc = None
            for j in range(n_var):
                t = blk[d * 36 + j * n_var + i] * up[d][j] + blk[108 + d * 36 + j * n_var + i] * lo[d][j]
                acc = t if acc is None else acc + t
            applied = applied + face[d] * acc
        new.append(adj[i] + (sens[i] - applied) / diag[i])
    return jnp.stack(new, axis=0)


def sweep_kernel(blk_ref, adj_ref, sens_ref, diag_ref, face_ref, hcl, hch, hsl, hsh, hwl, hwh,
                 inc_ref, tgt_ref, send_ref, orient_ref, weight_ref,
                 out_ref, rows_ref, c_lo, c_hi, s_lo, s_hi, w_lo, w_hi):
    n_var = adj_ref.shape[0]
    lanes = adj_ref.shape[3]
    halos = (hcl[...], hch[...], hsl[...], hsh[...], hwl[...], hwh[...])
    new = sweep_body(blk_ref, adj_ref[...], sens_ref[...], diag_ref[...], face_ref[...], halos,
                     inc_ref[...], tgt_ref)
    out_ref[...] = new
    write_faces(new, (c_lo, c_hi, s_lo, s_hi, w_lo, w_hi))
    rows_ref[...] = gather_rows(new, send_ref, orient_ref, weight_ref, blk_ref, n_var, lanes)


def last_kernel(blk_ref, adj_ref, sens_ref, diag_ref, face_ref, hcl, hch, hsl, hsh, hwl, hwh,
                inc_ref, tgt_ref, prod_ref, out_ref, grad_ref):
    n_var = adj_ref.shape[0]
    halos = (hcl[...], hch[...], hsl[...], hsh[...], hwl[...], hwh[...])
    new = sweep_body(blk_ref, adj_ref[...], sens_ref[...], diag_ref[...], face_ref[...], halos,
                     inc_ref[...], tgt_ref)
    out_ref[...] = new
    grad_ref[...] = prod_ref[...] * new[n_var - 1]


def face_shapes(shape):
    n_var, nx, ny, nz = shape
    c = jax.ShapeDtypeStruct((n_var, 1, ny, nz), F32)
    s = jax.ShapeDtypeStruct((n_var, nx, nz), F32)
    w = jax.ShapeDtypeStruct((n_var, nx * ny), F32)
    return [c, c, s, s, w, w]


def exchange(faces):
    c_lo, c_hi, s_lo, s_hi, w_lo, w_hi = faces
    out = []
    for axis, lo_face, hi_face in (("chord", c_lo, c_hi), ("span", s_lo, s_hi), ("wall", w_lo, w_hi)):
        count = lax.axis_size(axis)
        forward = [(i, i + 1) for i in range(count - 1)]
        backward = [(i + 1, i) for i in range(count - 1)]
        out.append(lax.ppermute(hi_face, axis, forward))
        out.append(lax.ppermute(lo_face, axis, backward))
    return out


def local(sensitivity, diagonal, face_coef, upper_blocks, lower_blocks, iface_blocks, production,
          send_cell, target_cell, orient, iface_weight):
    n_span = lax.axis_size("span")
    n_var = sensitivity.shape[0]
    slots = send_cell.shape[-1]
    n_rows = n_span * slots
    shape = sensitivity.shape
    blk = jnp.concatenate([upper_blocks.reshape(-1), lower_blocks.reshape(-1), iface_blocks.reshape(-1)])
    send_row = send_cell.reshape(1, n_rows)
    orient_row = orient.reshape(1, n_rows)
    weight_row = iface_weight.reshape(1, n_rows)
    target_row = lax.all_to_all(
        target_cell.reshape(n_span, slots), "span", split_axis=0, concat_axis=0, tiled=True
    ).reshape(1, n_rows)

    vmem = pl.BlockSpec(memory_space=pltpu.VMEM)
    smem = pl.BlockSpec(memory_space=pltpu.SMEM)
    adj_sds = jax.ShapeDtypeStruct(shape, F32)
    rows_sds = jax.ShapeDtypeStruct((n_var, n_rows), F32)

    init = pl.pallas_call(
        init_kernel,
        out_shape=[adj_sds, rows_sds] + face_shapes(shape),
        in_specs=[smem] + [vmem] * 5,
        out_specs=[vmem] * 8,
    )
    adj, rows, *faces = init(blk, sensitivity, diagonal, send_row, orient_row, weight_row)

    step = pl.pallas_call(
        sweep_kernel,
        out_shape=[adj_sds, rows_sds] + face_shapes(shape),
        in_specs=[smem] + [vmem] * 15,
        out_specs=[vmem] * 8,
    )
    last = pl.pallas_call(
        last_kernel,
        out_shape=[adj_sds, jax.ShapeDtypeStruct(production.shape, F32)],
        in_specs=[smem] + [vmem] * 13,
        out_specs=[vmem] * 2,
    )
    for sweep in range(SWEEPS):
        halos = exchange(faces)
        incoming = lax.all_to_all(
            rows.reshape(n_var, n_span, slots), "span", split_axis=1, concat_axis=1, tiled=True
        ).reshape(n_var, n_rows)
        if sweep < SWEEPS - 1:
            adj, rows, *faces = step(blk, adj, sensitivity, diagonal, face_coef, *halos, incoming,
                                     target_row, send_row, orient_row, weight_row)
        else:
            adj, gradient = last(blk, adj, sensitivity, diagonal, face_coef, *halos, incoming,
                                 target_row, production)
    return (adj, gradient)


def solution(mesh):
    placed = (
        P(None, "chord", "span", "wall"),
        P(None, "chord", "span", "wall"),
        P(None, "chord", "span", "wall"),
        P(),
        P(),
        P(),
        P("chord", "span", "wall"),
        P("chord", "span", "wall", None, None),
        P("chord", "span", "wall", None, None),
        P("chord", "span", "wall", None, None),
        P("chord", "span", "wall", None, None),
    )
    return jax.shard_map(
        local,
        mesh=mesh,
        in_specs=placed,
        out_specs=(P(None, "chord", "span", "wall"), P("chord", "span", "wall")),
        check_vma=False,
    )
```

```python
import jax
import jax.numpy as jnp
from jax import lax
from jax.experimental import pallas as pl
from jax.experimental.pallas import tpu as pltpu
from jax.sharding import PartitionSpec as P

SWEEPS = 3
F32 = jnp.float32
BF16 = jnp.bfloat16


def split3(x):
    p1 = x.astype(BF16)
    r1 = x - p1.astype(F32)
    p2 = r1.astype(BF16)
    p3 = (r1 - p2.astype(F32)).astype(BF16)
    return p1, p2, p3


def gather_rows(adj, send_ref, orient_ref, weight_ref, blk, n_var, lanes):
    rows = adj.shape[1] * adj.shape[2]
    n_rows = send_ref.shape[1]
    cell = send_ref[...]
    row_of = cell // lanes
    lane_of = cell % lanes
    lane_hot = (lax.broadcasted_iota(jnp.int32, (lanes, n_rows), 0) == lane_of).astype(BF16)
    row_hot = (lax.broadcasted_iota(jnp.int32, (rows, n_rows), 0) == row_of).astype(F32)
    flat = adj.reshape(n_var * rows, lanes)
    picked = None
    for part in split3(flat):
        term = jnp.dot(part, lane_hot, preferred_element_type=F32)
        picked = term if picked is None else picked + term
    src = jnp.sum(picked.reshape(n_var, rows, n_rows) * row_hot[None], axis=1)
    orient = orient_ref[...]
    weight = weight_ref[...]
    out = []
    for i in range(n_var):
        first = None
        second = None
        for j in range(n_var):
            a = blk[216 + j * n_var + i] * src[j:j + 1]
            b = blk[216 + 36 + j * n_var + i] * src[j:j + 1]
            first = a if first is None else first + a
            second = b if second is None else second + b
        out.append(jnp.where(orient == 1, second, first) * weight)
    return out


def to_chunks(rows_ref, pieces, slots):
    n_dest = rows_ref.shape[0]
    for t in range(n_dest):
        rows_ref[t] = jnp.concatenate([p[:, t * slots:(t + 1) * slots] for p in pieces], axis=1)


def from_chunks(inc, count, slots):
    n_src = inc.shape[0]
    return [jnp.concatenate([inc[s][:, v * slots:(v + 1) * slots] for s in range(n_src)], axis=1)
            for v in range(count)]


def wall_columns(adj):
    n_var, nx, ny, nz = adj.shape
    lo, hi = [], []
    for v in range(n_var):
        t = adj[v].reshape(nx * ny, nz).T
        lo.append(t[0:1])
        hi.append(t[nz - 1:nz])
    return jnp.concatenate(lo, axis=0), jnp.concatenate(hi, axis=0)


def write_faces(adj, faces):
    c_lo, c_hi, s_lo, s_hi, w_lo, w_hi = faces
    nx, ny, nz = adj.shape[1], adj.shape[2], adj.shape[3]
    j_idx = lax.broadcasted_iota(jnp.int32, adj.shape, 2)
    c_lo[...] = adj[:, 0:1]
    c_hi[...] = adj[:, nx - 1:nx]
    s_lo[...] = jnp.sum(jnp.where(j_idx == 0, adj, 0.0), axis=2)
    s_hi[...] = jnp.sum(jnp.where(j_idx == ny - 1, adj, 0.0), axis=2)
    lo, hi = wall_columns(adj)
    w_lo[...] = lo
    w_hi[...] = hi


def init_kernel(blk_ref, sens_ref, diag_ref, send_ref, orient_ref, weight_ref, tgt_ref,
                adj_ref, rows_ref, c_lo, c_hi, s_lo, s_hi, w_lo, w_hi):
    n_var = sens_ref.shape[0]
    lanes = sens_ref.shape[3]
    slots = send_ref.shape[1] // rows_ref.shape[0]
    adj = sens_ref[...] / diag_ref[...]
    adj_ref[...] = adj
    write_faces(adj, (c_lo, c_hi, s_lo, s_hi, w_lo, w_hi))
    pieces = gather_rows(adj, send_ref, orient_ref, weight_ref, blk_ref, n_var, lanes)
    to_chunks(rows_ref, pieces + [tgt_ref[...].astype(F32)], slots)


def sweep_body(blk, adj, sens, diag, face, halos, incoming, cell):
    n_var, nx, ny, nz = adj.shape
    rows = nx * ny
    h_c_lo, h_c_hi, h_s_lo, h_s_hi, h_w_lo, h_w_hi = halos
    j_idx = lax.broadcasted_iota(jnp.int32, adj.shape, 2)
    k_idx = lax.broadcasted_iota(jnp.int32, adj.shape, 3)
    kk = lax.broadcasted_iota(jnp.int32, (nz, rows), 0)
    wall = []
    for v in range(n_var):
        z = jnp.where(kk == 0, h_w_lo[v:v + 1], jnp.where(kk == nz - 1, h_w_hi[v:v + 1], 0.0))
        wall.append(z.T.reshape(nx, ny, nz))
    wall = jnp.stack(wall, axis=0)
    up = [
        jnp.concatenate([adj[:, 1:], h_c_hi], axis=1),
        jnp.where(j_idx == ny - 1, h_s_hi[:, :, None, :], pltpu.roll(adj, ny - 1, 2)),
        jnp.where(k_idx == nz - 1, wall, pltpu.roll(adj, nz - 1, 3)),
    ]
    lo = [
        jnp.concatenate([h_c_lo, adj[:, :-1]], axis=1),
        jnp.where(j_idx == 0, h_s_lo[:, :, None, :], pltpu.roll(adj, 1, 2)),
        jnp.where(k_idx == 0, wall, pltpu.roll(adj, 1, 3)),
    ]
    n_rows = incoming.shape[1]
    row_of = cell // nz
    lane_of = cell % nz
    row_hot = (lax.broadcasted_iota(jnp.int32, (rows, n_rows), 0) == row_of).astype(F32)
    lane_hot = (lax.broadcasted_iota(jnp.int32, (nz, n_rows), 0) == lane_of).astype(BF16)
    coupled = None
    for part in split3(incoming):
        lhs = (row_hot[None] * part.astype(F32)[:, None, :]).astype(BF16).reshape(n_var * rows, n_rows)
        term = lax.dot_general(lhs, lane_hot, (((1,), (1,)), ((), ())), preferred_element_type=F32)
        coupled = term if coupled is None else coupled + term
    coupled = coupled.reshape(n_var, nx, ny, nz)
    new = []
    for i in range(n_var):
        applied = diag[i] * adj[i] + coupled[i]
        for d in range(3):
            acc = None
            for j in range(n_var):
                t = blk[d * 36 + j * n_var + i] * up[d][j] + blk[108 + d * 36 + j * n_var + i] * lo[d][j]
                acc = t if acc is None else acc + t
            applied = applied + face[d] * acc
        new.append(adj[i] + (sens[i] - applied) / diag[i])
    return jnp.stack(new, axis=0)


def sweep_kernel(blk_ref, adj_ref, sens_ref, diag_ref, face_ref, hcl, hch, hsl, hsh, hwl, hwh,
                 inc_ref, tgt_ref, send_ref, orient_ref, weight_ref,
                 out_ref, rows_ref, tgt_out, c_lo, c_hi, s_lo, s_hi, w_lo, w_hi):
    n_var = adj_ref.shape[0]
    lanes = adj_ref.shape[3]
    slots = send_ref.shape[1] // rows_ref.shape[0]
    halos = (hcl[...], hch[...], hsl[...], hsh[...], hwl[...], hwh[...])
    inc = inc_ref[...]
    if tgt_ref is None:
        got = from_chunks(inc, n_var + 1, slots)
        cell = got[n_var].astype(jnp.int32)
    else:
        got = from_chunks(inc, n_var, slots)
        cell = tgt_ref[...]
    tgt_out[...] = cell
    new = sweep_body(blk_ref, adj_ref[...], sens_ref[...], diag_ref[...], face_ref[...], halos,
                     jnp.concatenate(got[:n_var], axis=0), cell)
    out_ref[...] = new
    write_faces(new, (c_lo, c_hi, s_lo, s_hi, w_lo, w_hi))
    to_chunks(rows_ref, gather_rows(new, send_ref, orient_ref, weight_ref, blk_ref, n_var, lanes), slots)


def first_sweep_kernel(blk_ref, adj_ref, sens_ref, diag_ref, face_ref, hcl, hch, hsl, hsh, hwl, hwh,
                       inc_ref, send_ref, orient_ref, weight_ref, *outs):
    sweep_kernel(blk_ref, adj_ref, sens_ref, diag_ref, face_ref, hcl, hch, hsl, hsh, hwl, hwh,
                 inc_ref, None, send_ref, orient_ref, weight_ref, *outs)


def last_kernel(blk_ref, adj_ref, sens_ref, diag_ref, face_ref, hcl, hch, hsl, hsh, hwl, hwh,
                inc_ref, tgt_ref, prod_ref, out_ref, grad_ref):
    n_var = adj_ref.shape[0]
    slots = inc_ref.shape[2] // n_var
    halos = (hcl[...], hch[...], hsl[...], hsh[...], hwl[...], hwh[...])
    got = from_chunks(inc_ref[...], n_var, slots)
    new = sweep_body(blk_ref, adj_ref[...], sens_ref[...], diag_ref[...], face_ref[...], halos,
                     jnp.concatenate(got, axis=0), tgt_ref[...])
    out_ref[...] = new
    grad_ref[...] = prod_ref[...] * new[n_var - 1]


def face_shapes(shape):
    n_var, nx, ny, nz = shape
    c = jax.ShapeDtypeStruct((n_var, 1, ny, nz), F32)
    s = jax.ShapeDtypeStruct((n_var, nx, nz), F32)
    w = jax.ShapeDtypeStruct((n_var, nx * ny), F32)
    return [c, c, s, s, w, w]


def exchange(faces):
    c_lo, c_hi, s_lo, s_hi, w_lo, w_hi = faces
    out = []
    for axis, lo_face, hi_face in (("chord", c_lo, c_hi), ("span", s_lo, s_hi), ("wall", w_lo, w_hi)):
        count = lax.axis_size(axis)
        forward = [(i, i + 1) for i in range(count - 1)]
        backward = [(i + 1, i) for i in range(count - 1)]
        out.append(lax.ppermute(hi_face, axis, forward))
        out.append(lax.ppermute(lo_face, axis, backward))
    return out


def local(sensitivity, diagonal, face_coef, upper_blocks, lower_blocks, iface_blocks, production,
          send_cell, target_cell, orient, iface_weight):
    n_span = lax.axis_size("span")
    n_var = sensitivity.shape[0]
    slots = send_cell.shape[-1]
    n_rows = n_span * slots
    shape = sensitivity.shape
    blk = jnp.concatenate([upper_blocks.reshape(-1), lower_blocks.reshape(-1), iface_blocks.reshape(-1)])
    send_row = send_cell.reshape(1, n_rows)
    orient_row = orient.reshape(1, n_rows)
    weight_row = iface_weight.reshape(1, n_rows)
    target_row = target_cell.reshape(1, n_rows)

    vmem = pl.BlockSpec(memory_space=pltpu.VMEM)
    smem = pl.BlockSpec(memory_space=pltpu.SMEM)
    adj_sds = jax.ShapeDtypeStruct(shape, F32)
    tgt_sds = jax.ShapeDtypeStruct((1, n_rows), jnp.int32)
    first_rows = jax.ShapeDtypeStruct((n_span, 1, (n_var + 1) * slots), F32)
    rows_sds = jax.ShapeDtypeStruct((n_span, 1, n_var * slots), F32)

    init = pl.pallas_call(
        init_kernel,
        out_shape=[adj_sds, first_rows] + face_shapes(shape),
        in_specs=[smem] + [vmem] * 6,
        out_specs=[vmem] * 8,
    )
    adj, rows, *faces = init(blk, sensitivity, diagonal, send_row, orient_row, weight_row, target_row)

    first = pl.pallas_call(
        first_sweep_kernel,
        out_shape=[adj_sds, rows_sds, tgt_sds] + face_shapes(shape),
        in_specs=[smem] + [vmem] * 14,
        out_specs=[vmem] * 9,
    )
    step = pl.pallas_call(
        sweep_kernel,
        out_shape=[adj_sds, rows_sds, tgt_sds] + face_shapes(shape),
        in_specs=[smem] + [vmem] * 15,
        out_specs=[vmem] * 9,
    )
    last = pl.pallas_call(
        last_kernel,
        out_shape=[adj_sds, jax.ShapeDtypeStruct(production.shape, F32)],
        in_specs=[smem] + [vmem] * 13,
        out_specs=[vmem] * 2,
    )
    received = None
    for sweep in range(SWEEPS):
        halos = exchange(faces)
        incoming = lax.all_to_all(rows, "span", split_axis=0, concat_axis=0, tiled=True)
        if sweep == 0:
            adj, rows, received, *faces = first(blk, adj, sensitivity, diagonal, face_coef, *halos,
                                                incoming, send_row, orient_row, weight_row)
        elif sweep < SWEEPS - 1:
            adj, rows, received, *faces = step(blk, adj, sensitivity, diagonal, face_coef, *halos,
                                               incoming, received, send_row, orient_row, weight_row)
        else:
            adj, gradient = last(blk, adj, sensitivity, diagonal, face_coef, *halos, incoming,
                                 received, production)
    return (adj, gradient)


def solution(mesh):
    placed = (
        P(None, "chord", "span", "wall"),
        P(None, "chord", "span", "wall"),
        P(None, "chord", "span", "wall"),
        P(),
        P(),
        P(),
        P("chord", "span", "wall"),
        P("chord", "span", "wall", None, None),
        P("chord", "span", "wall", None, None),
        P("chord", "span", "wall", None, None),
        P("chord", "span", "wall", None, None),
    )
    return jax.shard_map(
        local,
        mesh=mesh,
        in_specs=placed,
        out_specs=(P(None, "chord", "span", "wall"), P("chord", "span", "wall")),
        check_vma=False,
    )
```

```python
import jax
import jax.numpy as jnp
from jax import lax
from jax.experimental import pallas as pl
from jax.experimental.pallas import tpu as pltpu
from jax.sharding import PartitionSpec as P

SWEEPS = 3
F32 = jnp.float32
BF16 = jnp.bfloat16


def split3(x):
    p1 = x.astype(BF16)
    r1 = x - p1.astype(F32)
    p2 = r1.astype(BF16)
    p3 = (r1 - p2.astype(F32)).astype(BF16)
    return p1, p2, p3


def gather_rows(adj, send_ref, orient_ref, weight_ref, blk, n_var, lanes):
    rows = adj.shape[1] * adj.shape[2]
    cell = flat_row(send_ref[...])
    n_rows = cell.shape[1]
    row_of = cell // lanes
    lane_of = cell % lanes
    lane_hot = (lax.broadcasted_iota(jnp.int32, (lanes, n_rows), 0) == lane_of).astype(BF16)
    row_hot = (lax.broadcasted_iota(jnp.int32, (rows, n_rows), 0) == row_of).astype(F32)
    flat = adj.reshape(n_var * rows, lanes)
    picked = None
    for part in split3(flat):
        term = jnp.dot(part, lane_hot, preferred_element_type=F32)
        picked = term if picked is None else picked + term
    src = jnp.sum(picked.reshape(n_var, rows, n_rows) * row_hot[None], axis=1)
    orient = flat_row(orient_ref[...])
    weight = flat_row(weight_ref[...])
    out = []
    for i in range(n_var):
        first = None
        second = None
        for j in range(n_var):
            a = blk[2][0, j, i] * src[j:j + 1]
            b = blk[2][1, j, i] * src[j:j + 1]
            first = a if first is None else first + a
            second = b if second is None else second + b
        out.append(jnp.where(orient == 1, second, first) * weight)
    return out


def flat_row(x):
    return jnp.concatenate([x[t:t + 1] for t in range(x.shape[0])], axis=1)


def to_chunks(rows_ref, pieces, slots):
    n_dest = rows_ref.shape[0]
    for t in range(n_dest):
        rows_ref[t] = jnp.concatenate([p[:, t * slots:(t + 1) * slots] for p in pieces], axis=1)


def from_chunks(inc, count, slots):
    n_src = inc.shape[0]
    return [jnp.concatenate([inc[s][:, v * slots:(v + 1) * slots] for s in range(n_src)], axis=1)
            for v in range(count)]


def wall_columns(adj):
    n_var, nx, ny, nz = adj.shape
    lo, hi = [], []
    for v in range(n_var):
        t = adj[v].reshape(nx * ny, nz).T
        lo.append(t[0:1])
        hi.append(t[nz - 1:nz])
    return jnp.concatenate(lo, axis=0), jnp.concatenate(hi, axis=0)


def write_faces(adj, faces):
    c_lo, c_hi, s_lo, s_hi, w_lo, w_hi = faces
    nx, ny, nz = adj.shape[1], adj.shape[2], adj.shape[3]
    j_idx = lax.broadcasted_iota(jnp.int32, adj.shape, 2)
    c_lo[...] = adj[:, 0:1]
    c_hi[...] = adj[:, nx - 1:nx]
    s_lo[...] = jnp.sum(jnp.where(j_idx == 0, adj, 0.0), axis=2)
    s_hi[...] = jnp.sum(jnp.where(j_idx == ny - 1, adj, 0.0), axis=2)
    lo, hi = wall_columns(adj)
    w_lo[...] = lo
    w_hi[...] = hi


def init_kernel(ub_ref, lb_ref, ib_ref, sens_ref, diag_ref, send_ref, orient_ref, weight_ref, tgt_ref,
                adj_ref, rows_ref, c_lo, c_hi, s_lo, s_hi, w_lo, w_hi):
    n_var = sens_ref.shape[0]
    lanes = sens_ref.shape[3]
    slots = send_ref.shape[1]
    blk_ref = (ub_ref, lb_ref, ib_ref)
    adj = sens_ref[...] / diag_ref[...]
    adj_ref[...] = adj
    write_faces(adj, (c_lo, c_hi, s_lo, s_hi, w_lo, w_hi))
    pieces = gather_rows(adj, send_ref, orient_ref, weight_ref, blk_ref, n_var, lanes)
    to_chunks(rows_ref, pieces + [flat_row(tgt_ref[...]).astype(F32)], slots)


def sweep_body(blk, adj, sens, diag, face, halos, incoming, cell):
    n_var, nx, ny, nz = adj.shape
    rows = nx * ny
    h_c_lo, h_c_hi, h_s_lo, h_s_hi, h_w_lo, h_w_hi = halos
    j_idx = lax.broadcasted_iota(jnp.int32, adj.shape, 2)
    k_idx = lax.broadcasted_iota(jnp.int32, adj.shape, 3)
    kk = lax.broadcasted_iota(jnp.int32, (nz, rows), 0)
    wall = []
    for v in range(n_var):
        z = jnp.where(kk == 0, h_w_lo[v:v + 1], jnp.where(kk == nz - 1, h_w_hi[v:v + 1], 0.0))
        wall.append(z.T.reshape(nx, ny, nz))
    wall = jnp.stack(wall, axis=0)
    up = [
        jnp.concatenate([adj[:, 1:], h_c_hi], axis=1),
        jnp.where(j_idx == ny - 1, h_s_hi[:, :, None, :], pltpu.roll(adj, ny - 1, 2)),
        jnp.where(k_idx == nz - 1, wall, pltpu.roll(adj, nz - 1, 3)),
    ]
    lo = [
        jnp.concatenate([h_c_lo, adj[:, :-1]], axis=1),
        jnp.where(j_idx == 0, h_s_lo[:, :, None, :], pltpu.roll(adj, 1, 2)),
        jnp.where(k_idx == 0, wall, pltpu.roll(adj, 1, 3)),
    ]
    n_rows = incoming.shape[1]
    row_of = cell // nz
    lane_of = cell % nz
    row_hot = (lax.broadcasted_iota(jnp.int32, (rows, n_rows), 0) == row_of).astype(BF16)
    lane_hot = (lax.broadcasted_iota(jnp.int32, (nz, n_rows), 0) == lane_of).astype(BF16)
    coupled = None
    for part in split3(incoming):
        lhs = (row_hot[None] * part[:, None, :]).reshape(n_var * rows, n_rows)
        term = lax.dot_general(lhs, lane_hot, (((1,), (1,)), ((), ())), preferred_element_type=F32)
        coupled = term if coupled is None else coupled + term
    coupled = coupled.reshape(n_var, nx, ny, nz)
    new = []
    for i in range(n_var):
        applied = diag[i] * adj[i] + coupled[i]
        for d in range(3):
            acc = None
            for j in range(n_var):
                t = blk[0][d, j, i] * up[d][j] + blk[1][d, j, i] * lo[d][j]
                acc = t if acc is None else acc + t
            applied = applied + face[d] * acc
        new.append(adj[i] + (sens[i] - applied) / diag[i])
    return jnp.stack(new, axis=0)


def sweep_kernel(ub_ref, lb_ref, ib_ref, adj_ref, sens_ref, diag_ref, face_ref, hcl, hch, hsl, hsh, hwl, hwh,
                 inc_ref, tgt_ref, send_ref, orient_ref, weight_ref,
                 out_ref, rows_ref, tgt_out, c_lo, c_hi, s_lo, s_hi, w_lo, w_hi):
    n_var = adj_ref.shape[0]
    lanes = adj_ref.shape[3]
    slots = send_ref.shape[1]
    blk_ref = (ub_ref, lb_ref, ib_ref)
    halos = (hcl[...], hch[...], hsl[...], hsh[...], hwl[...], hwh[...])
    inc = inc_ref[...]
    if tgt_ref is None:
        got = from_chunks(inc, n_var + 1, slots)
        cell = got[n_var].astype(jnp.int32)
    else:
        got = from_chunks(inc, n_var, slots)
        cell = tgt_ref[...]
    tgt_out[...] = cell
    new = sweep_body(blk_ref, adj_ref[...], sens_ref[...], diag_ref[...], face_ref[...], halos,
                     jnp.concatenate(got[:n_var], axis=0), cell)
    out_ref[...] = new
    write_faces(new, (c_lo, c_hi, s_lo, s_hi, w_lo, w_hi))
    to_chunks(rows_ref, gather_rows(new, send_ref, orient_ref, weight_ref, blk_ref, n_var, lanes), slots)


def first_sweep_kernel(ub_ref, lb_ref, ib_ref, adj_ref, sens_ref, diag_ref, face_ref, hcl, hch, hsl, hsh, hwl, hwh,
                       inc_ref, send_ref, orient_ref, weight_ref, *outs):
    sweep_kernel(ub_ref, lb_ref, ib_ref, adj_ref, sens_ref, diag_ref, face_ref, hcl, hch, hsl, hsh, hwl, hwh,
                 inc_ref, None, send_ref, orient_ref, weight_ref, *outs)


def last_kernel(ub_ref, lb_ref, ib_ref, adj_ref, sens_ref, diag_ref, face_ref, hcl, hch, hsl, hsh, hwl, hwh,
                inc_ref, tgt_ref, prod_ref, out_ref, grad_ref):
    n_var = adj_ref.shape[0]
    slots = inc_ref.shape[2] // n_var
    blk_ref = (ub_ref, lb_ref, ib_ref)
    halos = (hcl[...], hch[...], hsl[...], hsh[...], hwl[...], hwh[...])
    got = from_chunks(inc_ref[...], n_var, slots)
    new = sweep_body(blk_ref, adj_ref[...], sens_ref[...], diag_ref[...], face_ref[...], halos,
                     jnp.concatenate(got, axis=0), tgt_ref[...])
    out_ref[...] = new
    grad_ref[...] = prod_ref[...] * new[n_var - 1]


def face_shapes(shape):
    n_var, nx, ny, nz = shape
    c = jax.ShapeDtypeStruct((n_var, 1, ny, nz), F32)
    s = jax.ShapeDtypeStruct((n_var, nx, nz), F32)
    w = jax.ShapeDtypeStruct((n_var, nx * ny), F32)
    return [c, c, s, s, w, w]


def exchange(faces):
    c_lo, c_hi, s_lo, s_hi, w_lo, w_hi = faces
    out = []
    for axis, lo_face, hi_face in (("chord", c_lo, c_hi), ("span", s_lo, s_hi), ("wall", w_lo, w_hi)):
        count = lax.axis_size(axis)
        forward = [(i, i + 1) for i in range(count - 1)]
        backward = [(i + 1, i) for i in range(count - 1)]
        out.append(lax.ppermute(hi_face, axis, forward))
        out.append(lax.ppermute(lo_face, axis, backward))
    return out


def local(sensitivity, diagonal, face_coef, upper_blocks, lower_blocks, iface_blocks, production,
          send_cell, target_cell, orient, iface_weight):
    n_span = lax.axis_size("span")
    n_var = sensitivity.shape[0]
    slots = send_cell.shape[-1]
    n_rows = n_span * slots
    shape = sensitivity.shape
    blk = (upper_blocks, lower_blocks, iface_blocks)
    send_row = send_cell.reshape(n_span, slots)
    orient_row = orient.reshape(n_span, slots)
    weight_row = iface_weight.reshape(n_span, slots)
    target_row = target_cell.reshape(n_span, slots)

    vmem = pl.BlockSpec(memory_space=pltpu.VMEM)
    smem = pl.BlockSpec(memory_space=pltpu.SMEM)
    adj_sds = jax.ShapeDtypeStruct(shape, F32)
    tgt_sds = jax.ShapeDtypeStruct((1, n_rows), jnp.int32)
    first_rows = jax.ShapeDtypeStruct((n_span, 1, (n_var + 1) * slots), F32)
    rows_sds = jax.ShapeDtypeStruct((n_span, 1, n_var * slots), F32)

    init = pl.pallas_call(
        init_kernel,
        out_shape=[adj_sds, first_rows] + face_shapes(shape),
        in_specs=[smem] * 3 + [vmem] * 6,
        out_specs=[vmem] * 8,
    )
    adj, rows, *faces = init(*blk, sensitivity, diagonal, send_row, orient_row, weight_row, target_row)

    first = pl.pallas_call(
        first_sweep_kernel,
        out_shape=[adj_sds, rows_sds, tgt_sds] + face_shapes(shape),
        in_specs=[smem] * 3 + [vmem] * 14,
        out_specs=[vmem] * 9,
    )
    step = pl.pallas_call(
        sweep_kernel,
        out_shape=[adj_sds, rows_sds, tgt_sds] + face_shapes(shape),
        in_specs=[smem] * 3 + [vmem] * 15,
        out_specs=[vmem] * 9,
    )
    last = pl.pallas_call(
        last_kernel,
        out_shape=[adj_sds, jax.ShapeDtypeStruct(production.shape, F32)],
        in_specs=[smem] * 3 + [vmem] * 13,
        out_specs=[vmem] * 2,
    )
    received = None
    for sweep in range(SWEEPS):
        halos = exchange(faces)
        incoming = lax.all_to_all(rows, "span", split_axis=0, concat_axis=0, tiled=True)
        if sweep == 0:
            adj, rows, received, *faces = first(*blk, adj, sensitivity, diagonal, face_coef, *halos,
                                                incoming, send_row, orient_row, weight_row)
        elif sweep < SWEEPS - 1:
            adj, rows, received, *faces = step(*blk, adj, sensitivity, diagonal, face_coef, *halos,
                                               incoming, received, send_row, orient_row, weight_row)
        else:
            adj, gradient = last(*blk, adj, sensitivity, diagonal, face_coef, *halos, incoming,
                                 received, production)
    return (adj, gradient)


def solution(mesh):
    placed = (
        P(None, "chord", "span", "wall"),
        P(None, "chord", "span", "wall"),
        P(None, "chord", "span", "wall"),
        P(),
        P(),
        P(),
        P("chord", "span", "wall"),
        P("chord", "span", "wall", None, None),
        P("chord", "span", "wall", None, None),
        P("chord", "span", "wall", None, None),
        P("chord", "span", "wall", None, None),
    )
    return jax.shard_map(
        local,
        mesh=mesh,
        in_specs=placed,
        out_specs=(P(None, "chord", "span", "wall"), P("chord", "span", "wall")),
        check_vma=False,
    )
```

```python
import jax
import jax.numpy as jnp
from jax import lax
from jax.experimental import pallas as pl
from jax.experimental.pallas import tpu as pltpu
from jax.sharding import PartitionSpec as P

SWEEPS = 3
F32 = jnp.float32
BF16 = jnp.bfloat16


def split3(x):
    p1 = x.astype(BF16)
    r1 = x - p1.astype(F32)
    p2 = r1.astype(BF16)
    p3 = (r1 - p2.astype(F32)).astype(BF16)
    return p1, p2, p3


def gather_rows(adj, send_ref, orient_ref, weight_ref, blk, n_var, lanes):
    rows = adj.shape[1] * adj.shape[2]
    cell = flat_row(send_ref[...])
    n_rows = cell.shape[1]
    row_of = cell // lanes
    lane_of = cell % lanes
    lane_hot = (lax.broadcasted_iota(jnp.int32, (lanes, n_rows), 0) == lane_of).astype(BF16)
    row_hot = (lax.broadcasted_iota(jnp.int32, (rows, n_rows), 0) == row_of).astype(F32)
    flat = adj.reshape(n_var * rows, lanes)
    picked = None
    for part in split3(flat):
        term = jnp.dot(part, lane_hot, preferred_element_type=F32)
        picked = term if picked is None else picked + term
    src = jnp.sum(picked.reshape(n_var, rows, n_rows) * row_hot[None], axis=1)
    orient = flat_row(orient_ref[...])
    weight = flat_row(weight_ref[...])
    out = []
    for i in range(n_var):
        first = None
        second = None
        for j in range(n_var):
            a = blk[2][0, j, i] * src[j:j + 1]
            b = blk[2][1, j, i] * src[j:j + 1]
            first = a if first is None else first + a
            second = b if second is None else second + b
        out.append(jnp.where(orient == 1, second, first) * weight)
    return out


def flat_row(x):
    return jnp.concatenate([x[t:t + 1] for t in range(x.shape[0])], axis=1)


def to_chunks(rows_ref, pieces, slots):
    n_dest = rows_ref.shape[0]
    for t in range(n_dest):
        rows_ref[t] = jnp.concatenate([p[:, t * slots:(t + 1) * slots] for p in pieces], axis=1)


def from_chunks(inc, count, slots):
    n_src = inc.shape[0]
    return [jnp.concatenate([inc[s][:, v * slots:(v + 1) * slots] for s in range(n_src)], axis=1)
            for v in range(count)]


def wall_columns(adj):
    n_var, nx, ny, nz = adj.shape
    lo, hi = [], []
    for v in range(n_var):
        t = adj[v].reshape(nx * ny, nz).T
        lo.append(t[0:1])
        hi.append(t[nz - 1:nz])
    return jnp.concatenate(lo, axis=0), jnp.concatenate(hi, axis=0)


def write_faces(adj, faces):
    c_lo, c_hi, s_lo, s_hi, w_lo, w_hi = faces
    nx, ny, nz = adj.shape[1], adj.shape[2], adj.shape[3]
    j_idx = lax.broadcasted_iota(jnp.int32, adj.shape, 2)
    c_lo[...] = adj[:, 0:1]
    c_hi[...] = adj[:, nx - 1:nx]
    s_lo[...] = jnp.sum(jnp.where(j_idx == 0, adj, 0.0), axis=2)
    s_hi[...] = jnp.sum(jnp.where(j_idx == ny - 1, adj, 0.0), axis=2)
    lo, hi = wall_columns(adj)
    w_lo[...] = lo
    w_hi[...] = hi


def init_kernel(ub_ref, lb_ref, ib_ref, sens_ref, diag_ref, send_ref, orient_ref, weight_ref, tgt_ref,
                adj_ref, rows_ref, c_lo, c_hi, s_lo, s_hi, w_lo, w_hi):
    n_var = sens_ref.shape[0]
    lanes = sens_ref.shape[3]
    slots = send_ref.shape[1]
    blk_ref = (ub_ref, lb_ref, ib_ref)
    adj = sens_ref[...] / diag_ref[...]
    adj_ref[...] = adj
    write_faces(adj, (c_lo, c_hi, s_lo, s_hi, w_lo, w_hi))
    pieces = gather_rows(adj, send_ref, orient_ref, weight_ref, blk_ref, n_var, lanes)
    to_chunks(rows_ref, pieces + [flat_row(tgt_ref[...]).astype(F32)], slots)


def sweep_body(blk, adj, sens, diag, face, halos, incoming, cell):
    n_var, nx, ny, nz = adj.shape
    rows = nx * ny
    h_c_lo, h_c_hi, h_s_lo, h_s_hi, h_w_lo, h_w_hi = halos
    j_idx = lax.broadcasted_iota(jnp.int32, adj.shape, 2)
    k_idx = lax.broadcasted_iota(jnp.int32, adj.shape, 3)
    kk = lax.broadcasted_iota(jnp.int32, (nz, rows), 0)
    wall = []
    for v in range(n_var):
        z = jnp.where(kk == 0, h_w_lo[v:v + 1], jnp.where(kk == nz - 1, h_w_hi[v:v + 1], 0.0))
        wall.append(z.T.reshape(nx, ny, nz))
    wall = jnp.stack(wall, axis=0)
    up = [
        jnp.concatenate([adj[:, 1:], h_c_hi], axis=1),
        jnp.where(j_idx == ny - 1, h_s_hi[:, :, None, :], pltpu.roll(adj, ny - 1, 2)),
        jnp.where(k_idx == nz - 1, wall, pltpu.roll(adj, nz - 1, 3)),
    ]
    lo = [
        jnp.concatenate([h_c_lo, adj[:, :-1]], axis=1),
        jnp.where(j_idx == 0, h_s_lo[:, :, None, :], pltpu.roll(adj, 1, 2)),
        jnp.where(k_idx == 0, wall, pltpu.roll(adj, 1, 3)),
    ]
    n_rows = incoming.shape[1]
    row_of = cell // nz
    lane_of = cell % nz
    row_hot = (lax.broadcasted_iota(jnp.int32, (rows, n_rows), 0) == row_of).astype(BF16)
    lane_hot = (lax.broadcasted_iota(jnp.int32, (nz, n_rows), 0) == lane_of).astype(BF16)
    coupled = None
    for part in split3(incoming):
        lhs = (row_hot[None] * part[:, None, :]).reshape(n_var * rows, n_rows)
        term = lax.dot_general(lhs, lane_hot, (((1,), (1,)), ((), ())), preferred_element_type=F32)
        coupled = term if coupled is None else coupled + term
    coupled = coupled.reshape(n_var, nx, ny, nz)
    new = []
    for i in range(n_var):
        applied = diag[i] * adj[i] + coupled[i]
        for d in range(3):
            acc = None
            for j in range(n_var):
                t = blk[0][d, j, i] * up[d][j] + blk[1][d, j, i] * lo[d][j]
                acc = t if acc is None else acc + t
            applied = applied + face[d] * acc
        new.append(adj[i] + (sens[i] - applied) / diag[i])
    return jnp.stack(new, axis=0)


def sweep_kernel(ub_ref, lb_ref, ib_ref, adj_ref, sens_ref, diag_ref, face_ref, hcl, hch, hsl, hsh, hwl, hwh,
                 inc_ref, tgt_ref, send_ref, orient_ref, weight_ref,
                 out_ref, rows_ref, tgt_out, c_lo, c_hi, s_lo, s_hi, w_lo, w_hi):
    n_var = adj_ref.shape[0]
    lanes = adj_ref.shape[3]
    slots = send_ref.shape[1]
    blk_ref = (ub_ref, lb_ref, ib_ref)
    halos = (hcl[...], hch[...], hsl[...], hsh[...], hwl[...], hwh[...])
    inc = inc_ref[...]
    if tgt_ref is None:
        got = from_chunks(inc, n_var + 1, slots)
        cell = got[n_var].astype(jnp.int32)
    else:
        got = from_chunks(inc, n_var, slots)
        cell = tgt_ref[...]
    tgt_out[...] = cell
    new = sweep_body(blk_ref, adj_ref[...], sens_ref[...], diag_ref[...], face_ref[...], halos,
                     jnp.concatenate(got[:n_var], axis=0), cell)
    out_ref[...] = new
    write_faces(new, (c_lo, c_hi, s_lo, s_hi, w_lo, w_hi))
    to_chunks(rows_ref, gather_rows(new, send_ref, orient_ref, weight_ref, blk_ref, n_var, lanes), slots)


def first_sweep_kernel(ub_ref, lb_ref, ib_ref, adj_ref, sens_ref, diag_ref, face_ref, hcl, hch, hsl, hsh, hwl, hwh,
                       inc_ref, send_ref, orient_ref, weight_ref, *outs):
    sweep_kernel(ub_ref, lb_ref, ib_ref, adj_ref, sens_ref, diag_ref, face_ref, hcl, hch, hsl, hsh, hwl, hwh,
                 inc_ref, None, send_ref, orient_ref, weight_ref, *outs)


def last_kernel(ub_ref, lb_ref, ib_ref, adj_ref, sens_ref, diag_ref, face_ref, hcl, hch, hsl, hsh, hwl, hwh,
                inc_ref, tgt_ref, prod_ref, out_ref, grad_ref):
    n_var = adj_ref.shape[0]
    slots = inc_ref.shape[2] // n_var
    blk_ref = (ub_ref, lb_ref, ib_ref)
    halos = (hcl[...], hch[...], hsl[...], hsh[...], hwl[...], hwh[...])
    got = from_chunks(inc_ref[...], n_var, slots)
    new = sweep_body(blk_ref, adj_ref[...], sens_ref[...], diag_ref[...], face_ref[...], halos,
                     jnp.concatenate(got, axis=0), tgt_ref[...])
    out_ref[...] = new
    grad_ref[...] = prod_ref[...] * new[n_var - 1]


def face_shapes(shape):
    n_var, nx, ny, nz = shape
    c = jax.ShapeDtypeStruct((n_var, 1, ny, nz), F32)
    s = jax.ShapeDtypeStruct((n_var, nx, nz), F32)
    w = jax.ShapeDtypeStruct((n_var, nx * ny), F32)
    return [c, c, s, s, w, w]


def exchange(faces):
    c_lo, c_hi, s_lo, s_hi, w_lo, w_hi = faces
    out = []
    for axis, lo_face, hi_face in (("chord", c_lo, c_hi), ("span", s_lo, s_hi), ("wall", w_lo, w_hi)):
        count = lax.axis_size(axis)
        forward = [(i, i + 1) for i in range(count - 1)]
        backward = [(i + 1, i) for i in range(count - 1)]
        out.append(lax.ppermute(hi_face, axis, forward))
        out.append(lax.ppermute(lo_face, axis, backward))
    return out


def local(sensitivity, diagonal, face_coef, upper_blocks, lower_blocks, iface_blocks, production,
          send_cell, target_cell, orient, iface_weight):
    n_span = lax.axis_size("span")
    n_var = sensitivity.shape[0]
    slots = send_cell.shape[-1]
    n_rows = n_span * slots
    shape = sensitivity.shape
    blk = (upper_blocks, lower_blocks, iface_blocks)
    send_row = send_cell.reshape(n_span, slots)
    orient_row = orient.reshape(n_span, slots)
    weight_row = iface_weight.reshape(n_span, slots)
    target_row = target_cell.reshape(n_span, slots)

    vmem = pl.BlockSpec(memory_space=pltpu.VMEM)
    smem = pl.BlockSpec(memory_space=pltpu.SMEM)
    adj_sds = jax.ShapeDtypeStruct(shape, F32)
    tgt_sds = jax.ShapeDtypeStruct((1, n_rows), jnp.int32)
    first_rows = jax.ShapeDtypeStruct((n_span, 1, (n_var + 1) * slots), F32)
    rows_sds = jax.ShapeDtypeStruct((n_span, 1, n_var * slots), F32)

    init = pl.pallas_call(
        init_kernel,
        out_shape=[adj_sds, first_rows] + face_shapes(shape),
        in_specs=[smem] * 3 + [vmem] * 6,
        out_specs=[vmem] * 8,
    )
    adj, rows, *faces = init(*blk, sensitivity, diagonal, send_row, orient_row, weight_row, target_row)

    first = pl.pallas_call(
        first_sweep_kernel,
        out_shape=[adj_sds, rows_sds, tgt_sds] + face_shapes(shape),
        in_specs=[smem] * 3 + [vmem] * 14,
        out_specs=[vmem] * 9,
    )
    step = pl.pallas_call(
        sweep_kernel,
        out_shape=[adj_sds, rows_sds, tgt_sds] + face_shapes(shape),
        in_specs=[smem] * 3 + [vmem] * 15,
        out_specs=[vmem] * 9,
    )
    last = pl.pallas_call(
        last_kernel,
        out_shape=[adj_sds, jax.ShapeDtypeStruct(production.shape, F32)],
        in_specs=[smem] * 3 + [vmem] * 13,
        out_specs=[vmem] * 2,
    )
    received = None
    for sweep in range(SWEEPS):
        incoming = lax.all_to_all(rows, "span", split_axis=0, concat_axis=0, tiled=True)
        incoming, faces = lax.optimization_barrier((incoming, faces))
        halos = exchange(faces)
        if sweep == 0:
            adj, rows, received, *faces = first(*blk, adj, sensitivity, diagonal, face_coef, *halos,
                                                incoming, send_row, orient_row, weight_row)
        elif sweep < SWEEPS - 1:
            adj, rows, received, *faces = step(*blk, adj, sensitivity, diagonal, face_coef, *halos,
                                               incoming, received, send_row, orient_row, weight_row)
        else:
            adj, gradient = last(*blk, adj, sensitivity, diagonal, face_coef, *halos, incoming,
                                 received, production)
    return (adj, gradient)


def solution(mesh):
    placed = (
        P(None, "chord", "span", "wall"),
        P(None, "chord", "span", "wall"),
        P(None, "chord", "span", "wall"),
        P(),
        P(),
        P(),
        P("chord", "span", "wall"),
        P("chord", "span", "wall", None, None),
        P("chord", "span", "wall", None, None),
        P("chord", "span", "wall", None, None),
        P("chord", "span", "wall", None, None),
    )
    return jax.shard_map(
        local,
        mesh=mesh,
        in_specs=placed,
        out_specs=(P(None, "chord", "span", "wall"), P("chord", "span", "wall")),
        check_vma=False,
    )
```

```python
import jax
import jax.numpy as jnp
from jax import lax
from jax.experimental import pallas as pl
from jax.experimental.pallas import tpu as pltpu
from jax.sharding import PartitionSpec as P

SWEEPS = 3
F32 = jnp.float32
BF16 = jnp.bfloat16


def split3(x):
    p1 = x.astype(BF16)
    r1 = x - p1.astype(F32)
    p2 = r1.astype(BF16)
    p3 = (r1 - p2.astype(F32)).astype(BF16)
    return p1, p2, p3


def gather_rows(adj, send_ref, orient_ref, weight_ref, blk, n_var, lanes):
    rows = adj.shape[1] * adj.shape[2]
    cell = flat_row(send_ref[...])
    n_rows = cell.shape[1]
    row_of = cell // lanes
    lane_of = cell % lanes
    lane_hot = (lax.broadcasted_iota(jnp.int32, (lanes, n_rows), 0) == lane_of).astype(BF16)
    row_hot = (lax.broadcasted_iota(jnp.int32, (rows, n_rows), 0) == row_of).astype(F32)
    flat = adj.reshape(n_var * rows, lanes)
    picked = jnp.dot(jnp.concatenate(split3(flat), axis=1),
                     jnp.concatenate([lane_hot] * 3, axis=0), preferred_element_type=F32)
    src = jnp.sum(picked.reshape(n_var, rows, n_rows) * row_hot[None], axis=1)
    orient = flat_row(orient_ref[...])
    weight = flat_row(weight_ref[...])
    out = []
    for i in range(n_var):
        first = None
        second = None
        for j in range(n_var):
            a = blk[2][0, j, i] * src[j:j + 1]
            b = blk[2][1, j, i] * src[j:j + 1]
            first = a if first is None else first + a
            second = b if second is None else second + b
        out.append(jnp.where(orient == 1, second, first) * weight)
    return out


def flat_row(x):
    return jnp.concatenate([x[t:t + 1] for t in range(x.shape[0])], axis=1)


def to_chunks(rows_ref, pieces, slots):
    n_dest = rows_ref.shape[0]
    for t in range(n_dest):
        rows_ref[t] = jnp.concatenate([p[:, t * slots:(t + 1) * slots] for p in pieces], axis=1)


def from_chunks(inc, count, slots):
    n_src = inc.shape[0]
    return [jnp.concatenate([inc[s][:, v * slots:(v + 1) * slots] for s in range(n_src)], axis=1)
            for v in range(count)]


def wall_columns(adj):
    n_var, nx, ny, nz = adj.shape
    lo, hi = [], []
    for v in range(n_var):
        t = adj[v].reshape(nx * ny, nz).T
        lo.append(t[0:1])
        hi.append(t[nz - 1:nz])
    return jnp.concatenate(lo, axis=0), jnp.concatenate(hi, axis=0)


def write_faces(adj, faces):
    c_lo, c_hi, s_lo, s_hi, w_lo, w_hi = faces
    nx, ny, nz = adj.shape[1], adj.shape[2], adj.shape[3]
    j_idx = lax.broadcasted_iota(jnp.int32, adj.shape, 2)
    c_lo[...] = adj[:, 0:1]
    c_hi[...] = adj[:, nx - 1:nx]
    s_lo[...] = jnp.sum(jnp.where(j_idx == 0, adj, 0.0), axis=2)
    s_hi[...] = jnp.sum(jnp.where(j_idx == ny - 1, adj, 0.0), axis=2)
    lo, hi = wall_columns(adj)
    w_lo[...] = lo
    w_hi[...] = hi


def init_kernel(ub_ref, lb_ref, ib_ref, sens_ref, diag_ref, send_ref, orient_ref, weight_ref, tgt_ref,
                adj_ref, rows_ref, c_lo, c_hi, s_lo, s_hi, w_lo, w_hi):
    n_var = sens_ref.shape[0]
    lanes = sens_ref.shape[3]
    slots = send_ref.shape[1]
    blk_ref = (ub_ref, lb_ref, ib_ref)
    adj = sens_ref[...] / diag_ref[...]
    adj_ref[...] = adj
    write_faces(adj, (c_lo, c_hi, s_lo, s_hi, w_lo, w_hi))
    pieces = gather_rows(adj, send_ref, orient_ref, weight_ref, blk_ref, n_var, lanes)
    to_chunks(rows_ref, pieces + [flat_row(tgt_ref[...]).astype(F32)], slots)


def sweep_body(blk, adj, sens, diag, face, halos, incoming, cell):
    n_var, nx, ny, nz = adj.shape
    rows = nx * ny
    h_c_lo, h_c_hi, h_s_lo, h_s_hi, h_w_lo, h_w_hi = halos
    j_idx = lax.broadcasted_iota(jnp.int32, adj.shape, 2)
    k_idx = lax.broadcasted_iota(jnp.int32, adj.shape, 3)
    kk = lax.broadcasted_iota(jnp.int32, (nz, rows), 0)
    wall = []
    for v in range(n_var):
        z = jnp.where(kk == 0, h_w_lo[v:v + 1], jnp.where(kk == nz - 1, h_w_hi[v:v + 1], 0.0))
        wall.append(z.T.reshape(nx, ny, nz))
    wall = jnp.stack(wall, axis=0)
    up = [
        jnp.concatenate([adj[:, 1:], h_c_hi], axis=1),
        jnp.where(j_idx == ny - 1, h_s_hi[:, :, None, :], pltpu.roll(adj, ny - 1, 2)),
        jnp.where(k_idx == nz - 1, wall, pltpu.roll(adj, nz - 1, 3)),
    ]
    lo = [
        jnp.concatenate([h_c_lo, adj[:, :-1]], axis=1),
        jnp.where(j_idx == 0, h_s_lo[:, :, None, :], pltpu.roll(adj, 1, 2)),
        jnp.where(k_idx == 0, wall, pltpu.roll(adj, 1, 3)),
    ]
    n_rows = incoming.shape[1]
    row_of = cell // nz
    lane_of = cell % nz
    row_hot = (lax.broadcasted_iota(jnp.int32, (rows, n_rows), 0) == row_of).astype(BF16)
    lane_hot = (lax.broadcasted_iota(jnp.int32, (nz, n_rows), 0) == lane_of).astype(BF16)
    lhs = jnp.concatenate([(row_hot[None] * part[:, None, :]).reshape(n_var * rows, n_rows)
                           for part in split3(incoming)], axis=1)
    coupled = lax.dot_general(lhs, jnp.concatenate([lane_hot] * 3, axis=1), (((1,), (1,)), ((), ())),
                              preferred_element_type=F32)
    coupled = coupled.reshape(n_var, nx, ny, nz)
    new = []
    for i in range(n_var):
        applied = diag[i] * adj[i] + coupled[i]
        for d in range(3):
            acc = None
            for j in range(n_var):
                t = blk[0][d, j, i] * up[d][j] + blk[1][d, j, i] * lo[d][j]
                acc = t if acc is None else acc + t
            applied = applied + face[d] * acc
        new.append(adj[i] + (sens[i] - applied) / diag[i])
    return jnp.stack(new, axis=0)


def sweep_kernel(ub_ref, lb_ref, ib_ref, adj_ref, sens_ref, diag_ref, face_ref, hcl, hch, hsl, hsh, hwl, hwh,
                 inc_ref, tgt_ref, send_ref, orient_ref, weight_ref,
                 out_ref, rows_ref, tgt_out, c_lo, c_hi, s_lo, s_hi, w_lo, w_hi):
    n_var = adj_ref.shape[0]
    lanes = adj_ref.shape[3]
    slots = send_ref.shape[1]
    blk_ref = (ub_ref, lb_ref, ib_ref)
    halos = (hcl[...], hch[...], hsl[...], hsh[...], hwl[...], hwh[...])
    inc = inc_ref[...]
    if tgt_ref is None:
        got = from_chunks(inc, n_var + 1, slots)
        cell = got[n_var].astype(jnp.int32)
    else:
        got = from_chunks(inc, n_var, slots)
        cell = tgt_ref[...]
    tgt_out[...] = cell
    new = sweep_body(blk_ref, adj_ref[...], sens_ref[...], diag_ref[...], face_ref[...], halos,
                     jnp.concatenate(got[:n_var], axis=0), cell)
    out_ref[...] = new
    write_faces(new, (c_lo, c_hi, s_lo, s_hi, w_lo, w_hi))
    to_chunks(rows_ref, gather_rows(new, send_ref, orient_ref, weight_ref, blk_ref, n_var, lanes), slots)


def first_sweep_kernel(ub_ref, lb_ref, ib_ref, adj_ref, sens_ref, diag_ref, face_ref, hcl, hch, hsl, hsh, hwl, hwh,
                       inc_ref, send_ref, orient_ref, weight_ref, *outs):
    sweep_kernel(ub_ref, lb_ref, ib_ref, adj_ref, sens_ref, diag_ref, face_ref, hcl, hch, hsl, hsh, hwl, hwh,
                 inc_ref, None, send_ref, orient_ref, weight_ref, *outs)


def last_kernel(ub_ref, lb_ref, ib_ref, adj_ref, sens_ref, diag_ref, face_ref, hcl, hch, hsl, hsh, hwl, hwh,
                inc_ref, tgt_ref, prod_ref, out_ref, grad_ref):
    n_var = adj_ref.shape[0]
    slots = inc_ref.shape[2] // n_var
    blk_ref = (ub_ref, lb_ref, ib_ref)
    halos = (hcl[...], hch[...], hsl[...], hsh[...], hwl[...], hwh[...])
    got = from_chunks(inc_ref[...], n_var, slots)
    new = sweep_body(blk_ref, adj_ref[...], sens_ref[...], diag_ref[...], face_ref[...], halos,
                     jnp.concatenate(got, axis=0), tgt_ref[...])
    out_ref[...] = new
    grad_ref[...] = prod_ref[...] * new[n_var - 1]


def face_shapes(shape):
    n_var, nx, ny, nz = shape
    c = jax.ShapeDtypeStruct((n_var, 1, ny, nz), F32)
    s = jax.ShapeDtypeStruct((n_var, nx, nz), F32)
    w = jax.ShapeDtypeStruct((n_var, nx * ny), F32)
    return [c, c, s, s, w, w]


def exchange(faces):
    c_lo, c_hi, s_lo, s_hi, w_lo, w_hi = faces
    out = []
    for axis, lo_face, hi_face in (("chord", c_lo, c_hi), ("span", s_lo, s_hi), ("wall", w_lo, w_hi)):
        count = lax.axis_size(axis)
        forward = [(i, i + 1) for i in range(count - 1)]
        backward = [(i + 1, i) for i in range(count - 1)]
        out.append(lax.ppermute(hi_face, axis, forward))
        out.append(lax.ppermute(lo_face, axis, backward))
    return out


def local(sensitivity, diagonal, face_coef, upper_blocks, lower_blocks, iface_blocks, production,
          send_cell, target_cell, orient, iface_weight):
    n_span = lax.axis_size("span")
    n_var = sensitivity.shape[0]
    slots = send_cell.shape[-1]
    n_rows = n_span * slots
    shape = sensitivity.shape
    blk = (upper_blocks, lower_blocks, iface_blocks)
    send_row = send_cell.reshape(n_span, slots)
    orient_row = orient.reshape(n_span, slots)
    weight_row = iface_weight.reshape(n_span, slots)
    target_row = target_cell.reshape(n_span, slots)

    vmem = pl.BlockSpec(memory_space=pltpu.VMEM)
    smem = pl.BlockSpec(memory_space=pltpu.SMEM)
    adj_sds = jax.ShapeDtypeStruct(shape, F32)
    tgt_sds = jax.ShapeDtypeStruct((1, n_rows), jnp.int32)
    first_rows = jax.ShapeDtypeStruct((n_span, 1, (n_var + 1) * slots), F32)
    rows_sds = jax.ShapeDtypeStruct((n_span, 1, n_var * slots), F32)

    init = pl.pallas_call(
        init_kernel,
        out_shape=[adj_sds, first_rows] + face_shapes(shape),
        in_specs=[smem] * 3 + [vmem] * 6,
        out_specs=[vmem] * 8,
    )
    adj, rows, *faces = init(*blk, sensitivity, diagonal, send_row, orient_row, weight_row, target_row)

    first = pl.pallas_call(
        first_sweep_kernel,
        out_shape=[adj_sds, rows_sds, tgt_sds] + face_shapes(shape),
        in_specs=[smem] * 3 + [vmem] * 14,
        out_specs=[vmem] * 9,
    )
    step = pl.pallas_call(
        sweep_kernel,
        out_shape=[adj_sds, rows_sds, tgt_sds] + face_shapes(shape),
        in_specs=[smem] * 3 + [vmem] * 15,
        out_specs=[vmem] * 9,
    )
    last = pl.pallas_call(
        last_kernel,
        out_shape=[adj_sds, jax.ShapeDtypeStruct(production.shape, F32)],
        in_specs=[smem] * 3 + [vmem] * 13,
        out_specs=[vmem] * 2,
    )
    received = None
    for sweep in range(SWEEPS):
        halos = exchange(faces)
        incoming = lax.all_to_all(rows, "span", split_axis=0, concat_axis=0, tiled=True)
        if sweep == 0:
            adj, rows, received, *faces = first(*blk, adj, sensitivity, diagonal, face_coef, *halos,
                                                incoming, send_row, orient_row, weight_row)
        elif sweep < SWEEPS - 1:
            adj, rows, received, *faces = step(*blk, adj, sensitivity, diagonal, face_coef, *halos,
                                               incoming, received, send_row, orient_row, weight_row)
        else:
            adj, gradient = last(*blk, adj, sensitivity, diagonal, face_coef, *halos, incoming,
                                 received, production)
    return (adj, gradient)


def solution(mesh):
    placed = (
        P(None, "chord", "span", "wall"),
        P(None, "chord", "span", "wall"),
        P(None, "chord", "span", "wall"),
        P(),
        P(),
        P(),
        P("chord", "span", "wall"),
        P("chord", "span", "wall", None, None),
        P("chord", "span", "wall", None, None),
        P("chord", "span", "wall", None, None),
        P("chord", "span", "wall", None, None),
    )
    return jax.shard_map(
        local,
        mesh=mesh,
        in_specs=placed,
        out_specs=(P(None, "chord", "span", "wall"), P("chord", "span", "wall")),
        check_vma=False,
    )
```

```python
import jax
import jax.numpy as jnp
from jax import lax
from jax.experimental import pallas as pl
from jax.experimental.pallas import tpu as pltpu
from jax.sharding import PartitionSpec as P

SWEEPS = 3
F32 = jnp.float32
BF16 = jnp.bfloat16


def split3(x):
    p1 = x.astype(BF16)
    r1 = x - p1.astype(F32)
    p2 = r1.astype(BF16)
    p3 = (r1 - p2.astype(F32)).astype(BF16)
    return p1, p2, p3


def gather_rows(adj, send_ref, orient_ref, weight_ref, blk, n_var, lanes):
    rows = adj.shape[1] * adj.shape[2]
    cell = flat_row(send_ref[...])
    n_rows = cell.shape[1]
    row_of = cell // lanes
    lane_of = cell % lanes
    lane_hot = (lax.broadcasted_iota(jnp.int32, (lanes, n_rows), 0) == lane_of).astype(BF16)
    row_hot = (lax.broadcasted_iota(jnp.int32, (rows, n_rows), 0) == row_of).astype(F32)
    flat = adj.reshape(n_var * rows, lanes)
    picked = jnp.dot(jnp.concatenate(split3(flat), axis=1),
                     jnp.concatenate([lane_hot] * 3, axis=0), preferred_element_type=F32)
    src = jnp.sum(picked.reshape(n_var, rows, n_rows) * row_hot[None], axis=1)
    orient = flat_row(orient_ref[...])
    weight = flat_row(weight_ref[...])
    out = []
    for i in range(n_var):
        first = None
        second = None
        for j in range(n_var):
            a = blk[2][0, j, i] * src[j:j + 1]
            b = blk[2][1, j, i] * src[j:j + 1]
            first = a if first is None else first + a
            second = b if second is None else second + b
        out.append(jnp.where(orient == 1, second, first) * weight)
    return out


def flat_row(x):
    return jnp.concatenate([x[t:t + 1] for t in range(x.shape[0])], axis=1)


def to_chunks(rows_ref, pieces, slots):
    n_dest = rows_ref.shape[0]
    for t in range(n_dest):
        rows_ref[t] = jnp.concatenate([p[:, t * slots:(t + 1) * slots] for p in pieces], axis=1)


def from_chunks(inc, count, slots):
    n_src = inc.shape[0]
    return [jnp.concatenate([inc[s][:, v * slots:(v + 1) * slots] for s in range(n_src)], axis=1)
            for v in range(count)]


def wall_columns(adj):
    n_var, nx, ny, nz = adj.shape
    lo, hi = [], []
    for v in range(n_var):
        t = adj[v].reshape(nx * ny, nz).T
        lo.append(t[0:1])
        hi.append(t[nz - 1:nz])
    return jnp.concatenate(lo, axis=0), jnp.concatenate(hi, axis=0)


def write_faces(adj, faces):
    c_lo, c_hi, s_lo, s_hi, w_buf, wall_me = faces
    nx, ny, nz = adj.shape[1], adj.shape[2], adj.shape[3]
    j_idx = lax.broadcasted_iota(jnp.int32, adj.shape, 2)
    c_lo[...] = adj[:, 0:1]
    c_hi[...] = adj[:, nx - 1:nx]
    s_lo[...] = jnp.sum(jnp.where(j_idx == 0, adj, 0.0), axis=2)
    s_hi[...] = jnp.sum(jnp.where(j_idx == ny - 1, adj, 0.0), axis=2)
    lo, hi = wall_columns(adj)
    me = wall_me[0]
    n_wall = w_buf.shape[0]
    lo = jnp.concatenate([lo[v:v + 1] for v in range(lo.shape[0])], axis=1)
    hi = jnp.concatenate([hi[v:v + 1] for v in range(hi.shape[0])], axis=1)
    for t in range(n_wall):
        w_buf[t] = jnp.where(me + 1 == t, hi, jnp.where(me - 1 == t, lo, 0.0))


def wall_halos(w_inc, wall_me, n_var):
    me = wall_me[0]
    n_wall, _, width = w_inc.shape
    below = None
    above = None
    for t in range(n_wall):
        b = jnp.where(me - 1 == t, w_inc[t], 0.0)
        a = jnp.where(me + 1 == t, w_inc[t], 0.0)
        below = b if below is None else below + b
        above = a if above is None else above + a
    rows = width // n_var
    unflat = lambda x: jnp.concatenate([x[:, v * rows:(v + 1) * rows] for v in range(n_var)], axis=0)
    return unflat(below), unflat(above)


def init_kernel(ub_ref, lb_ref, ib_ref, wall_me, sens_ref, diag_ref, send_ref, orient_ref, weight_ref, tgt_ref,
                adj_ref, rows_ref, c_lo, c_hi, s_lo, s_hi, w_buf):
    n_var = sens_ref.shape[0]
    lanes = sens_ref.shape[3]
    slots = send_ref.shape[1]
    blk_ref = (ub_ref, lb_ref, ib_ref)
    adj = sens_ref[...] / diag_ref[...]
    adj_ref[...] = adj
    write_faces(adj, (c_lo, c_hi, s_lo, s_hi, w_buf, wall_me))
    pieces = gather_rows(adj, send_ref, orient_ref, weight_ref, blk_ref, n_var, lanes)
    to_chunks(rows_ref, pieces + [flat_row(tgt_ref[...]).astype(F32)], slots)


def sweep_body(blk, adj, sens, diag, face, halos, incoming, cell):
    n_var, nx, ny, nz = adj.shape
    rows = nx * ny
    h_c_lo, h_c_hi, h_s_lo, h_s_hi, h_w_lo, h_w_hi = halos
    j_idx = lax.broadcasted_iota(jnp.int32, adj.shape, 2)
    k_idx = lax.broadcasted_iota(jnp.int32, adj.shape, 3)
    kk = lax.broadcasted_iota(jnp.int32, (nz, rows), 0)
    wall = []
    for v in range(n_var):
        z = jnp.where(kk == 0, h_w_lo[v:v + 1], jnp.where(kk == nz - 1, h_w_hi[v:v + 1], 0.0))
        wall.append(z.T.reshape(nx, ny, nz))
    wall = jnp.stack(wall, axis=0)
    up = [
        jnp.concatenate([adj[:, 1:], h_c_hi], axis=1),
        jnp.where(j_idx == ny - 1, h_s_hi[:, :, None, :], pltpu.roll(adj, ny - 1, 2)),
        jnp.where(k_idx == nz - 1, wall, pltpu.roll(adj, nz - 1, 3)),
    ]
    lo = [
        jnp.concatenate([h_c_lo, adj[:, :-1]], axis=1),
        jnp.where(j_idx == 0, h_s_lo[:, :, None, :], pltpu.roll(adj, 1, 2)),
        jnp.where(k_idx == 0, wall, pltpu.roll(adj, 1, 3)),
    ]
    n_rows = incoming.shape[1]
    row_of = cell // nz
    lane_of = cell % nz
    row_hot = (lax.broadcasted_iota(jnp.int32, (rows, n_rows), 0) == row_of).astype(BF16)
    lane_hot = (lax.broadcasted_iota(jnp.int32, (nz, n_rows), 0) == lane_of).astype(BF16)
    lhs = jnp.concatenate([(row_hot[None] * part[:, None, :]).reshape(n_var * rows, n_rows)
                           for part in split3(incoming)], axis=1)
    coupled = lax.dot_general(lhs, jnp.concatenate([lane_hot] * 3, axis=1), (((1,), (1,)), ((), ())),
                              preferred_element_type=F32)
    coupled = coupled.reshape(n_var, nx, ny, nz)
    new = []
    for i in range(n_var):
        applied = diag[i] * adj[i] + coupled[i]
        for d in range(3):
            acc = None
            for j in range(n_var):
                t = blk[0][d, j, i] * up[d][j] + blk[1][d, j, i] * lo[d][j]
                acc = t if acc is None else acc + t
            applied = applied + face[d] * acc
        new.append(adj[i] + (sens[i] - applied) / diag[i])
    return jnp.stack(new, axis=0)


def sweep_kernel(ub_ref, lb_ref, ib_ref, wall_me, adj_ref, sens_ref, diag_ref, face_ref, hcl, hch, hsl, hsh, w_inc,
                 inc_ref, tgt_ref, send_ref, orient_ref, weight_ref,
                 out_ref, rows_ref, tgt_out, c_lo, c_hi, s_lo, s_hi, w_buf):
    n_var = adj_ref.shape[0]
    lanes = adj_ref.shape[3]
    slots = send_ref.shape[1]
    blk_ref = (ub_ref, lb_ref, ib_ref)
    halos = (hcl[...], hch[...], hsl[...], hsh[...]) + wall_halos(w_inc[...], wall_me, n_var)
    inc = inc_ref[...]
    if tgt_ref is None:
        got = from_chunks(inc, n_var + 1, slots)
        cell = got[n_var].astype(jnp.int32)
    else:
        got = from_chunks(inc, n_var, slots)
        cell = tgt_ref[...]
    tgt_out[...] = cell
    new = sweep_body(blk_ref, adj_ref[...], sens_ref[...], diag_ref[...], face_ref[...], halos,
                     jnp.concatenate(got[:n_var], axis=0), cell)
    out_ref[...] = new
    write_faces(new, (c_lo, c_hi, s_lo, s_hi, w_buf, wall_me))
    to_chunks(rows_ref, gather_rows(new, send_ref, orient_ref, weight_ref, blk_ref, n_var, lanes), slots)


def first_sweep_kernel(ub_ref, lb_ref, ib_ref, wall_me, adj_ref, sens_ref, diag_ref, face_ref, hcl, hch, hsl, hsh,
                       w_inc, inc_ref, send_ref, orient_ref, weight_ref, *outs):
    sweep_kernel(ub_ref, lb_ref, ib_ref, wall_me, adj_ref, sens_ref, diag_ref, face_ref, hcl, hch, hsl, hsh, w_inc,
                 inc_ref, None, send_ref, orient_ref, weight_ref, *outs)


def last_kernel(ub_ref, lb_ref, ib_ref, wall_me, adj_ref, sens_ref, diag_ref, face_ref, hcl, hch, hsl, hsh, w_inc,
                inc_ref, tgt_ref, prod_ref, out_ref, grad_ref):
    n_var = adj_ref.shape[0]
    slots = inc_ref.shape[2] // n_var
    blk_ref = (ub_ref, lb_ref, ib_ref)
    halos = (hcl[...], hch[...], hsl[...], hsh[...]) + wall_halos(w_inc[...], wall_me, n_var)
    got = from_chunks(inc_ref[...], n_var, slots)
    new = sweep_body(blk_ref, adj_ref[...], sens_ref[...], diag_ref[...], face_ref[...], halos,
                     jnp.concatenate(got, axis=0), tgt_ref[...])
    out_ref[...] = new
    grad_ref[...] = prod_ref[...] * new[n_var - 1]


def face_shapes(shape, n_wall):
    n_var, nx, ny, nz = shape
    c = jax.ShapeDtypeStruct((n_var, 1, ny, nz), F32)
    s = jax.ShapeDtypeStruct((n_var, nx, nz), F32)
    w = jax.ShapeDtypeStruct((n_wall, 1, n_var * nx * ny), F32)
    return [c, c, s, s, w]


def exchange(faces):
    c_lo, c_hi, s_lo, s_hi, w_buf = faces
    out = []
    for axis, lo_face, hi_face in (("chord", c_lo, c_hi), ("span", s_lo, s_hi)):
        count = lax.axis_size(axis)
        forward = [(i, i + 1) for i in range(count - 1)]
        backward = [(i + 1, i) for i in range(count - 1)]
        out.append(lax.ppermute(hi_face, axis, forward))
        out.append(lax.ppermute(lo_face, axis, backward))
    out.append(lax.all_to_all(w_buf, "wall", split_axis=0, concat_axis=0, tiled=True))
    return out


def local(sensitivity, diagonal, face_coef, upper_blocks, lower_blocks, iface_blocks, production,
          send_cell, target_cell, orient, iface_weight):
    n_span = lax.axis_size("span")
    n_var = sensitivity.shape[0]
    slots = send_cell.shape[-1]
    n_rows = n_span * slots
    shape = sensitivity.shape
    n_wall = lax.axis_size("wall")
    wall_me = lax.axis_index("wall").astype(jnp.int32).reshape(1)
    blk = (upper_blocks, lower_blocks, iface_blocks, wall_me)
    send_row = send_cell.reshape(n_span, slots)
    orient_row = orient.reshape(n_span, slots)
    weight_row = iface_weight.reshape(n_span, slots)
    target_row = target_cell.reshape(n_span, slots)

    vmem = pl.BlockSpec(memory_space=pltpu.VMEM)
    smem = pl.BlockSpec(memory_space=pltpu.SMEM)
    adj_sds = jax.ShapeDtypeStruct(shape, F32)
    tgt_sds = jax.ShapeDtypeStruct((1, n_rows), jnp.int32)
    first_rows = jax.ShapeDtypeStruct((n_span, 1, (n_var + 1) * slots), F32)
    rows_sds = jax.ShapeDtypeStruct((n_span, 1, n_var * slots), F32)

    init = pl.pallas_call(
        init_kernel,
        out_shape=[adj_sds, first_rows] + face_shapes(shape, n_wall),
        in_specs=[smem] * 4 + [vmem] * 6,
        out_specs=[vmem] * 7,
    )
    adj, rows, *faces = init(*blk, sensitivity, diagonal, send_row, orient_row, weight_row, target_row)

    first = pl.pallas_call(
        first_sweep_kernel,
        out_shape=[adj_sds, rows_sds, tgt_sds] + face_shapes(shape, n_wall),
        in_specs=[smem] * 4 + [vmem] * 13,
        out_specs=[vmem] * 8,
    )
    step = pl.pallas_call(
        sweep_kernel,
        out_shape=[adj_sds, rows_sds, tgt_sds] + face_shapes(shape, n_wall),
        in_specs=[smem] * 4 + [vmem] * 14,
        out_specs=[vmem] * 8,
    )
    last = pl.pallas_call(
        last_kernel,
        out_shape=[adj_sds, jax.ShapeDtypeStruct(production.shape, F32)],
        in_specs=[smem] * 4 + [vmem] * 12,
        out_specs=[vmem] * 2,
    )
    received = None
    for sweep in range(SWEEPS):
        halos = exchange(faces)
        incoming = lax.all_to_all(rows, "span", split_axis=0, concat_axis=0, tiled=True)
        if sweep == 0:
            adj, rows, received, *faces = first(*blk, adj, sensitivity, diagonal, face_coef, *halos,
                                                incoming, send_row, orient_row, weight_row)
        elif sweep < SWEEPS - 1:
            adj, rows, received, *faces = step(*blk, adj, sensitivity, diagonal, face_coef, *halos,
                                               incoming, received, send_row, orient_row, weight_row)
        else:
            adj, gradient = last(*blk, adj, sensitivity, diagonal, face_coef, *halos, incoming,
                                 received, production)
    return (adj, gradient)


def solution(mesh):
    placed = (
        P(None, "chord", "span", "wall"),
        P(None, "chord", "span", "wall"),
        P(None, "chord", "span", "wall"),
        P(),
        P(),
        P(),
        P("chord", "span", "wall"),
        P("chord", "span", "wall", None, None),
        P("chord", "span", "wall", None, None),
        P("chord", "span", "wall", None, None),
        P("chord", "span", "wall", None, None),
    )
    return jax.shard_map(
        local,
        mesh=mesh,
        in_specs=placed,
        out_specs=(P(None, "chord", "span", "wall"), P("chord", "span", "wall")),
        check_vma=False,
    )
```

```python
import jax
import jax.numpy as jnp
from jax import lax
from jax.experimental import pallas as pl
from jax.experimental.pallas import tpu as pltpu
from jax.sharding import PartitionSpec as P

SWEEPS = 3
F32 = jnp.float32
BF16 = jnp.bfloat16


def split3(x):
    p1 = x.astype(BF16)
    r1 = x - p1.astype(F32)
    p2 = r1.astype(BF16)
    p3 = (r1 - p2.astype(F32)).astype(BF16)
    return p1, p2, p3


def gather_rows(adj, send_ref, orient_ref, weight_ref, blk, n_var, lanes):
    rows = adj.shape[1] * adj.shape[2]
    cell = flat_row(send_ref[...])
    n_rows = cell.shape[1]
    row_of = cell // lanes
    lane_of = cell % lanes
    lane_hot = (lax.broadcasted_iota(jnp.int32, (lanes, n_rows), 0) == lane_of).astype(BF16)
    row_hot = (lax.broadcasted_iota(jnp.int32, (rows, n_rows), 0) == row_of).astype(F32)
    flat = adj.reshape(n_var * rows, lanes)
    picked = jnp.dot(jnp.concatenate(split3(flat), axis=1),
                     jnp.concatenate([lane_hot] * 3, axis=0), preferred_element_type=F32)
    src = jnp.sum(picked.reshape(n_var, rows, n_rows) * row_hot[None], axis=1)
    orient = flat_row(orient_ref[...])
    weight = flat_row(weight_ref[...])
    out = []
    for i in range(n_var):
        first = None
        second = None
        for j in range(n_var):
            a = blk[2][0, j, i] * src[j:j + 1]
            b = blk[2][1, j, i] * src[j:j + 1]
            first = a if first is None else first + a
            second = b if second is None else second + b
        out.append(jnp.where(orient == 1, second, first) * weight)
    return out


def flat_row(x):
    return jnp.concatenate([x[t:t + 1] for t in range(x.shape[0])], axis=1)


def to_chunks(rows_ref, pieces, slots):
    n_dest = rows_ref.shape[0]
    for t in range(n_dest):
        rows_ref[t] = jnp.concatenate([p[:, t * slots:(t + 1) * slots] for p in pieces], axis=1)


def from_chunks(inc, count, slots):
    n_src = inc.shape[0]
    return [jnp.concatenate([inc[s][:, v * slots:(v + 1) * slots] for s in range(n_src)], axis=1)
            for v in range(count)]


def wall_columns(adj):
    n_var, nx, ny, nz = adj.shape
    lo, hi = [], []
    for v in range(n_var):
        t = adj[v].reshape(nx * ny, nz).T
        lo.append(t[0:1])
        hi.append(t[nz - 1:nz])
    return jnp.concatenate(lo, axis=0), jnp.concatenate(hi, axis=0)


def write_faces(adj, faces):
    c_lo, c_hi, s_lo, s_hi, w_buf, wall_me = faces
    nx, ny, nz = adj.shape[1], adj.shape[2], adj.shape[3]
    j_idx = lax.broadcasted_iota(jnp.int32, adj.shape, 2)
    c_lo[...] = adj[:, 0:1]
    c_hi[...] = adj[:, nx - 1:nx]
    s_lo[...] = jnp.sum(jnp.where(j_idx == 0, adj, 0.0), axis=2)
    s_hi[...] = jnp.sum(jnp.where(j_idx == ny - 1, adj, 0.0), axis=2)
    lo, hi = wall_columns(adj)
    me = wall_me[0]
    n_wall = w_buf.shape[0]
    lo = jnp.concatenate([lo[v:v + 1] for v in range(lo.shape[0])], axis=1)
    hi = jnp.concatenate([hi[v:v + 1] for v in range(hi.shape[0])], axis=1)
    for t in range(n_wall):
        w_buf[t] = jnp.where(me + 1 == t, hi, jnp.where(me - 1 == t, lo, 0.0))


def wall_halos(w_inc, wall_me, n_var):
    me = wall_me[0]
    n_wall, _, width = w_inc.shape
    below = None
    above = None
    for t in range(n_wall):
        b = jnp.where(me - 1 == t, w_inc[t], 0.0)
        a = jnp.where(me + 1 == t, w_inc[t], 0.0)
        below = b if below is None else below + b
        above = a if above is None else above + a
    rows = width // n_var
    unflat = lambda x: jnp.concatenate([x[:, v * rows:(v + 1) * rows] for v in range(n_var)], axis=0)
    return unflat(below), unflat(above)


def init_kernel(ub_ref, lb_ref, ib_ref, wall_me, sens_ref, diag_ref, send_ref, orient_ref, weight_ref, tgt_ref,
                adj_ref, rows_ref, c_lo, c_hi, s_lo, s_hi, w_buf):
    n_var = sens_ref.shape[0]
    lanes = sens_ref.shape[3]
    slots = send_ref.shape[1]
    blk_ref = (ub_ref, lb_ref, ib_ref)
    adj = sens_ref[...] / diag_ref[...]
    adj_ref[...] = adj
    write_faces(adj, (c_lo, c_hi, s_lo, s_hi, w_buf, wall_me))
    pieces = gather_rows(adj, send_ref, orient_ref, weight_ref, blk_ref, n_var, lanes)
    to_chunks(rows_ref, pieces + [flat_row(tgt_ref[...]).astype(F32)], slots)


def sweep_body(blk, adj, sens, diag, face, halos, incoming, cell):
    n_var, nx, ny, nz = adj.shape
    rows = nx * ny
    h_c_lo, h_c_hi, h_s_lo, h_s_hi, h_w_lo, h_w_hi = halos
    j_idx = lax.broadcasted_iota(jnp.int32, adj.shape, 2)
    k_idx = lax.broadcasted_iota(jnp.int32, adj.shape, 3)
    kk = lax.broadcasted_iota(jnp.int32, (nz, rows), 0)
    wall = []
    for v in range(n_var):
        z = jnp.where(kk == 0, h_w_lo[v:v + 1], jnp.where(kk == nz - 1, h_w_hi[v:v + 1], 0.0))
        wall.append(z.T.reshape(nx, ny, nz))
    wall = jnp.stack(wall, axis=0)
    up = [
        jnp.concatenate([adj[:, 1:], h_c_hi], axis=1),
        jnp.where(j_idx == ny - 1, h_s_hi[:, :, None, :], pltpu.roll(adj, ny - 1, 2)),
        jnp.where(k_idx == nz - 1, wall, pltpu.roll(adj, nz - 1, 3)),
    ]
    lo = [
        jnp.concatenate([h_c_lo, adj[:, :-1]], axis=1),
        jnp.where(j_idx == 0, h_s_lo[:, :, None, :], pltpu.roll(adj, 1, 2)),
        jnp.where(k_idx == 0, wall, pltpu.roll(adj, 1, 3)),
    ]
    n_rows = incoming.shape[1]
    row_of = cell // nz
    lane_of = cell % nz
    row_hot = (lax.broadcasted_iota(jnp.int32, (rows, n_rows), 0) == row_of).astype(BF16)
    lane_hot = (lax.broadcasted_iota(jnp.int32, (nz, n_rows), 0) == lane_of).astype(BF16)
    lhs = jnp.concatenate([(row_hot[None] * part[:, None, :]).reshape(n_var * rows, n_rows)
                           for part in split3(incoming)], axis=1)
    coupled = lax.dot_general(lhs, jnp.concatenate([lane_hot] * 3, axis=1), (((1,), (1,)), ((), ())),
                              preferred_element_type=F32)
    coupled = coupled.reshape(n_var, nx, ny, nz)
    new = []
    for i in range(n_var):
        applied = diag[i] * adj[i] + coupled[i]
        for d in range(3):
            acc = None
            for j in range(n_var):
                t = blk[0][d, j, i] * up[d][j] + blk[1][d, j, i] * lo[d][j]
                acc = t if acc is None else acc + t
            applied = applied + face[d] * acc
        new.append(adj[i] + (sens[i] - applied) / diag[i])
    return jnp.stack(new, axis=0)


def sweep_kernel(ub_ref, lb_ref, ib_ref, wall_me, adj_ref, sens_ref, diag_ref, face_ref, hcl, hch, hsl, hsh, w_inc,
                 inc_ref, tgt_ref, send_ref, orient_ref, weight_ref,
                 out_ref, rows_ref, tgt_out, c_lo, c_hi, s_lo, s_hi, w_buf):
    n_var = adj_ref.shape[0]
    lanes = adj_ref.shape[3]
    slots = send_ref.shape[1]
    blk_ref = (ub_ref, lb_ref, ib_ref)
    halos = (hcl[...], hch[...], hsl[...], hsh[...]) + wall_halos(w_inc[...], wall_me, n_var)
    inc = inc_ref[...]
    if tgt_ref is None:
        got = from_chunks(inc, n_var + 1, slots)
        cell = got[n_var].astype(jnp.int32)
    else:
        got = from_chunks(inc, n_var, slots)
        cell = tgt_ref[...]
    tgt_out[...] = cell
    new = sweep_body(blk_ref, adj_ref[...], sens_ref[...], diag_ref[...], face_ref[...], halos,
                     jnp.concatenate(got[:n_var], axis=0), cell)
    out_ref[...] = new
    write_faces(new, (c_lo, c_hi, s_lo, s_hi, w_buf, wall_me))
    to_chunks(rows_ref, gather_rows(new, send_ref, orient_ref, weight_ref, blk_ref, n_var, lanes), slots)


def first_sweep_kernel(ub_ref, lb_ref, ib_ref, wall_me, adj_ref, sens_ref, diag_ref, face_ref, hcl, hch, hsl, hsh,
                       w_inc, inc_ref, send_ref, orient_ref, weight_ref, *outs):
    sweep_kernel(ub_ref, lb_ref, ib_ref, wall_me, adj_ref, sens_ref, diag_ref, face_ref, hcl, hch, hsl, hsh, w_inc,
                 inc_ref, None, send_ref, orient_ref, weight_ref, *outs)


def last_kernel(ub_ref, lb_ref, ib_ref, wall_me, adj_ref, sens_ref, diag_ref, face_ref, hcl, hch, hsl, hsh, w_inc,
                inc_ref, tgt_ref, prod_ref, out_ref, grad_ref):
    n_var = adj_ref.shape[0]
    slots = inc_ref.shape[2] // n_var
    blk_ref = (ub_ref, lb_ref, ib_ref)
    halos = (hcl[...], hch[...], hsl[...], hsh[...]) + wall_halos(w_inc[...], wall_me, n_var)
    got = from_chunks(inc_ref[...], n_var, slots)
    new = sweep_body(blk_ref, adj_ref[...], sens_ref[...], diag_ref[...], face_ref[...], halos,
                     jnp.concatenate(got, axis=0), tgt_ref[...])
    out_ref[...] = new
    grad_ref[...] = prod_ref[...] * new[n_var - 1]


def face_shapes(shape, n_wall):
    n_var, nx, ny, nz = shape
    c = jax.ShapeDtypeStruct((n_var, 1, ny, nz), F32)
    s = jax.ShapeDtypeStruct((n_var, nx, nz), F32)
    w = jax.ShapeDtypeStruct((n_wall, 1, n_var * nx * ny), F32)
    return [c, c, s, s, w]


def exchange(faces):
    c_lo, c_hi, s_lo, s_hi, w_buf = faces
    out = []
    for axis, lo_face, hi_face in (("chord", c_lo, c_hi), ("span", s_lo, s_hi)):
        count = lax.axis_size(axis)
        forward = [(i, i + 1) for i in range(count - 1)]
        backward = [(i + 1, i) for i in range(count - 1)]
        out.append(lax.ppermute(hi_face, axis, forward))
        out.append(lax.ppermute(lo_face, axis, backward))
    out.append(lax.all_to_all(w_buf, "wall", split_axis=0, concat_axis=0, tiled=True))
    return out


def local(sensitivity, diagonal, face_coef, upper_blocks, lower_blocks, iface_blocks, production,
          send_cell, target_cell, orient, iface_weight):
    n_span = lax.axis_size("span")
    n_var = sensitivity.shape[0]
    slots = send_cell.shape[-1]
    n_rows = n_span * slots
    shape = sensitivity.shape
    n_wall = lax.axis_size("wall")
    wall_me = lax.axis_index("wall").astype(jnp.int32).reshape(1)
    blk = (upper_blocks, lower_blocks, iface_blocks, wall_me)
    send_row = send_cell.reshape(n_span, slots)
    orient_row = orient.reshape(n_span, slots)
    weight_row = iface_weight.reshape(n_span, slots)
    target_row = target_cell.reshape(n_span, slots)

    vmem = pl.BlockSpec(memory_space=pltpu.VMEM)
    smem = pl.BlockSpec(memory_space=pltpu.SMEM)
    adj_sds = jax.ShapeDtypeStruct(shape, F32)
    tgt_sds = jax.ShapeDtypeStruct((1, n_rows), jnp.int32)
    first_rows = jax.ShapeDtypeStruct((n_span, 1, (n_var + 1) * slots), F32)
    rows_sds = jax.ShapeDtypeStruct((n_span, 1, n_var * slots), F32)

    init = pl.pallas_call(
        init_kernel,
        out_shape=[adj_sds, first_rows] + face_shapes(shape, n_wall),
        in_specs=[smem] * 4 + [vmem] * 6,
        out_specs=[vmem] * 7,
    )
    adj, rows, *faces = init(*blk, sensitivity, diagonal, send_row, orient_row, weight_row, target_row)

    first = pl.pallas_call(
        first_sweep_kernel,
        out_shape=[adj_sds, rows_sds, tgt_sds] + face_shapes(shape, n_wall),
        in_specs=[smem] * 4 + [vmem] * 13,
        out_specs=[vmem] * 8,
    )
    step = pl.pallas_call(
        sweep_kernel,
        out_shape=[adj_sds, rows_sds, tgt_sds] + face_shapes(shape, n_wall),
        in_specs=[smem] * 4 + [vmem] * 14,
        out_specs=[vmem] * 8,
    )
    last = pl.pallas_call(
        last_kernel,
        out_shape=[adj_sds, jax.ShapeDtypeStruct(production.shape, F32)],
        in_specs=[smem] * 4 + [vmem] * 12,
        out_specs=[vmem] * 2,
    )
    received = None
    for sweep in range(SWEEPS):
        halos = exchange(faces)
        rows, halos[2], halos[3] = lax.optimization_barrier((rows, halos[2], halos[3]))
        incoming = lax.all_to_all(rows, "span", split_axis=0, concat_axis=0, tiled=True)
        if sweep == 0:
            adj, rows, received, *faces = first(*blk, adj, sensitivity, diagonal, face_coef, *halos,
                                                incoming, send_row, orient_row, weight_row)
        elif sweep < SWEEPS - 1:
            adj, rows, received, *faces = step(*blk, adj, sensitivity, diagonal, face_coef, *halos,
                                               incoming, received, send_row, orient_row, weight_row)
        else:
            adj, gradient = last(*blk, adj, sensitivity, diagonal, face_coef, *halos, incoming,
                                 received, production)
    return (adj, gradient)


def solution(mesh):
    placed = (
        P(None, "chord", "span", "wall"),
        P(None, "chord", "span", "wall"),
        P(None, "chord", "span", "wall"),
        P(),
        P(),
        P(),
        P("chord", "span", "wall"),
        P("chord", "span", "wall", None, None),
        P("chord", "span", "wall", None, None),
        P("chord", "span", "wall", None, None),
        P("chord", "span", "wall", None, None),
    )
    return jax.shard_map(
        local,
        mesh=mesh,
        in_specs=placed,
        out_specs=(P(None, "chord", "span", "wall"), P("chord", "span", "wall")),
        check_vma=False,
    )
```

```python
import jax
import jax.numpy as jnp
from jax import lax
from jax.experimental import pallas as pl
from jax.experimental.pallas import tpu as pltpu
from jax.sharding import PartitionSpec as P

SWEEPS = 3
F32 = jnp.float32
BF16 = jnp.bfloat16


def split3(x):
    p1 = x.astype(BF16)
    p2 = (x - p1.astype(F32)).astype(BF16)
    return p1, p2


def gather_rows(adj, send_ref, orient_ref, weight_ref, blk, n_var, lanes):
    rows = adj.shape[1] * adj.shape[2]
    cell = flat_row(send_ref[...])
    n_rows = cell.shape[1]
    row_of = cell // lanes
    lane_of = cell % lanes
    lane_hot = (lax.broadcasted_iota(jnp.int32, (lanes, n_rows), 0) == lane_of).astype(BF16)
    row_hot = (lax.broadcasted_iota(jnp.int32, (rows, n_rows), 0) == row_of).astype(F32)
    flat = adj.reshape(n_var * rows, lanes)
    picked = jnp.dot(jnp.concatenate(split3(flat), axis=1),
                     jnp.concatenate([lane_hot] * 2, axis=0), preferred_element_type=F32)
    src = jnp.sum(picked.reshape(n_var, rows, n_rows) * row_hot[None], axis=1)
    orient = flat_row(orient_ref[...])
    weight = flat_row(weight_ref[...])
    out = []
    for i in range(n_var):
        first = None
        second = None
        for j in range(n_var):
            a = blk[2][0, j, i] * src[j:j + 1]
            b = blk[2][1, j, i] * src[j:j + 1]
            first = a if first is None else first + a
            second = b if second is None else second + b
        out.append(jnp.where(orient == 1, second, first) * weight)
    return out


def flat_row(x):
    return jnp.concatenate([x[t:t + 1] for t in range(x.shape[0])], axis=1)


def to_chunks(rows_ref, pieces, slots):
    n_dest = rows_ref.shape[0]
    for t in range(n_dest):
        rows_ref[t] = jnp.concatenate([p[:, t * slots:(t + 1) * slots] for p in pieces], axis=1)


def from_chunks(inc, count, slots):
    n_src = inc.shape[0]
    return [jnp.concatenate([inc[s][:, v * slots:(v + 1) * slots] for s in range(n_src)], axis=1)
            for v in range(count)]


def wall_columns(adj):
    n_var, nx, ny, nz = adj.shape
    lo, hi = [], []
    for v in range(n_var):
        t = adj[v].reshape(nx * ny, nz).T
        lo.append(t[0:1])
        hi.append(t[nz - 1:nz])
    return jnp.concatenate(lo, axis=0), jnp.concatenate(hi, axis=0)


def write_faces(adj, faces):
    c_lo, c_hi, s_lo, s_hi, w_buf, wall_me = faces
    nx, ny, nz = adj.shape[1], adj.shape[2], adj.shape[3]
    j_idx = lax.broadcasted_iota(jnp.int32, adj.shape, 2)
    c_lo[...] = adj[:, 0:1]
    c_hi[...] = adj[:, nx - 1:nx]
    s_lo[...] = jnp.sum(jnp.where(j_idx == 0, adj, 0.0), axis=2)
    s_hi[...] = jnp.sum(jnp.where(j_idx == ny - 1, adj, 0.0), axis=2)
    lo, hi = wall_columns(adj)
    me = wall_me[0]
    n_wall = w_buf.shape[0]
    lo = jnp.concatenate([lo[v:v + 1] for v in range(lo.shape[0])], axis=1)
    hi = jnp.concatenate([hi[v:v + 1] for v in range(hi.shape[0])], axis=1)
    for t in range(n_wall):
        w_buf[t] = jnp.where(me + 1 == t, hi, jnp.where(me - 1 == t, lo, 0.0))


def wall_halos(w_inc, wall_me, n_var):
    me = wall_me[0]
    n_wall, _, width = w_inc.shape
    below = None
    above = None
    for t in range(n_wall):
        b = jnp.where(me - 1 == t, w_inc[t], 0.0)
        a = jnp.where(me + 1 == t, w_inc[t], 0.0)
        below = b if below is None else below + b
        above = a if above is None else above + a
    rows = width // n_var
    unflat = lambda x: jnp.concatenate([x[:, v * rows:(v + 1) * rows] for v in range(n_var)], axis=0)
    return unflat(below), unflat(above)


def init_kernel(ub_ref, lb_ref, ib_ref, wall_me, sens_ref, diag_ref, send_ref, orient_ref, weight_ref, tgt_ref,
                adj_ref, rows_ref, c_lo, c_hi, s_lo, s_hi, w_buf):
    n_var = sens_ref.shape[0]
    lanes = sens_ref.shape[3]
    slots = send_ref.shape[1]
    blk_ref = (ub_ref, lb_ref, ib_ref)
    adj = sens_ref[...] / diag_ref[...]
    adj_ref[...] = adj
    write_faces(adj, (c_lo, c_hi, s_lo, s_hi, w_buf, wall_me))
    pieces = gather_rows(adj, send_ref, orient_ref, weight_ref, blk_ref, n_var, lanes)
    to_chunks(rows_ref, pieces + [flat_row(tgt_ref[...]).astype(F32)], slots)


def sweep_body(blk, adj, sens, diag, face, halos, incoming, cell):
    n_var, nx, ny, nz = adj.shape
    rows = nx * ny
    h_c_lo, h_c_hi, h_s_lo, h_s_hi, h_w_lo, h_w_hi = halos
    j_idx = lax.broadcasted_iota(jnp.int32, adj.shape, 2)
    k_idx = lax.broadcasted_iota(jnp.int32, adj.shape, 3)
    kk = lax.broadcasted_iota(jnp.int32, (nz, rows), 0)
    wall = []
    for v in range(n_var):
        z = jnp.where(kk == 0, h_w_lo[v:v + 1], jnp.where(kk == nz - 1, h_w_hi[v:v + 1], 0.0))
        wall.append(z.T.reshape(nx, ny, nz))
    wall = jnp.stack(wall, axis=0)
    up = [
        jnp.concatenate([adj[:, 1:], h_c_hi], axis=1),
        jnp.where(j_idx == ny - 1, h_s_hi[:, :, None, :], pltpu.roll(adj, ny - 1, 2)),
        jnp.where(k_idx == nz - 1, wall, pltpu.roll(adj, nz - 1, 3)),
    ]
    lo = [
        jnp.concatenate([h_c_lo, adj[:, :-1]], axis=1),
        jnp.where(j_idx == 0, h_s_lo[:, :, None, :], pltpu.roll(adj, 1, 2)),
        jnp.where(k_idx == 0, wall, pltpu.roll(adj, 1, 3)),
    ]
    n_rows = incoming.shape[1]
    row_of = cell // nz
    lane_of = cell % nz
    row_hot = (lax.broadcasted_iota(jnp.int32, (rows, n_rows), 0) == row_of).astype(BF16)
    lane_hot = (lax.broadcasted_iota(jnp.int32, (nz, n_rows), 0) == lane_of).astype(BF16)
    lhs = jnp.concatenate([(row_hot[None] * part[:, None, :]).reshape(n_var * rows, n_rows)
                           for part in split3(incoming)], axis=1)
    coupled = lax.dot_general(lhs, jnp.concatenate([lane_hot] * 2, axis=1), (((1,), (1,)), ((), ())),
                              preferred_element_type=F32)
    coupled = coupled.reshape(n_var, nx, ny, nz)
    new = []
    for i in range(n_var):
        applied = diag[i] * adj[i] + coupled[i]
        for d in range(3):
            acc = None
            for j in range(n_var):
                t = blk[0][d, j, i] * up[d][j] + blk[1][d, j, i] * lo[d][j]
                acc = t if acc is None else acc + t
            applied = applied + face[d] * acc
        new.append(adj[i] + (sens[i] - applied) / diag[i])
    return jnp.stack(new, axis=0)


def sweep_kernel(ub_ref, lb_ref, ib_ref, wall_me, adj_ref, sens_ref, diag_ref, face_ref, hcl, hch, hsl, hsh, w_inc,
                 inc_ref, tgt_ref, send_ref, orient_ref, weight_ref,
                 out_ref, rows_ref, tgt_out, c_lo, c_hi, s_lo, s_hi, w_buf):
    n_var = adj_ref.shape[0]
    lanes = adj_ref.shape[3]
    slots = send_ref.shape[1]
    blk_ref = (ub_ref, lb_ref, ib_ref)
    halos = (hcl[...], hch[...], hsl[...], hsh[...]) + wall_halos(w_inc[...], wall_me, n_var)
    inc = inc_ref[...]
    if tgt_ref is None:
        got = from_chunks(inc, n_var + 1, slots)
        cell = got[n_var].astype(jnp.int32)
    else:
        got = from_chunks(inc, n_var, slots)
        cell = tgt_ref[...]
    tgt_out[...] = cell
    new = sweep_body(blk_ref, adj_ref[...], sens_ref[...], diag_ref[...], face_ref[...], halos,
                     jnp.concatenate(got[:n_var], axis=0), cell)
    out_ref[...] = new
    write_faces(new, (c_lo, c_hi, s_lo, s_hi, w_buf, wall_me))
    to_chunks(rows_ref, gather_rows(new, send_ref, orient_ref, weight_ref, blk_ref, n_var, lanes), slots)


def first_sweep_kernel(ub_ref, lb_ref, ib_ref, wall_me, adj_ref, sens_ref, diag_ref, face_ref, hcl, hch, hsl, hsh,
                       w_inc, inc_ref, send_ref, orient_ref, weight_ref, *outs):
    sweep_kernel(ub_ref, lb_ref, ib_ref, wall_me, adj_ref, sens_ref, diag_ref, face_ref, hcl, hch, hsl, hsh, w_inc,
                 inc_ref, None, send_ref, orient_ref, weight_ref, *outs)


def last_kernel(ub_ref, lb_ref, ib_ref, wall_me, adj_ref, sens_ref, diag_ref, face_ref, hcl, hch, hsl, hsh, w_inc,
                inc_ref, tgt_ref, prod_ref, out_ref, grad_ref):
    n_var = adj_ref.shape[0]
    slots = inc_ref.shape[2] // n_var
    blk_ref = (ub_ref, lb_ref, ib_ref)
    halos = (hcl[...], hch[...], hsl[...], hsh[...]) + wall_halos(w_inc[...], wall_me, n_var)
    got = from_chunks(inc_ref[...], n_var, slots)
    new = sweep_body(blk_ref, adj_ref[...], sens_ref[...], diag_ref[...], face_ref[...], halos,
                     jnp.concatenate(got, axis=0), tgt_ref[...])
    out_ref[...] = new
    grad_ref[...] = prod_ref[...] * new[n_var - 1]


def face_shapes(shape, n_wall):
    n_var, nx, ny, nz = shape
    c = jax.ShapeDtypeStruct((n_var, 1, ny, nz), F32)
    s = jax.ShapeDtypeStruct((n_var, nx, nz), F32)
    w = jax.ShapeDtypeStruct((n_wall, 1, n_var * nx * ny), F32)
    return [c, c, s, s, w]


def exchange(faces):
    c_lo, c_hi, s_lo, s_hi, w_buf = faces
    out = []
    for axis, lo_face, hi_face in (("chord", c_lo, c_hi), ("span", s_lo, s_hi)):
        count = lax.axis_size(axis)
        forward = [(i, i + 1) for i in range(count - 1)]
        backward = [(i + 1, i) for i in range(count - 1)]
        out.append(lax.ppermute(hi_face, axis, forward))
        out.append(lax.ppermute(lo_face, axis, backward))
    out.append(lax.all_to_all(w_buf, "wall", split_axis=0, concat_axis=0, tiled=True))
    return out


def local(sensitivity, diagonal, face_coef, upper_blocks, lower_blocks, iface_blocks, production,
          send_cell, target_cell, orient, iface_weight):
    n_span = lax.axis_size("span")
    n_var = sensitivity.shape[0]
    slots = send_cell.shape[-1]
    n_rows = n_span * slots
    shape = sensitivity.shape
    n_wall = lax.axis_size("wall")
    wall_me = lax.axis_index("wall").astype(jnp.int32).reshape(1)
    blk = (upper_blocks, lower_blocks, iface_blocks, wall_me)
    send_row = send_cell.reshape(n_span, slots)
    orient_row = orient.reshape(n_span, slots)
    weight_row = iface_weight.reshape(n_span, slots)
    target_row = target_cell.reshape(n_span, slots)

    vmem = pl.BlockSpec(memory_space=pltpu.VMEM)
    smem = pl.BlockSpec(memory_space=pltpu.SMEM)
    adj_sds = jax.ShapeDtypeStruct(shape, F32)
    tgt_sds = jax.ShapeDtypeStruct((1, n_rows), jnp.int32)
    first_rows = jax.ShapeDtypeStruct((n_span, 1, (n_var + 1) * slots), F32)
    rows_sds = jax.ShapeDtypeStruct((n_span, 1, n_var * slots), F32)

    init = pl.pallas_call(
        init_kernel,
        out_shape=[adj_sds, first_rows] + face_shapes(shape, n_wall),
        in_specs=[smem] * 4 + [vmem] * 6,
        out_specs=[vmem] * 7,
    )
    adj, rows, *faces = init(*blk, sensitivity, diagonal, send_row, orient_row, weight_row, target_row)

    first = pl.pallas_call(
        first_sweep_kernel,
        out_shape=[adj_sds, rows_sds, tgt_sds] + face_shapes(shape, n_wall),
        in_specs=[smem] * 4 + [vmem] * 13,
        out_specs=[vmem] * 8,
    )
    step = pl.pallas_call(
        sweep_kernel,
        out_shape=[adj_sds, rows_sds, tgt_sds] + face_shapes(shape, n_wall),
        in_specs=[smem] * 4 + [vmem] * 14,
        out_specs=[vmem] * 8,
    )
    last = pl.pallas_call(
        last_kernel,
        out_shape=[adj_sds, jax.ShapeDtypeStruct(production.shape, F32)],
        in_specs=[smem] * 4 + [vmem] * 12,
        out_specs=[vmem] * 2,
    )
    received = None
    for sweep in range(SWEEPS):
        halos = exchange(faces)
        incoming = lax.all_to_all(rows, "span", split_axis=0, concat_axis=0, tiled=True)
        if sweep == 0:
            adj, rows, received, *faces = first(*blk, adj, sensitivity, diagonal, face_coef, *halos,
                                                incoming, send_row, orient_row, weight_row)
        elif sweep < SWEEPS - 1:
            adj, rows, received, *faces = step(*blk, adj, sensitivity, diagonal, face_coef, *halos,
                                               incoming, received, send_row, orient_row, weight_row)
        else:
            adj, gradient = last(*blk, adj, sensitivity, diagonal, face_coef, *halos, incoming,
                                 received, production)
    return (adj, gradient)


def solution(mesh):
    placed = (
        P(None, "chord", "span", "wall"),
        P(None, "chord", "span", "wall"),
        P(None, "chord", "span", "wall"),
        P(),
        P(),
        P(),
        P("chord", "span", "wall"),
        P("chord", "span", "wall", None, None),
        P("chord", "span", "wall", None, None),
        P("chord", "span", "wall", None, None),
        P("chord", "span", "wall", None, None),
    )
    return jax.shard_map(
        local,
        mesh=mesh,
        in_specs=placed,
        out_specs=(P(None, "chord", "span", "wall"), P("chord", "span", "wall")),
        check_vma=False,
    )
```

```python
import jax
import jax.numpy as jnp
from jax import lax
from jax.experimental import pallas as pl
from jax.experimental.pallas import tpu as pltpu
from jax.sharding import PartitionSpec as P

SWEEPS = 3
F32 = jnp.float32
BF16 = jnp.bfloat16


def split3(x):
    p1 = x.astype(BF16)
    p2 = (x - p1.astype(F32)).astype(BF16)
    return p1, p2


def gather_rows(adj, send_ref, orient_ref, weight_ref, blk, n_var, lanes):
    rows = adj.shape[1] * adj.shape[2]
    cell = flat_row(send_ref[...])
    n_rows = cell.shape[1]
    row_of = cell // lanes
    lane_of = cell % lanes
    lane_hot = (lax.broadcasted_iota(jnp.int32, (lanes, n_rows), 0) == lane_of).astype(BF16)
    row_hot = (lax.broadcasted_iota(jnp.int32, (rows, n_rows), 0) == row_of).astype(F32)
    flat = adj.reshape(n_var * rows, lanes)
    picked = jnp.dot(jnp.concatenate(split3(flat), axis=1),
                     jnp.concatenate([lane_hot] * 2, axis=0), preferred_element_type=F32)
    src = jnp.sum(picked.reshape(n_var, rows, n_rows) * row_hot[None], axis=1)
    orient = flat_row(orient_ref[...])
    weight = flat_row(weight_ref[...])
    out = []
    for i in range(n_var):
        first = None
        second = None
        for j in range(n_var):
            a = blk[2][0, j, i] * src[j:j + 1]
            b = blk[2][1, j, i] * src[j:j + 1]
            first = a if first is None else first + a
            second = b if second is None else second + b
        out.append(jnp.where(orient == 1, second, first) * weight)
    return out


def flat_row(x):
    return jnp.concatenate([x[t:t + 1] for t in range(x.shape[0])], axis=1)


def to_chunks(rows_ref, pieces, slots):
    n_dest = rows_ref.shape[0]
    for t in range(n_dest):
        rows_ref[t] = jnp.concatenate([p[:, t * slots:(t + 1) * slots] for p in pieces], axis=1)


def from_chunks(inc, count, slots):
    n_src = inc.shape[0]
    return [jnp.concatenate([inc[s][:, v * slots:(v + 1) * slots] for s in range(n_src)], axis=1)
            for v in range(count)]


def wall_columns(adj):
    n_var, nx, ny, nz = adj.shape
    lo, hi = [], []
    for v in range(n_var):
        t = adj[v].reshape(nx * ny, nz).T
        lo.append(t[0:1])
        hi.append(t[nz - 1:nz])
    return jnp.concatenate(lo, axis=0), jnp.concatenate(hi, axis=0)


def write_faces(adj, faces):
    c_lo, c_hi, s_lo, s_hi, w_buf, wall_me = faces
    nx, ny, nz = adj.shape[1], adj.shape[2], adj.shape[3]
    j_idx = lax.broadcasted_iota(jnp.int32, adj.shape, 2)
    c_lo[...] = adj[:, 0:1]
    c_hi[...] = adj[:, nx - 1:nx]
    s_lo[...] = jnp.sum(jnp.where(j_idx == 0, adj, 0.0), axis=2)
    s_hi[...] = jnp.sum(jnp.where(j_idx == ny - 1, adj, 0.0), axis=2)
    lo, hi = wall_columns(adj)
    me = wall_me[0]
    n_wall = w_buf.shape[0]
    lo = jnp.concatenate([lo[v:v + 1] for v in range(lo.shape[0])], axis=1)
    hi = jnp.concatenate([hi[v:v + 1] for v in range(hi.shape[0])], axis=1)
    for t in range(n_wall):
        w_buf[t] = jnp.where(me + 1 == t, hi, jnp.where(me - 1 == t, lo, 0.0))


def wall_halos(w_inc, wall_me, n_var):
    me = wall_me[0]
    n_wall, _, width = w_inc.shape
    below = None
    above = None
    for t in range(n_wall):
        b = jnp.where(me - 1 == t, w_inc[t], 0.0)
        a = jnp.where(me + 1 == t, w_inc[t], 0.0)
        below = b if below is None else below + b
        above = a if above is None else above + a
    rows = width // n_var
    unflat = lambda x: jnp.concatenate([x[:, v * rows:(v + 1) * rows] for v in range(n_var)], axis=0)
    return unflat(below), unflat(above)


def init_kernel(ub_ref, lb_ref, ib_ref, wall_me, sens_ref, diag_ref, send_ref, orient_ref, weight_ref, tgt_ref,
                adj_ref, rows_ref, c_lo, c_hi, s_lo, s_hi, w_buf):
    n_var = sens_ref.shape[0]
    lanes = sens_ref.shape[3]
    slots = send_ref.shape[1]
    blk_ref = (ub_ref, lb_ref, ib_ref)
    adj = sens_ref[...] / diag_ref[...]
    adj_ref[...] = adj
    write_faces(adj, (c_lo, c_hi, s_lo, s_hi, w_buf, wall_me))
    pieces = gather_rows(adj, send_ref, orient_ref, weight_ref, blk_ref, n_var, lanes)
    to_chunks(rows_ref, pieces + [flat_row(tgt_ref[...]).astype(F32)], slots)


def sweep_body(blk, adj, sens, diag, face, halos, incoming, cell):
    n_var, nx, ny, nz = adj.shape
    rows = nx * ny
    h_c_lo, h_c_hi, h_s_lo, h_s_hi, h_w_lo, h_w_hi = halos
    j_idx = lax.broadcasted_iota(jnp.int32, adj.shape, 2)
    k_idx = lax.broadcasted_iota(jnp.int32, adj.shape, 3)
    kk = lax.broadcasted_iota(jnp.int32, (nz, rows), 0)
    wall = []
    for v in range(n_var):
        z = jnp.where(kk == 0, h_w_lo[v:v + 1], jnp.where(kk == nz - 1, h_w_hi[v:v + 1], 0.0))
        wall.append(z.T.reshape(nx, ny, nz))
    wall = jnp.stack(wall, axis=0)
    up = [
        jnp.concatenate([adj[:, 1:], h_c_hi], axis=1),
        jnp.where(j_idx == ny - 1, h_s_hi[:, :, None, :], pltpu.roll(adj, ny - 1, 2)),
        jnp.where(k_idx == nz - 1, wall, pltpu.roll(adj, nz - 1, 3)),
    ]
    lo = [
        jnp.concatenate([h_c_lo, adj[:, :-1]], axis=1),
        jnp.where(j_idx == 0, h_s_lo[:, :, None, :], pltpu.roll(adj, 1, 2)),
        jnp.where(k_idx == 0, wall, pltpu.roll(adj, 1, 3)),
    ]
    n_rows = incoming.shape[1]
    row_of = cell // nz
    lane_of = cell % nz
    row_hot = (lax.broadcasted_iota(jnp.int32, (rows, n_rows), 0) == row_of).astype(BF16)
    lane_hot = (lax.broadcasted_iota(jnp.int32, (nz, n_rows), 0) == lane_of).astype(BF16)
    lhs = jnp.concatenate([(row_hot[None] * part[:, None, :]).reshape(n_var * rows, n_rows)
                           for part in split3(incoming)], axis=1)
    coupled = lax.dot_general(lhs, jnp.concatenate([lane_hot] * 2, axis=1), (((1,), (1,)), ((), ())),
                              preferred_element_type=F32)
    coupled = coupled.reshape(n_var, nx, ny, nz)
    new = []
    for i in range(n_var):
        applied = diag[i] * adj[i] + coupled[i]
        for d in range(3):
            acc = None
            for j in range(n_var):
                t = blk[0][d, j, i] * up[d][j] + blk[1][d, j, i] * lo[d][j]
                acc = t if acc is None else acc + t
            applied = applied + face[d] * acc
        new.append(adj[i] + (sens[i] - applied) / diag[i])
    return jnp.stack(new, axis=0)


def make_part_a(first, slots):
    def kernel(ub_ref, lb_ref, ib_ref, wall_me, adj_ref, sens_ref, diag_ref, face_ref, hcl, hch, w_inc,
               inc_ref, *rest):
        if first:
            out_ref, tgt_out = rest
        else:
            tgt_ref, out_ref = rest
        n_var, nx, ny, nz = adj_ref.shape
        blk_ref = (ub_ref, lb_ref, ib_ref)
        inc = inc_ref[...]
        if first:
            got = from_chunks(inc, n_var + 1, slots)
            cell = got[n_var].astype(jnp.int32)
            tgt_out[...] = cell
        else:
            got = from_chunks(inc, n_var, slots)
            cell = tgt_ref[...]
        none = jnp.zeros((n_var, nx, nz), F32)
        halos = (hcl[...], hch[...], none, none) + wall_halos(w_inc[...], wall_me, n_var)
        out_ref[...] = sweep_body(blk_ref, adj_ref[...], sens_ref[...], diag_ref[...], face_ref[...], halos,
                                  jnp.concatenate(got[:n_var], axis=0), cell)
    return kernel


def make_part_b(last, slots):
    def kernel(ub_ref, lb_ref, ib_ref, part_ref, diag_ref, face_ref, hsl, hsh, *rest):
        n_var, nx, ny, nz = part_ref.shape
        part = part_ref[...]
        diag = diag_ref[...]
        face_y = face_ref[1]
        h_lo = hsl[...]
        h_hi = hsh[...]
        j_idx = lax.broadcasted_iota(jnp.int32, (nx, ny, nz), 1)
        new = []
        for i in range(n_var):
            above = None
            below = None
            for j in range(n_var):
                a = ub_ref[1, j, i] * h_hi[j]
                b = lb_ref[1, j, i] * h_lo[j]
                above = a if above is None else above + a
                below = b if below is None else below + b
            edge = (jnp.where(j_idx == ny - 1, above[:, None, :], 0.0)
                    + jnp.where(j_idx == 0, below[:, None, :], 0.0))
            new.append(part[i] - face_y * edge / diag[i])
        new = jnp.stack(new, axis=0)
        if last:
            prod_ref, out_ref, grad_ref = rest
            out_ref[...] = new
            grad_ref[...] = prod_ref[...] * new[n_var - 1]
        else:
            send_ref, orient_ref, weight_ref, wall_me, out_ref, rows_ref, c_lo, c_hi, s_lo, s_hi, w_buf = rest
            out_ref[...] = new
            write_faces(new, (c_lo, c_hi, s_lo, s_hi, w_buf, wall_me))
            blk_ref = (ub_ref, lb_ref, ib_ref)
            to_chunks(rows_ref, gather_rows(new, send_ref, orient_ref, weight_ref, blk_ref, n_var, nz), slots)
    return kernel


def face_shapes(shape, n_wall):
    n_var, nx, ny, nz = shape
    c = jax.ShapeDtypeStruct((n_var, 1, ny, nz), F32)
    s = jax.ShapeDtypeStruct((n_var, nx, nz), F32)
    w = jax.ShapeDtypeStruct((n_wall, 1, n_var * nx * ny), F32)
    return [c, c, s, s, w]


def exchange(faces):
    c_lo, c_hi, s_lo, s_hi, w_buf = faces
    out = []
    for axis, lo_face, hi_face in (("chord", c_lo, c_hi), ("span", s_lo, s_hi)):
        count = lax.axis_size(axis)
        forward = [(i, i + 1) for i in range(count - 1)]
        backward = [(i + 1, i) for i in range(count - 1)]
        out.append(lax.ppermute(hi_face, axis, forward))
        out.append(lax.ppermute(lo_face, axis, backward))
    out.append(lax.all_to_all(w_buf, "wall", split_axis=0, concat_axis=0, tiled=True))
    return out


def local(sensitivity, diagonal, face_coef, upper_blocks, lower_blocks, iface_blocks, production,
          send_cell, target_cell, orient, iface_weight):
    n_span = lax.axis_size("span")
    n_var = sensitivity.shape[0]
    slots = send_cell.shape[-1]
    n_rows = n_span * slots
    shape = sensitivity.shape
    n_wall = lax.axis_size("wall")
    wall_me = lax.axis_index("wall").astype(jnp.int32).reshape(1)
    blk = (upper_blocks, lower_blocks, iface_blocks, wall_me)
    send_row = send_cell.reshape(n_span, slots)
    orient_row = orient.reshape(n_span, slots)
    weight_row = iface_weight.reshape(n_span, slots)
    target_row = target_cell.reshape(n_span, slots)

    vmem = pl.BlockSpec(memory_space=pltpu.VMEM)
    smem = pl.BlockSpec(memory_space=pltpu.SMEM)
    adj_sds = jax.ShapeDtypeStruct(shape, F32)
    tgt_sds = jax.ShapeDtypeStruct((1, n_rows), jnp.int32)
    first_rows = jax.ShapeDtypeStruct((n_span, 1, (n_var + 1) * slots), F32)
    rows_sds = jax.ShapeDtypeStruct((n_span, 1, n_var * slots), F32)

    init = pl.pallas_call(
        init_kernel,
        out_shape=[adj_sds, first_rows] + face_shapes(shape, n_wall),
        in_specs=[smem] * 4 + [vmem] * 6,
        out_specs=[vmem] * 7,
    )
    adj, rows, *faces = init(*blk, sensitivity, diagonal, send_row, orient_row, weight_row, target_row)

    part_a_first = pl.pallas_call(
        make_part_a(True, slots),
        out_shape=[adj_sds, tgt_sds],
        in_specs=[smem] * 4 + [vmem] * 8,
        out_specs=[vmem] * 2,
    )
    part_a = pl.pallas_call(
        make_part_a(False, slots),
        out_shape=adj_sds,
        in_specs=[smem] * 4 + [vmem] * 9,
        out_specs=vmem,
    )
    part_b = pl.pallas_call(
        make_part_b(False, slots),
        out_shape=[adj_sds, rows_sds] + face_shapes(shape, n_wall),
        in_specs=[smem] * 3 + [vmem] * 8 + [smem],
        out_specs=[vmem] * 7,
    )
    part_b_last = pl.pallas_call(
        make_part_b(True, slots),
        out_shape=[adj_sds, jax.ShapeDtypeStruct(production.shape, F32)],
        in_specs=[smem] * 3 + [vmem] * 6,
        out_specs=[vmem] * 2,
    )
    ub, lb, ib, _ = blk
    received = None
    for sweep in range(SWEEPS):
        hcl, hch, hsl, hsh, w_inc = exchange(faces)
        incoming = lax.all_to_all(rows, "span", split_axis=0, concat_axis=0, tiled=True)
        if sweep == 0:
            partial, received = part_a_first(*blk, adj, sensitivity, diagonal, face_coef, hcl, hch, w_inc, incoming)
        else:
            partial = part_a(*blk, adj, sensitivity, diagonal, face_coef, hcl, hch, w_inc, incoming, received)
        if sweep < SWEEPS - 1:
            adj, rows, *faces = part_b(ub, lb, ib, partial, diagonal, face_coef, hsl, hsh,
                                       send_row, orient_row, weight_row, wall_me)
        else:
            adj, gradient = part_b_last(ub, lb, ib, partial, diagonal, face_coef, hsl, hsh, production)
    return (adj, gradient)


def solution(mesh):
    placed = (
        P(None, "chord", "span", "wall"),
        P(None, "chord", "span", "wall"),
        P(None, "chord", "span", "wall"),
        P(),
        P(),
        P(),
        P("chord", "span", "wall"),
        P("chord", "span", "wall", None, None),
        P("chord", "span", "wall", None, None),
        P("chord", "span", "wall", None, None),
        P("chord", "span", "wall", None, None),
    )
    return jax.shard_map(
        local,
        mesh=mesh,
        in_specs=placed,
        out_specs=(P(None, "chord", "span", "wall"), P("chord", "span", "wall")),
        check_vma=False,
    )
```

```python
import jax
import jax.numpy as jnp
from jax import lax
from jax.experimental import pallas as pl
from jax.experimental.pallas import tpu as pltpu
from jax.sharding import PartitionSpec as P

SWEEPS = 3
F32 = jnp.float32
BF16 = jnp.bfloat16


def split3(x):
    p1 = x.astype(BF16)
    p2 = (x - p1.astype(F32)).astype(BF16)
    return p1, p2


def gather_rows(adj, send_ref, orient_ref, weight_ref, blk, n_var, lanes):
    rows = adj.shape[1] * adj.shape[2]
    cell = flat_row(send_ref[...])
    n_rows = cell.shape[1]
    row_of = cell // lanes
    lane_of = cell % lanes
    lane_hot = (lax.broadcasted_iota(jnp.int32, (lanes, n_rows), 0) == lane_of).astype(BF16)
    row_hot = (lax.broadcasted_iota(jnp.int32, (rows, n_rows), 0) == row_of).astype(F32)
    flat = adj.reshape(n_var * rows, lanes)
    picked = jnp.dot(jnp.concatenate(split3(flat), axis=1),
                     jnp.concatenate([lane_hot] * 2, axis=0), preferred_element_type=F32)
    src = jnp.sum(picked.reshape(n_var, rows, n_rows) * row_hot[None], axis=1)
    orient = flat_row(orient_ref[...])
    weight = flat_row(weight_ref[...])
    out = []
    for i in range(n_var):
        first = None
        second = None
        for j in range(n_var):
            a = blk[2][0, j, i] * src[j:j + 1]
            b = blk[2][1, j, i] * src[j:j + 1]
            first = a if first is None else first + a
            second = b if second is None else second + b
        out.append(jnp.where(orient == 1, second, first) * weight)
    return out


def flat_row(x):
    return jnp.concatenate([x[t:t + 1] for t in range(x.shape[0])], axis=1)


def own_rows(g_ref, me):
    n_src, _, _, width = g_ref.shape
    return g_ref[:, pl.ds(me, 1)].reshape(n_src, 1, width)


def to_chunks(rows_ref, pieces, slots):
    n_dest = rows_ref.shape[0]
    for t in range(n_dest):
        rows_ref[t] = jnp.concatenate([p[:, t * slots:(t + 1) * slots] for p in pieces], axis=1)


def from_chunks(inc, count, slots):
    n_src = inc.shape[0]
    return [jnp.concatenate([inc[s][:, v * slots:(v + 1) * slots] for s in range(n_src)], axis=1)
            for v in range(count)]


def wall_columns(adj):
    n_var, nx, ny, nz = adj.shape
    lo, hi = [], []
    for v in range(n_var):
        t = adj[v].reshape(nx * ny, nz).T
        lo.append(t[0:1])
        hi.append(t[nz - 1:nz])
    return jnp.concatenate(lo, axis=0), jnp.concatenate(hi, axis=0)


def write_faces(adj, faces):
    c_lo, c_hi, s_lo, s_hi, w_buf, wall_me = faces
    nx, ny, nz = adj.shape[1], adj.shape[2], adj.shape[3]
    j_idx = lax.broadcasted_iota(jnp.int32, adj.shape, 2)
    c_lo[...] = adj[:, 0:1]
    c_hi[...] = adj[:, nx - 1:nx]
    s_lo[...] = jnp.sum(jnp.where(j_idx == 0, adj, 0.0), axis=2)
    s_hi[...] = jnp.sum(jnp.where(j_idx == ny - 1, adj, 0.0), axis=2)
    lo, hi = wall_columns(adj)
    me = wall_me[0]
    n_wall = w_buf.shape[0]
    lo = jnp.concatenate([lo[v:v + 1] for v in range(lo.shape[0])], axis=1)
    hi = jnp.concatenate([hi[v:v + 1] for v in range(hi.shape[0])], axis=1)
    for t in range(n_wall):
        w_buf[t] = jnp.where(me + 1 == t, hi, jnp.where(me - 1 == t, lo, 0.0))


def wall_halos(w_inc, wall_me, n_var):
    me = wall_me[0]
    n_wall, _, width = w_inc.shape
    below = None
    above = None
    for t in range(n_wall):
        b = jnp.where(me - 1 == t, w_inc[t], 0.0)
        a = jnp.where(me + 1 == t, w_inc[t], 0.0)
        below = b if below is None else below + b
        above = a if above is None else above + a
    rows = width // n_var
    unflat = lambda x: jnp.concatenate([x[:, v * rows:(v + 1) * rows] for v in range(n_var)], axis=0)
    return unflat(below), unflat(above)


def init_kernel(ub_ref, lb_ref, ib_ref, wall_me, sens_ref, diag_ref, send_ref, orient_ref, weight_ref, tgt_ref,
                adj_ref, rows_ref, c_lo, c_hi, s_lo, s_hi, w_buf):
    n_var = sens_ref.shape[0]
    lanes = sens_ref.shape[3]
    slots = send_ref.shape[1]
    blk_ref = (ub_ref, lb_ref, ib_ref)
    adj = sens_ref[...] / diag_ref[...]
    adj_ref[...] = adj
    write_faces(adj, (c_lo, c_hi, s_lo, s_hi, w_buf, wall_me))
    pieces = gather_rows(adj, send_ref, orient_ref, weight_ref, blk_ref, n_var, lanes)
    to_chunks(rows_ref, pieces + [flat_row(tgt_ref[...]).astype(F32)], slots)


def sweep_body(blk, adj, sens, diag, face, halos, incoming, cell):
    n_var, nx, ny, nz = adj.shape
    rows = nx * ny
    h_c_lo, h_c_hi, h_s_lo, h_s_hi, h_w_lo, h_w_hi = halos
    j_idx = lax.broadcasted_iota(jnp.int32, adj.shape, 2)
    k_idx = lax.broadcasted_iota(jnp.int32, adj.shape, 3)
    kk = lax.broadcasted_iota(jnp.int32, (nz, rows), 0)
    wall = []
    for v in range(n_var):
        z = jnp.where(kk == 0, h_w_lo[v:v + 1], jnp.where(kk == nz - 1, h_w_hi[v:v + 1], 0.0))
        wall.append(z.T.reshape(nx, ny, nz))
    wall = jnp.stack(wall, axis=0)
    up = [
        jnp.concatenate([adj[:, 1:], h_c_hi], axis=1),
        jnp.where(j_idx == ny - 1, h_s_hi[:, :, None, :], pltpu.roll(adj, ny - 1, 2)),
        jnp.where(k_idx == nz - 1, wall, pltpu.roll(adj, nz - 1, 3)),
    ]
    lo = [
        jnp.concatenate([h_c_lo, adj[:, :-1]], axis=1),
        jnp.where(j_idx == 0, h_s_lo[:, :, None, :], pltpu.roll(adj, 1, 2)),
        jnp.where(k_idx == 0, wall, pltpu.roll(adj, 1, 3)),
    ]
    n_rows = incoming.shape[1]
    row_of = cell // nz
    lane_of = cell % nz
    row_hot = (lax.broadcasted_iota(jnp.int32, (rows, n_rows), 0) == row_of).astype(BF16)
    lane_hot = (lax.broadcasted_iota(jnp.int32, (nz, n_rows), 0) == lane_of).astype(BF16)
    lhs = jnp.concatenate([(row_hot[None] * part[:, None, :]).reshape(n_var * rows, n_rows)
                           for part in split3(incoming)], axis=1)
    coupled = lax.dot_general(lhs, jnp.concatenate([lane_hot] * 2, axis=1), (((1,), (1,)), ((), ())),
                              preferred_element_type=F32)
    coupled = coupled.reshape(n_var, nx, ny, nz)
    new = []
    for i in range(n_var):
        applied = diag[i] * adj[i] + coupled[i]
        for d in range(3):
            acc = None
            for j in range(n_var):
                t = blk[0][d, j, i] * up[d][j] + blk[1][d, j, i] * lo[d][j]
                acc = t if acc is None else acc + t
            applied = applied + face[d] * acc
        new.append(adj[i] + (sens[i] - applied) / diag[i])
    return jnp.stack(new, axis=0)


def make_part_a(first, slots):
    def kernel(ub_ref, lb_ref, ib_ref, wall_me, span_me, adj_ref, sens_ref, diag_ref, face_ref, hcl, hch, w_inc,
               inc_ref, *rest):
        if first:
            out_ref, tgt_out = rest
        else:
            tgt_ref, out_ref = rest
        n_var, nx, ny, nz = adj_ref.shape
        blk_ref = (ub_ref, lb_ref, ib_ref)
        inc = own_rows(inc_ref, span_me[0])
        if first:
            got = from_chunks(inc, n_var + 1, slots)
            cell = got[n_var].astype(jnp.int32)
            tgt_out[...] = cell
        else:
            got = from_chunks(inc, n_var, slots)
            cell = tgt_ref[...]
        none = jnp.zeros((n_var, nx, nz), F32)
        halos = (hcl[...], hch[...], none, none) + wall_halos(w_inc[...], wall_me, n_var)
        out_ref[...] = sweep_body(blk_ref, adj_ref[...], sens_ref[...], diag_ref[...], face_ref[...], halos,
                                  jnp.concatenate(got[:n_var], axis=0), cell)
    return kernel


def make_part_b(last, slots):
    def kernel(ub_ref, lb_ref, ib_ref, part_ref, diag_ref, face_ref, hsl, hsh, *rest):
        n_var, nx, ny, nz = part_ref.shape
        part = part_ref[...]
        diag = diag_ref[...]
        face_y = face_ref[1]
        h_lo = hsl[...]
        h_hi = hsh[...]
        j_idx = lax.broadcasted_iota(jnp.int32, (nx, ny, nz), 1)
        new = []
        for i in range(n_var):
            above = None
            below = None
            for j in range(n_var):
                a = ub_ref[1, j, i] * h_hi[j]
                b = lb_ref[1, j, i] * h_lo[j]
                above = a if above is None else above + a
                below = b if below is None else below + b
            edge = (jnp.where(j_idx == ny - 1, above[:, None, :], 0.0)
                    + jnp.where(j_idx == 0, below[:, None, :], 0.0))
            new.append(part[i] - face_y * edge / diag[i])
        new = jnp.stack(new, axis=0)
        if last:
            prod_ref, out_ref, grad_ref = rest
            out_ref[...] = new
            grad_ref[...] = prod_ref[...] * new[n_var - 1]
        else:
            send_ref, orient_ref, weight_ref, wall_me, out_ref, rows_ref, c_lo, c_hi, s_lo, s_hi, w_buf = rest
            out_ref[...] = new
            write_faces(new, (c_lo, c_hi, s_lo, s_hi, w_buf, wall_me))
            blk_ref = (ub_ref, lb_ref, ib_ref)
            to_chunks(rows_ref, gather_rows(new, send_ref, orient_ref, weight_ref, blk_ref, n_var, nz), slots)
    return kernel


def face_shapes(shape, n_wall):
    n_var, nx, ny, nz = shape
    c = jax.ShapeDtypeStruct((n_var, 1, ny, nz), F32)
    s = jax.ShapeDtypeStruct((n_var, nx, nz), F32)
    w = jax.ShapeDtypeStruct((n_wall, 1, n_var * nx * ny), F32)
    return [c, c, s, s, w]


def exchange(faces):
    c_lo, c_hi, s_lo, s_hi, w_buf = faces
    out = []
    for axis, lo_face, hi_face in (("chord", c_lo, c_hi), ("span", s_lo, s_hi)):
        count = lax.axis_size(axis)
        forward = [(i, i + 1) for i in range(count - 1)]
        backward = [(i + 1, i) for i in range(count - 1)]
        out.append(lax.ppermute(hi_face, axis, forward))
        out.append(lax.ppermute(lo_face, axis, backward))
    out.append(lax.all_to_all(w_buf, "wall", split_axis=0, concat_axis=0, tiled=True))
    return out


def local(sensitivity, diagonal, face_coef, upper_blocks, lower_blocks, iface_blocks, production,
          send_cell, target_cell, orient, iface_weight):
    n_span = lax.axis_size("span")
    n_var = sensitivity.shape[0]
    slots = send_cell.shape[-1]
    n_rows = n_span * slots
    shape = sensitivity.shape
    n_wall = lax.axis_size("wall")
    wall_me = lax.axis_index("wall").astype(jnp.int32).reshape(1)
    blk = (upper_blocks, lower_blocks, iface_blocks, wall_me)
    send_row = send_cell.reshape(n_span, slots)
    orient_row = orient.reshape(n_span, slots)
    weight_row = iface_weight.reshape(n_span, slots)
    target_row = target_cell.reshape(n_span, slots)

    vmem = pl.BlockSpec(memory_space=pltpu.VMEM)
    smem = pl.BlockSpec(memory_space=pltpu.SMEM)
    adj_sds = jax.ShapeDtypeStruct(shape, F32)
    tgt_sds = jax.ShapeDtypeStruct((1, n_rows), jnp.int32)
    first_rows = jax.ShapeDtypeStruct((n_span, 1, (n_var + 1) * slots), F32)
    rows_sds = jax.ShapeDtypeStruct((n_span, 1, n_var * slots), F32)

    init = pl.pallas_call(
        init_kernel,
        out_shape=[adj_sds, first_rows] + face_shapes(shape, n_wall),
        in_specs=[smem] * 4 + [vmem] * 6,
        out_specs=[vmem] * 7,
    )
    adj, rows, *faces = init(*blk, sensitivity, diagonal, send_row, orient_row, weight_row, target_row)

    part_a_first = pl.pallas_call(
        make_part_a(True, slots),
        out_shape=[adj_sds, tgt_sds],
        in_specs=[smem] * 5 + [vmem] * 8,
        out_specs=[vmem] * 2,
    )
    part_a = pl.pallas_call(
        make_part_a(False, slots),
        out_shape=adj_sds,
        in_specs=[smem] * 5 + [vmem] * 9,
        out_specs=vmem,
    )
    part_b = pl.pallas_call(
        make_part_b(False, slots),
        out_shape=[adj_sds, rows_sds] + face_shapes(shape, n_wall),
        in_specs=[smem] * 3 + [vmem] * 8 + [smem],
        out_specs=[vmem] * 7,
    )
    part_b_last = pl.pallas_call(
        make_part_b(True, slots),
        out_shape=[adj_sds, jax.ShapeDtypeStruct(production.shape, F32)],
        in_specs=[smem] * 3 + [vmem] * 6,
        out_specs=[vmem] * 2,
    )
    ub, lb, ib, _ = blk
    span_me = lax.axis_index("span").astype(jnp.int32).reshape(1)
    received = None
    for sweep in range(SWEEPS):
        hcl, hch, hsl, hsh, w_inc = exchange(faces)
        incoming = lax.all_gather(rows, "span", axis=0)
        if sweep == 0:
            partial, received = part_a_first(*blk, span_me, adj, sensitivity, diagonal, face_coef, hcl, hch, w_inc, incoming)
        else:
            partial = part_a(*blk, span_me, adj, sensitivity, diagonal, face_coef, hcl, hch, w_inc, incoming, received)
        if sweep < SWEEPS - 1:
            adj, rows, *faces = part_b(ub, lb, ib, partial, diagonal, face_coef, hsl, hsh,
                                       send_row, orient_row, weight_row, wall_me)
        else:
            adj, gradient = part_b_last(ub, lb, ib, partial, diagonal, face_coef, hsl, hsh, production)
    return (adj, gradient)


def solution(mesh):
    placed = (
        P(None, "chord", "span", "wall"),
        P(None, "chord", "span", "wall"),
        P(None, "chord", "span", "wall"),
        P(),
        P(),
        P(),
        P("chord", "span", "wall"),
        P("chord", "span", "wall", None, None),
        P("chord", "span", "wall", None, None),
        P("chord", "span", "wall", None, None),
        P("chord", "span", "wall", None, None),
    )
    return jax.shard_map(
        local,
        mesh=mesh,
        in_specs=placed,
        out_specs=(P(None, "chord", "span", "wall"), P("chord", "span", "wall")),
        check_vma=False,
    )
```

```python
import jax
import jax.numpy as jnp
from jax import lax
from jax.experimental import pallas as pl
from jax.experimental.pallas import tpu as pltpu
from jax.sharding import PartitionSpec as P

SWEEPS = 3
F32 = jnp.float32
BF16 = jnp.bfloat16


def split3(x):
    p1 = x.astype(BF16)
    p2 = (x - p1.astype(F32)).astype(BF16)
    return p1, p2


def gather_rows(adj, send_ref, orient_ref, weight_ref, blk, n_var, lanes):
    rows = adj.shape[1] * adj.shape[2]
    cell = flat_row(send_ref[...])
    n_rows = cell.shape[1]
    row_of = cell // lanes
    lane_of = cell % lanes
    lane_hot = (lax.broadcasted_iota(jnp.int32, (lanes, n_rows), 0) == lane_of).astype(BF16)
    row_hot = (lax.broadcasted_iota(jnp.int32, (rows, n_rows), 0) == row_of).astype(F32)
    flat = adj.reshape(n_var * rows, lanes)
    picked = jnp.dot(jnp.concatenate(split3(flat), axis=1),
                     jnp.concatenate([lane_hot] * 2, axis=0), preferred_element_type=F32)
    src = jnp.sum(picked.reshape(n_var, rows, n_rows) * row_hot[None], axis=1)
    orient = flat_row(orient_ref[...])
    weight = flat_row(weight_ref[...])
    out = []
    for i in range(n_var):
        first = None
        second = None
        for j in range(n_var):
            a = blk[2][0, j, i] * src[j:j + 1]
            b = blk[2][1, j, i] * src[j:j + 1]
            first = a if first is None else first + a
            second = b if second is None else second + b
        out.append(jnp.where(orient == 1, second, first) * weight)
    return out


def flat_row(x):
    return jnp.concatenate([x[t:t + 1] for t in range(x.shape[0])], axis=1)


def to_chunks(rows_ref, pieces, slots):
    n_dest = rows_ref.shape[0]
    for t in range(n_dest):
        rows_ref[t] = jnp.concatenate([p[:, t * slots:(t + 1) * slots] for p in pieces], axis=1)


def from_chunks(inc, count, slots):
    n_src = inc.shape[0]
    return [jnp.concatenate([inc[s][:, v * slots:(v + 1) * slots] for s in range(n_src)], axis=1)
            for v in range(count)]


def wall_columns(adj):
    n_var, nx, ny, nz = adj.shape
    lo, hi = [], []
    for v in range(n_var):
        t = adj[v].reshape(nx * ny, nz).T
        lo.append(t[0:1])
        hi.append(t[nz - 1:nz])
    return jnp.concatenate(lo, axis=0), jnp.concatenate(hi, axis=0)


def write_faces(adj, faces):
    c_lo, c_hi, s_lo, s_hi, w_buf, wall_me = faces
    nx, ny, nz = adj.shape[1], adj.shape[2], adj.shape[3]
    j_idx = lax.broadcasted_iota(jnp.int32, adj.shape, 2)
    c_lo[...] = adj[:, 0:1]
    c_hi[...] = adj[:, nx - 1:nx]
    s_lo[...] = jnp.sum(jnp.where(j_idx == 0, adj, 0.0), axis=2)
    s_hi[...] = jnp.sum(jnp.where(j_idx == ny - 1, adj, 0.0), axis=2)
    lo, hi = wall_columns(adj)
    me = wall_me[0]
    n_wall = w_buf.shape[0]
    lo = jnp.concatenate([lo[v:v + 1] for v in range(lo.shape[0])], axis=1)
    hi = jnp.concatenate([hi[v:v + 1] for v in range(hi.shape[0])], axis=1)
    for t in range(n_wall):
        w_buf[t] = jnp.where(me + 1 == t, hi, jnp.where(me - 1 == t, lo, 0.0))


def wall_halos(w_inc, wall_me, n_var):
    me = wall_me[0]
    n_wall, _, width = w_inc.shape
    below = None
    above = None
    for t in range(n_wall):
        b = jnp.where(me - 1 == t, w_inc[t], 0.0)
        a = jnp.where(me + 1 == t, w_inc[t], 0.0)
        below = b if below is None else below + b
        above = a if above is None else above + a
    rows = width // n_var
    unflat = lambda x: jnp.concatenate([x[:, v * rows:(v + 1) * rows] for v in range(n_var)], axis=0)
    return unflat(below), unflat(above)


def init_kernel(ub_ref, lb_ref, ib_ref, wall_me, sens_ref, diag_ref, send_ref, orient_ref, weight_ref, tgt_ref,
                adj_ref, rows_ref, c_lo, c_hi, s_lo, s_hi, w_buf):
    n_var = sens_ref.shape[0]
    lanes = sens_ref.shape[3]
    slots = send_ref.shape[1]
    blk_ref = (ub_ref, lb_ref, ib_ref)
    adj = sens_ref[...] / diag_ref[...]
    adj_ref[...] = adj
    write_faces(adj, (c_lo, c_hi, s_lo, s_hi, w_buf, wall_me))
    pieces = gather_rows(adj, send_ref, orient_ref, weight_ref, blk_ref, n_var, lanes)
    to_chunks(rows_ref, pieces + [flat_row(tgt_ref[...]).astype(F32)], slots)


def sweep_body(blk, adj, sens, diag, face, halos, incoming, cell):
    n_var, nx, ny, nz = adj.shape
    rows = nx * ny
    h_c_lo, h_c_hi, h_s_lo, h_s_hi, h_w_lo, h_w_hi = halos
    j_idx = lax.broadcasted_iota(jnp.int32, adj.shape, 2)
    k_idx = lax.broadcasted_iota(jnp.int32, adj.shape, 3)
    kk = lax.broadcasted_iota(jnp.int32, (nz, rows), 0)
    wall = []
    for v in range(n_var):
        z = jnp.where(kk == 0, h_w_lo[v:v + 1], jnp.where(kk == nz - 1, h_w_hi[v:v + 1], 0.0))
        wall.append(z.T.reshape(nx, ny, nz))
    wall = jnp.stack(wall, axis=0)
    up = [
        jnp.concatenate([adj[:, 1:], h_c_hi], axis=1),
        jnp.where(j_idx == ny - 1, h_s_hi[:, :, None, :], pltpu.roll(adj, ny - 1, 2)),
        jnp.where(k_idx == nz - 1, wall, pltpu.roll(adj, nz - 1, 3)),
    ]
    lo = [
        jnp.concatenate([h_c_lo, adj[:, :-1]], axis=1),
        jnp.where(j_idx == 0, h_s_lo[:, :, None, :], pltpu.roll(adj, 1, 2)),
        jnp.where(k_idx == 0, wall, pltpu.roll(adj, 1, 3)),
    ]
    n_rows = incoming.shape[1]
    row_of = cell // nz
    lane_of = cell % nz
    row_hot = (lax.broadcasted_iota(jnp.int32, (rows, n_rows), 0) == row_of).astype(BF16)
    lane_hot = (lax.broadcasted_iota(jnp.int32, (nz, n_rows), 0) == lane_of).astype(BF16)
    lhs = jnp.concatenate([(row_hot[None] * part[:, None, :]).reshape(n_var * rows, n_rows)
                           for part in split3(incoming)], axis=1)
    coupled = lax.dot_general(lhs, jnp.concatenate([lane_hot] * 2, axis=1), (((1,), (1,)), ((), ())),
                              preferred_element_type=F32)
    coupled = coupled.reshape(n_var, nx, ny, nz)
    new = []
    for i in range(n_var):
        applied = diag[i] * adj[i] + coupled[i]
        for d in range(3):
            acc = None
            for j in range(n_var):
                t = blk[0][d, j, i] * up[d][j] + blk[1][d, j, i] * lo[d][j]
                acc = t if acc is None else acc + t
            applied = applied + face[d] * acc
        new.append(adj[i] + (sens[i] - applied) / diag[i])
    return jnp.stack(new, axis=0)


def make_part_a(first, slots):
    def kernel(ub_ref, lb_ref, ib_ref, wall_me, adj_ref, sens_ref, diag_ref, face_ref, hcl, hch, w_inc,
               inc_ref, *rest):
        if first:
            out_ref, tgt_out = rest
        else:
            tgt_ref, out_ref = rest
        n_var, nx, ny, nz = adj_ref.shape
        blk_ref = (ub_ref, lb_ref, ib_ref)
        inc = inc_ref[...]
        if first:
            got = from_chunks(inc, n_var + 1, slots)
            cell = got[n_var].astype(jnp.int32)
            tgt_out[...] = cell
        else:
            got = from_chunks(inc, n_var, slots)
            cell = tgt_ref[...]
        none = jnp.zeros((n_var, nx, nz), F32)
        halos = (hcl[...], hch[...], none, none) + wall_halos(w_inc[...], wall_me, n_var)
        out_ref[...] = sweep_body(blk_ref, adj_ref[...], sens_ref[...], diag_ref[...], face_ref[...], halos,
                                  jnp.concatenate(got[:n_var], axis=0), cell)
    return kernel


def make_part_b(last, slots):
    def kernel(ub_ref, lb_ref, ib_ref, part_ref, diag_ref, face_ref, hsl, hsh, *rest):
        n_var, nx, ny, nz = part_ref.shape
        part = part_ref[...]
        diag = diag_ref[...]
        face_y = face_ref[1]
        h_lo = hsl[...]
        h_hi = hsh[...]
        j_idx = lax.broadcasted_iota(jnp.int32, (nx, ny, nz), 1)
        new = []
        for i in range(n_var):
            above = None
            below = None
            for j in range(n_var):
                a = ub_ref[1, j, i] * h_hi[j]
                b = lb_ref[1, j, i] * h_lo[j]
                above = a if above is None else above + a
                below = b if below is None else below + b
            edge = (jnp.where(j_idx == ny - 1, above[:, None, :], 0.0)
                    + jnp.where(j_idx == 0, below[:, None, :], 0.0))
            new.append(part[i] - face_y * edge / diag[i])
        new = jnp.stack(new, axis=0)
        if last:
            prod_ref, out_ref, grad_ref = rest
            out_ref[...] = new
            grad_ref[...] = prod_ref[...] * new[n_var - 1]
        else:
            wall_me, out_ref, c_lo, c_hi, s_lo, s_hi, w_buf = rest
            out_ref[...] = new
            write_faces(new, (c_lo, c_hi, s_lo, s_hi, w_buf, wall_me))
    return kernel


def make_rows(slots):
    def kernel(ub_ref, lb_ref, ib_ref, adj_ref, send_ref, orient_ref, weight_ref, rows_ref):
        n_var, nx, ny, nz = adj_ref.shape
        blk_ref = (ub_ref, lb_ref, ib_ref)
        to_chunks(rows_ref, gather_rows(adj_ref[...], send_ref, orient_ref, weight_ref, blk_ref, n_var, nz), slots)
    return kernel


def face_shapes(shape, n_wall):
    n_var, nx, ny, nz = shape
    c = jax.ShapeDtypeStruct((n_var, 1, ny, nz), F32)
    s = jax.ShapeDtypeStruct((n_var, nx, nz), F32)
    w = jax.ShapeDtypeStruct((n_wall, 1, n_var * nx * ny), F32)
    return [c, c, s, s, w]


def exchange(faces):
    c_lo, c_hi, s_lo, s_hi, w_buf = faces
    out = []
    for axis, lo_face, hi_face in (("chord", c_lo, c_hi), ("span", s_lo, s_hi)):
        count = lax.axis_size(axis)
        forward = [(i, i + 1) for i in range(count - 1)]
        backward = [(i + 1, i) for i in range(count - 1)]
        out.append(lax.ppermute(hi_face, axis, forward))
        out.append(lax.ppermute(lo_face, axis, backward))
    out.append(lax.all_to_all(w_buf, "wall", split_axis=0, concat_axis=0, tiled=True))
    return out


def local(sensitivity, diagonal, face_coef, upper_blocks, lower_blocks, iface_blocks, production,
          send_cell, target_cell, orient, iface_weight):
    n_span = lax.axis_size("span")
    n_var = sensitivity.shape[0]
    slots = send_cell.shape[-1]
    n_rows = n_span * slots
    shape = sensitivity.shape
    n_wall = lax.axis_size("wall")
    wall_me = lax.axis_index("wall").astype(jnp.int32).reshape(1)
    blk = (upper_blocks, lower_blocks, iface_blocks, wall_me)
    send_row = send_cell.reshape(n_span, slots)
    orient_row = orient.reshape(n_span, slots)
    weight_row = iface_weight.reshape(n_span, slots)
    target_row = target_cell.reshape(n_span, slots)

    vmem = pl.BlockSpec(memory_space=pltpu.VMEM)
    smem = pl.BlockSpec(memory_space=pltpu.SMEM)
    adj_sds = jax.ShapeDtypeStruct(shape, F32)
    tgt_sds = jax.ShapeDtypeStruct((1, n_rows), jnp.int32)
    first_rows = jax.ShapeDtypeStruct((n_span, 1, (n_var + 1) * slots), F32)
    rows_sds = jax.ShapeDtypeStruct((n_span, 1, n_var * slots), F32)

    init = pl.pallas_call(
        init_kernel,
        out_shape=[adj_sds, first_rows] + face_shapes(shape, n_wall),
        in_specs=[smem] * 4 + [vmem] * 6,
        out_specs=[vmem] * 7,
    )
    adj, rows, *faces = init(*blk, sensitivity, diagonal, send_row, orient_row, weight_row, target_row)

    part_a_first = pl.pallas_call(
        make_part_a(True, slots),
        out_shape=[adj_sds, tgt_sds],
        in_specs=[smem] * 4 + [vmem] * 8,
        out_specs=[vmem] * 2,
    )
    part_a = pl.pallas_call(
        make_part_a(False, slots),
        out_shape=adj_sds,
        in_specs=[smem] * 4 + [vmem] * 9,
        out_specs=vmem,
    )
    part_b = pl.pallas_call(
        make_part_b(False, slots),
        out_shape=[adj_sds] + face_shapes(shape, n_wall),
        in_specs=[smem] * 3 + [vmem] * 5 + [smem],
        out_specs=[vmem] * 6,
    )
    next_rows = pl.pallas_call(
        make_rows(slots),
        out_shape=rows_sds,
        in_specs=[smem] * 3 + [vmem] * 4,
        out_specs=vmem,
    )
    part_b_last = pl.pallas_call(
        make_part_b(True, slots),
        out_shape=[adj_sds, jax.ShapeDtypeStruct(production.shape, F32)],
        in_specs=[smem] * 3 + [vmem] * 6,
        out_specs=[vmem] * 2,
    )
    ub, lb, ib, _ = blk
    received = None
    for sweep in range(SWEEPS):
        hcl, hch, hsl, hsh, w_inc = exchange(faces)
        incoming = lax.all_to_all(rows, "span", split_axis=0, concat_axis=0, tiled=True)
        if sweep == 0:
            partial, received = part_a_first(*blk, adj, sensitivity, diagonal, face_coef, hcl, hch, w_inc, incoming)
        else:
            partial = part_a(*blk, adj, sensitivity, diagonal, face_coef, hcl, hch, w_inc, incoming, received)
        if sweep < SWEEPS - 1:
            adj, *faces = part_b(ub, lb, ib, partial, diagonal, face_coef, hsl, hsh, wall_me)
            rows = next_rows(ub, lb, ib, adj, send_row, orient_row, weight_row)
        else:
            adj, gradient = part_b_last(ub, lb, ib, partial, diagonal, face_coef, hsl, hsh, production)
    return (adj, gradient)


def solution(mesh):
    placed = (
        P(None, "chord", "span", "wall"),
        P(None, "chord", "span", "wall"),
        P(None, "chord", "span", "wall"),
        P(),
        P(),
        P(),
        P("chord", "span", "wall"),
        P("chord", "span", "wall", None, None),
        P("chord", "span", "wall", None, None),
        P("chord", "span", "wall", None, None),
        P("chord", "span", "wall", None, None),
    )
    return jax.shard_map(
        local,
        mesh=mesh,
        in_specs=placed,
        out_specs=(P(None, "chord", "span", "wall"), P("chord", "span", "wall")),
        check_vma=False,
    )
```

```python
import jax
import jax.numpy as jnp
from jax import lax
from jax.experimental import pallas as pl
from jax.experimental.pallas import tpu as pltpu
from jax.sharding import PartitionSpec as P

SWEEPS = 3
F32 = jnp.float32
BF16 = jnp.bfloat16


def split3(x):
    p1 = x.astype(BF16)
    p2 = (x - p1.astype(F32)).astype(BF16)
    return p1, p2


def gather_rows(adj, send_ref, orient_ref, weight_ref, blk, n_var, lanes):
    rows = adj.shape[1] * adj.shape[2]
    cell = flat_row(send_ref[...])
    n_rows = cell.shape[1]
    row_of = cell // lanes
    lane_of = cell % lanes
    lane_hot = (lax.broadcasted_iota(jnp.int32, (lanes, n_rows), 0) == lane_of).astype(BF16)
    row_hot = (lax.broadcasted_iota(jnp.int32, (rows, n_rows), 0) == row_of).astype(F32)
    flat = adj.reshape(n_var * rows, lanes)
    picked = jnp.dot(jnp.concatenate(split3(flat), axis=1),
                     jnp.concatenate([lane_hot] * 2, axis=0), preferred_element_type=F32)
    src = jnp.sum(picked.reshape(n_var, rows, n_rows) * row_hot[None], axis=1)
    orient = flat_row(orient_ref[...])
    weight = flat_row(weight_ref[...])
    out = []
    for i in range(n_var):
        first = None
        second = None
        for j in range(n_var):
            a = blk[2][0, j, i] * src[j:j + 1]
            b = blk[2][1, j, i] * src[j:j + 1]
            first = a if first is None else first + a
            second = b if second is None else second + b
        out.append(jnp.where(orient == 1, second, first) * weight)
    return out


def flat_row(x):
    return jnp.concatenate([x[t:t + 1] for t in range(x.shape[0])], axis=1)


def to_chunks(rows_ref, pieces, slots):
    n_dest = rows_ref.shape[0]
    for t in range(n_dest):
        rows_ref[t] = jnp.concatenate([p[:, t * slots:(t + 1) * slots] for p in pieces], axis=1)


def from_chunks(inc, count, slots):
    n_src = inc.shape[0]
    return [jnp.concatenate([inc[s][:, v * slots:(v + 1) * slots] for s in range(n_src)], axis=1)
            for v in range(count)]


def wall_columns(adj):
    n_var, nx, ny, nz = adj.shape
    lo, hi = [], []
    for v in range(n_var):
        t = adj[v].reshape(nx * ny, nz).T
        lo.append(t[0:1])
        hi.append(t[nz - 1:nz])
    return jnp.concatenate(lo, axis=0), jnp.concatenate(hi, axis=0)


def write_faces(adj, faces):
    c_buf, chord_me, s_lo, s_hi, w_buf, wall_me = faces
    nx, ny, nz = adj.shape[1], adj.shape[2], adj.shape[3]
    j_idx = lax.broadcasted_iota(jnp.int32, adj.shape, 2)
    cm = chord_me[0]
    c_lo = adj[:, 0]
    c_hi = adj[:, nx - 1]
    for t in range(c_buf.shape[0]):
        c_buf[t] = jnp.where(cm + 1 == t, c_hi, jnp.where(cm - 1 == t, c_lo, 0.0))
    s_lo[...] = jnp.sum(jnp.where(j_idx == 0, adj, 0.0), axis=2)
    s_hi[...] = jnp.sum(jnp.where(j_idx == ny - 1, adj, 0.0), axis=2)
    lo, hi = wall_columns(adj)
    me = wall_me[0]
    n_wall = w_buf.shape[0]
    lo = jnp.concatenate([lo[v:v + 1] for v in range(lo.shape[0])], axis=1)
    hi = jnp.concatenate([hi[v:v + 1] for v in range(hi.shape[0])], axis=1)
    for t in range(n_wall):
        w_buf[t] = jnp.where(me + 1 == t, hi, jnp.where(me - 1 == t, lo, 0.0))


def chord_halos(c_inc, chord_me):
    me = chord_me[0]
    below = None
    above = None
    for t in range(c_inc.shape[0]):
        b = jnp.where(me - 1 == t, c_inc[t], 0.0)
        a = jnp.where(me + 1 == t, c_inc[t], 0.0)
        below = b if below is None else below + b
        above = a if above is None else above + a
    return below[:, None], above[:, None]


def wall_halos(w_inc, wall_me, n_var):
    me = wall_me[0]
    n_wall, _, width = w_inc.shape
    below = None
    above = None
    for t in range(n_wall):
        b = jnp.where(me - 1 == t, w_inc[t], 0.0)
        a = jnp.where(me + 1 == t, w_inc[t], 0.0)
        below = b if below is None else below + b
        above = a if above is None else above + a
    rows = width // n_var
    unflat = lambda x: jnp.concatenate([x[:, v * rows:(v + 1) * rows] for v in range(n_var)], axis=0)
    return unflat(below), unflat(above)


def init_kernel(ub_ref, lb_ref, ib_ref, wall_me, chord_me, sens_ref, diag_ref, send_ref, orient_ref, weight_ref,
                tgt_ref, adj_ref, rows_ref, c_buf, s_lo, s_hi, w_buf):
    n_var = sens_ref.shape[0]
    lanes = sens_ref.shape[3]
    slots = send_ref.shape[1]
    blk_ref = (ub_ref, lb_ref, ib_ref)
    adj = sens_ref[...] / diag_ref[...]
    adj_ref[...] = adj
    write_faces(adj, (c_buf, chord_me, s_lo, s_hi, w_buf, wall_me))
    pieces = gather_rows(adj, send_ref, orient_ref, weight_ref, blk_ref, n_var, lanes)
    to_chunks(rows_ref, pieces + [flat_row(tgt_ref[...]).astype(F32)], slots)


def sweep_body(blk, adj, sens, diag, face, halos, incoming, cell):
    n_var, nx, ny, nz = adj.shape
    rows = nx * ny
    h_c_lo, h_c_hi, h_s_lo, h_s_hi, h_w_lo, h_w_hi = halos
    j_idx = lax.broadcasted_iota(jnp.int32, adj.shape, 2)
    k_idx = lax.broadcasted_iota(jnp.int32, adj.shape, 3)
    kk = lax.broadcasted_iota(jnp.int32, (nz, rows), 0)
    wall = []
    for v in range(n_var):
        z = jnp.where(kk == 0, h_w_lo[v:v + 1], jnp.where(kk == nz - 1, h_w_hi[v:v + 1], 0.0))
        wall.append(z.T.reshape(nx, ny, nz))
    wall = jnp.stack(wall, axis=0)
    up = [
        jnp.concatenate([adj[:, 1:], h_c_hi], axis=1),
        jnp.where(j_idx == ny - 1, h_s_hi[:, :, None, :], pltpu.roll(adj, ny - 1, 2)),
        jnp.where(k_idx == nz - 1, wall, pltpu.roll(adj, nz - 1, 3)),
    ]
    lo = [
        jnp.concatenate([h_c_lo, adj[:, :-1]], axis=1),
        jnp.where(j_idx == 0, h_s_lo[:, :, None, :], pltpu.roll(adj, 1, 2)),
        jnp.where(k_idx == 0, wall, pltpu.roll(adj, 1, 3)),
    ]
    n_rows = incoming.shape[1]
    row_of = cell // nz
    lane_of = cell % nz
    row_hot = (lax.broadcasted_iota(jnp.int32, (rows, n_rows), 0) == row_of).astype(BF16)
    lane_hot = (lax.broadcasted_iota(jnp.int32, (nz, n_rows), 0) == lane_of).astype(BF16)
    lhs = jnp.concatenate([(row_hot[None] * part[:, None, :]).reshape(n_var * rows, n_rows)
                           for part in split3(incoming)], axis=1)
    coupled = lax.dot_general(lhs, jnp.concatenate([lane_hot] * 2, axis=1), (((1,), (1,)), ((), ())),
                              preferred_element_type=F32)
    coupled = coupled.reshape(n_var, nx, ny, nz)
    new = []
    for i in range(n_var):
        applied = diag[i] * adj[i] + coupled[i]
        for d in range(3):
            acc = None
            for j in range(n_var):
                t = blk[0][d, j, i] * up[d][j] + blk[1][d, j, i] * lo[d][j]
                acc = t if acc is None else acc + t
            applied = applied + face[d] * acc
        new.append(adj[i] + (sens[i] - applied) / diag[i])
    return jnp.stack(new, axis=0)


def make_part_a(first, slots):
    def kernel(ub_ref, lb_ref, ib_ref, wall_me, chord_me, adj_ref, sens_ref, diag_ref, face_ref, c_inc, w_inc,
               inc_ref, *rest):
        if first:
            out_ref, tgt_out = rest
        else:
            tgt_ref, out_ref = rest
        n_var, nx, ny, nz = adj_ref.shape
        blk_ref = (ub_ref, lb_ref, ib_ref)
        inc = inc_ref[...]
        if first:
            got = from_chunks(inc, n_var + 1, slots)
            cell = got[n_var].astype(jnp.int32)
            tgt_out[...] = cell
        else:
            got = from_chunks(inc, n_var, slots)
            cell = tgt_ref[...]
        none = jnp.zeros((n_var, nx, nz), F32)
        halos = chord_halos(c_inc[...], chord_me) + (none, none) + wall_halos(w_inc[...], wall_me, n_var)
        out_ref[...] = sweep_body(blk_ref, adj_ref[...], sens_ref[...], diag_ref[...], face_ref[...], halos,
                                  jnp.concatenate(got[:n_var], axis=0), cell)
    return kernel


def make_part_b(last, slots):
    def kernel(ub_ref, lb_ref, ib_ref, part_ref, diag_ref, face_ref, hsl, hsh, *rest):
        n_var, nx, ny, nz = part_ref.shape
        part = part_ref[...]
        diag = diag_ref[...]
        face_y = face_ref[1]
        h_lo = hsl[...]
        h_hi = hsh[...]
        j_idx = lax.broadcasted_iota(jnp.int32, (nx, ny, nz), 1)
        new = []
        for i in range(n_var):
            above = None
            below = None
            for j in range(n_var):
                a = ub_ref[1, j, i] * h_hi[j]
                b = lb_ref[1, j, i] * h_lo[j]
                above = a if above is None else above + a
                below = b if below is None else below + b
            edge = (jnp.where(j_idx == ny - 1, above[:, None, :], 0.0)
                    + jnp.where(j_idx == 0, below[:, None, :], 0.0))
            new.append(part[i] - face_y * edge / diag[i])
        new = jnp.stack(new, axis=0)
        if last:
            prod_ref, out_ref, grad_ref = rest
            out_ref[...] = new
            grad_ref[...] = prod_ref[...] * new[n_var - 1]
        else:
            send_ref, orient_ref, weight_ref, wall_me, chord_me, out_ref, rows_ref, c_buf, s_lo, s_hi, w_buf = rest
            out_ref[...] = new
            write_faces(new, (c_buf, chord_me, s_lo, s_hi, w_buf, wall_me))
            blk_ref = (ub_ref, lb_ref, ib_ref)
            to_chunks(rows_ref, gather_rows(new, send_ref, orient_ref, weight_ref, blk_ref, n_var, nz), slots)
    return kernel


def face_shapes(shape, n_wall, n_chord):
    n_var, nx, ny, nz = shape
    c = jax.ShapeDtypeStruct((n_chord, n_var, ny, nz), F32)
    s = jax.ShapeDtypeStruct((n_var, nx, nz), F32)
    w = jax.ShapeDtypeStruct((n_wall, 1, n_var * nx * ny), F32)
    return [c, s, s, w]


def exchange(faces):
    c_buf, s_lo, s_hi, w_buf = faces
    out = [lax.all_to_all(c_buf, "chord", split_axis=0, concat_axis=0, tiled=True)]
    for axis, lo_face, hi_face in (("span", s_lo, s_hi),):
        count = lax.axis_size(axis)
        forward = [(i, i + 1) for i in range(count - 1)]
        backward = [(i + 1, i) for i in range(count - 1)]
        out.append(lax.ppermute(hi_face, axis, forward))
        out.append(lax.ppermute(lo_face, axis, backward))
    out.append(lax.all_to_all(w_buf, "wall", split_axis=0, concat_axis=0, tiled=True))
    return out


def local(sensitivity, diagonal, face_coef, upper_blocks, lower_blocks, iface_blocks, production,
          send_cell, target_cell, orient, iface_weight):
    n_span = lax.axis_size("span")
    n_var = sensitivity.shape[0]
    slots = send_cell.shape[-1]
    n_rows = n_span * slots
    shape = sensitivity.shape
    n_wall = lax.axis_size("wall")
    n_chord = lax.axis_size("chord")
    wall_me = lax.axis_index("wall").astype(jnp.int32).reshape(1)
    chord_me = lax.axis_index("chord").astype(jnp.int32).reshape(1)
    blk = (upper_blocks, lower_blocks, iface_blocks, wall_me, chord_me)
    send_row = send_cell.reshape(n_span, slots)
    orient_row = orient.reshape(n_span, slots)
    weight_row = iface_weight.reshape(n_span, slots)
    target_row = target_cell.reshape(n_span, slots)

    vmem = pl.BlockSpec(memory_space=pltpu.VMEM)
    smem = pl.BlockSpec(memory_space=pltpu.SMEM)
    adj_sds = jax.ShapeDtypeStruct(shape, F32)
    tgt_sds = jax.ShapeDtypeStruct((1, n_rows), jnp.int32)
    first_rows = jax.ShapeDtypeStruct((n_span, 1, (n_var + 1) * slots), F32)
    rows_sds = jax.ShapeDtypeStruct((n_span, 1, n_var * slots), F32)

    init = pl.pallas_call(
        init_kernel,
        out_shape=[adj_sds, first_rows] + face_shapes(shape, n_wall, n_chord),
        in_specs=[smem] * 5 + [vmem] * 6,
        out_specs=[vmem] * 6,
    )
    adj, rows, *faces = init(*blk, sensitivity, diagonal, send_row, orient_row, weight_row, target_row)

    part_a_first = pl.pallas_call(
        make_part_a(True, slots),
        out_shape=[adj_sds, tgt_sds],
        in_specs=[smem] * 5 + [vmem] * 7,
        out_specs=[vmem] * 2,
    )
    part_a = pl.pallas_call(
        make_part_a(False, slots),
        out_shape=adj_sds,
        in_specs=[smem] * 5 + [vmem] * 8,
        out_specs=vmem,
    )
    part_b = pl.pallas_call(
        make_part_b(False, slots),
        out_shape=[adj_sds, rows_sds] + face_shapes(shape, n_wall, n_chord),
        in_specs=[smem] * 3 + [vmem] * 8 + [smem] * 2,
        out_specs=[vmem] * 6,
    )
    part_b_last = pl.pallas_call(
        make_part_b(True, slots),
        out_shape=[adj_sds, jax.ShapeDtypeStruct(production.shape, F32)],
        in_specs=[smem] * 3 + [vmem] * 6,
        out_specs=[vmem] * 2,
    )
    ub, lb, ib, _, _ = blk
    received = None
    for sweep in range(SWEEPS):
        c_inc, hsl, hsh, w_inc = exchange(faces)
        incoming = lax.all_to_all(rows, "span", split_axis=0, concat_axis=0, tiled=True)
        if sweep == 0:
            partial, received = part_a_first(*blk, adj, sensitivity, diagonal, face_coef, c_inc, w_inc, incoming)
        else:
            partial = part_a(*blk, adj, sensitivity, diagonal, face_coef, c_inc, w_inc, incoming, received)
        if sweep < SWEEPS - 1:
            adj, rows, *faces = part_b(ub, lb, ib, partial, diagonal, face_coef, hsl, hsh,
                                       send_row, orient_row, weight_row, wall_me, chord_me)
        else:
            adj, gradient = part_b_last(ub, lb, ib, partial, diagonal, face_coef, hsl, hsh, production)
    return (adj, gradient)


def solution(mesh):
    placed = (
        P(None, "chord", "span", "wall"),
        P(None, "chord", "span", "wall"),
        P(None, "chord", "span", "wall"),
        P(),
        P(),
        P(),
        P("chord", "span", "wall"),
        P("chord", "span", "wall", None, None),
        P("chord", "span", "wall", None, None),
        P("chord", "span", "wall", None, None),
        P("chord", "span", "wall", None, None),
    )
    return jax.shard_map(
        local,
        mesh=mesh,
        in_specs=placed,
        out_specs=(P(None, "chord", "span", "wall"), P("chord", "span", "wall")),
        check_vma=False,
    )
```

```python
import jax
import jax.numpy as jnp
from jax import lax
from jax.experimental import pallas as pl
from jax.experimental.pallas import tpu as pltpu
from jax.sharding import PartitionSpec as P

SWEEPS = 3
F32 = jnp.float32
BF16 = jnp.bfloat16


def split3(x):
    p1 = x.astype(BF16)
    p2 = (x - p1.astype(F32)).astype(BF16)
    return p1, p2


def gather_rows(adj, send_ref, orient_ref, weight_ref, blk, n_var, lanes):
    rows = adj.shape[1] * adj.shape[2]
    cell = flat_row(send_ref[...])
    n_rows = cell.shape[1]
    row_of = cell // lanes
    lane_of = cell % lanes
    lane_hot = (lax.broadcasted_iota(jnp.int32, (lanes, n_rows), 0) == lane_of).astype(BF16)
    row_hot = (lax.broadcasted_iota(jnp.int32, (rows, n_rows), 0) == row_of).astype(F32)
    flat = adj.reshape(n_var * rows, lanes)
    picked = jnp.dot(jnp.concatenate(split3(flat), axis=1),
                     jnp.concatenate([lane_hot] * 2, axis=0), preferred_element_type=F32)
    src = jnp.sum(picked.reshape(n_var, rows, n_rows) * row_hot[None], axis=1)
    orient = flat_row(orient_ref[...])
    weight = flat_row(weight_ref[...])
    out = []
    for i in range(n_var):
        first = None
        second = None
        for j in range(n_var):
            a = blk[2][0, j, i] * src[j:j + 1]
            b = blk[2][1, j, i] * src[j:j + 1]
            first = a if first is None else first + a
            second = b if second is None else second + b
        out.append(jnp.where(orient == 1, second, first) * weight)
    return out


def flat_row(x):
    return jnp.concatenate([x[t:t + 1] for t in range(x.shape[0])], axis=1)


def to_chunks(rows_ref, pieces, slots):
    n_dest = rows_ref.shape[0]
    for t in range(n_dest):
        rows_ref[t] = jnp.concatenate([p[:, t * slots:(t + 1) * slots] for p in pieces], axis=1)


def from_chunks(inc, count, slots):
    n_src = inc.shape[0]
    return [jnp.concatenate([inc[s][:, v * slots:(v + 1) * slots] for s in range(n_src)], axis=1)
            for v in range(count)]


def wall_columns(adj):
    n_var, nx, ny, nz = adj.shape
    lo, hi = [], []
    for v in range(n_var):
        t = adj[v].reshape(nx * ny, nz).T
        lo.append(t[0:1])
        hi.append(t[nz - 1:nz])
    return jnp.concatenate(lo, axis=0), jnp.concatenate(hi, axis=0)


def write_faces(adj, faces):
    c_lo, c_hi, s_lo, s_hi, w_buf, wall_me = faces
    nx, ny, nz = adj.shape[1], adj.shape[2], adj.shape[3]
    j_idx = lax.broadcasted_iota(jnp.int32, adj.shape, 2)
    c_lo[...] = adj[:, 0:1]
    c_hi[...] = adj[:, nx - 1:nx]
    s_lo[...] = jnp.sum(jnp.where(j_idx == 0, adj, 0.0), axis=2)
    s_hi[...] = jnp.sum(jnp.where(j_idx == ny - 1, adj, 0.0), axis=2)
    lo, hi = wall_columns(adj)
    me = wall_me[0]
    n_wall = w_buf.shape[0]
    lo = jnp.concatenate([lo[v:v + 1] for v in range(lo.shape[0])], axis=1)
    hi = jnp.concatenate([hi[v:v + 1] for v in range(hi.shape[0])], axis=1)
    for t in range(n_wall):
        w_buf[t] = jnp.where(me + 1 == t, hi, jnp.where(me - 1 == t, lo, 0.0))


def wall_halos(w_inc, wall_me, n_var):
    me = wall_me[0]
    n_wall, _, width = w_inc.shape
    below = None
    above = None
    for t in range(n_wall):
        b = jnp.where(me - 1 == t, w_inc[t], 0.0)
        a = jnp.where(me + 1 == t, w_inc[t], 0.0)
        below = b if below is None else below + b
        above = a if above is None else above + a
    rows = width // n_var
    unflat = lambda x: jnp.concatenate([x[:, v * rows:(v + 1) * rows] for v in range(n_var)], axis=0)
    return unflat(below), unflat(above)


def init_kernel(ub_ref, lb_ref, ib_ref, wall_me, sens_ref, diag_ref, send_ref, orient_ref, weight_ref, tgt_ref,
                adj_ref, rows_ref, c_lo, c_hi, s_lo, s_hi, w_buf):
    n_var = sens_ref.shape[0]
    lanes = sens_ref.shape[3]
    slots = send_ref.shape[1]
    blk_ref = (ub_ref, lb_ref, ib_ref)
    adj = sens_ref[...] / diag_ref[...]
    adj_ref[...] = adj
    write_faces(adj, (c_lo, c_hi, s_lo, s_hi, w_buf, wall_me))
    pieces = gather_rows(adj, send_ref, orient_ref, weight_ref, blk_ref, n_var, lanes)
    to_chunks(rows_ref, pieces + [flat_row(tgt_ref[...]).astype(F32)], slots)


def scatter_rows(incoming, cell, shape):
    n_var, nx, ny, nz = shape
    rows = nx * ny
    n_rows = incoming.shape[1]
    row_of = cell // nz
    lane_of = cell % nz
    row_hot = (lax.broadcasted_iota(jnp.int32, (rows, n_rows), 0) == row_of).astype(BF16)
    lane_hot = (lax.broadcasted_iota(jnp.int32, (nz, n_rows), 0) == lane_of).astype(BF16)
    lhs = jnp.concatenate([(row_hot[None] * part[:, None, :]).reshape(n_var * rows, n_rows)
                           for part in split3(incoming)], axis=1)
    coupled = lax.dot_general(lhs, jnp.concatenate([lane_hot] * 2, axis=1), (((1,), (1,)), ((), ())),
                              preferred_element_type=F32)
    return coupled.reshape(n_var, nx, ny, nz)


def sweep_body(blk, adj, sens, diag, face, halos):
    n_var, nx, ny, nz = adj.shape
    rows = nx * ny
    h_c_lo, h_c_hi, h_s_lo, h_s_hi, h_w_lo, h_w_hi = halos
    j_idx = lax.broadcasted_iota(jnp.int32, adj.shape, 2)
    k_idx = lax.broadcasted_iota(jnp.int32, adj.shape, 3)
    kk = lax.broadcasted_iota(jnp.int32, (nz, rows), 0)
    wall = []
    for v in range(n_var):
        z = jnp.where(kk == 0, h_w_lo[v:v + 1], jnp.where(kk == nz - 1, h_w_hi[v:v + 1], 0.0))
        wall.append(z.T.reshape(nx, ny, nz))
    wall = jnp.stack(wall, axis=0)
    up = [
        jnp.concatenate([adj[:, 1:], h_c_hi], axis=1),
        jnp.where(j_idx == ny - 1, h_s_hi[:, :, None, :], pltpu.roll(adj, ny - 1, 2)),
        jnp.where(k_idx == nz - 1, wall, pltpu.roll(adj, nz - 1, 3)),
    ]
    lo = [
        jnp.concatenate([h_c_lo, adj[:, :-1]], axis=1),
        jnp.where(j_idx == 0, h_s_lo[:, :, None, :], pltpu.roll(adj, 1, 2)),
        jnp.where(k_idx == 0, wall, pltpu.roll(adj, 1, 3)),
    ]
    new = []
    for i in range(n_var):
        applied = diag[i] * adj[i]
        for d in range(3):
            acc = None
            for j in range(n_var):
                t = blk[0][d, j, i] * up[d][j] + blk[1][d, j, i] * lo[d][j]
                acc = t if acc is None else acc + t
            applied = applied + face[d] * acc
        new.append(adj[i] + (sens[i] - applied) / diag[i])
    return jnp.stack(new, axis=0)


def make_part_a(slots):
    def kernel(ub_ref, lb_ref, ib_ref, wall_me, adj_ref, sens_ref, diag_ref, face_ref, hcl, hch, w_inc, out_ref):
        n_var, nx, ny, nz = adj_ref.shape
        blk_ref = (ub_ref, lb_ref, ib_ref)
        none = jnp.zeros((n_var, nx, nz), F32)
        halos = (hcl[...], hch[...], none, none) + wall_halos(w_inc[...], wall_me, n_var)
        out_ref[...] = sweep_body(blk_ref, adj_ref[...], sens_ref[...], diag_ref[...], face_ref[...], halos)
    return kernel


def make_part_b(first, last, slots):
    def kernel(ub_ref, lb_ref, ib_ref, part_ref, diag_ref, face_ref, hsl, hsh, inc_ref, *rest):
        n_var, nx, ny, nz = part_ref.shape
        inc = inc_ref[...]
        if first:
            tgt_out, rest = rest[-1], rest[:-1]
            got = from_chunks(inc, n_var + 1, slots)
            cell = got[n_var].astype(jnp.int32)
            tgt_out[...] = cell
        else:
            tgt_ref, rest = rest[0], rest[1:]
            got = from_chunks(inc, n_var, slots)
            cell = tgt_ref[...]
        coupled = scatter_rows(jnp.concatenate(got[:n_var], axis=0), cell, part_ref.shape)
        part = part_ref[...]
        diag = diag_ref[...]
        face_y = face_ref[1]
        h_lo = hsl[...]
        h_hi = hsh[...]
        j_idx = lax.broadcasted_iota(jnp.int32, (nx, ny, nz), 1)
        new = []
        for i in range(n_var):
            above = None
            below = None
            for j in range(n_var):
                a = ub_ref[1, j, i] * h_hi[j]
                b = lb_ref[1, j, i] * h_lo[j]
                above = a if above is None else above + a
                below = b if below is None else below + b
            edge = (jnp.where(j_idx == ny - 1, above[:, None, :], 0.0)
                    + jnp.where(j_idx == 0, below[:, None, :], 0.0))
            new.append(part[i] - (face_y * edge + coupled[i]) / diag[i])
        new = jnp.stack(new, axis=0)
        if last:
            prod_ref, out_ref, grad_ref = rest
            out_ref[...] = new
            grad_ref[...] = prod_ref[...] * new[n_var - 1]
        else:
            send_ref, orient_ref, weight_ref, wall_me, out_ref, rows_ref, c_lo, c_hi, s_lo, s_hi, w_buf = rest
            out_ref[...] = new
            write_faces(new, (c_lo, c_hi, s_lo, s_hi, w_buf, wall_me))
            blk_ref = (ub_ref, lb_ref, ib_ref)
            to_chunks(rows_ref, gather_rows(new, send_ref, orient_ref, weight_ref, blk_ref, n_var, nz), slots)
    return kernel


def face_shapes(shape, n_wall):
    n_var, nx, ny, nz = shape
    c = jax.ShapeDtypeStruct((n_var, 1, ny, nz), F32)
    s = jax.ShapeDtypeStruct((n_var, nx, nz), F32)
    w = jax.ShapeDtypeStruct((n_wall, 1, n_var * nx * ny), F32)
    return [c, c, s, s, w]


def exchange(faces):
    c_lo, c_hi, s_lo, s_hi, w_buf = faces
    out = []
    for axis, lo_face, hi_face in (("chord", c_lo, c_hi), ("span", s_lo, s_hi)):
        count = lax.axis_size(axis)
        forward = [(i, i + 1) for i in range(count - 1)]
        backward = [(i + 1, i) for i in range(count - 1)]
        out.append(lax.ppermute(hi_face, axis, forward))
        out.append(lax.ppermute(lo_face, axis, backward))
    out.append(lax.all_to_all(w_buf, "wall", split_axis=0, concat_axis=0, tiled=True))
    return out


def local(sensitivity, diagonal, face_coef, upper_blocks, lower_blocks, iface_blocks, production,
          send_cell, target_cell, orient, iface_weight):
    n_span = lax.axis_size("span")
    n_var = sensitivity.shape[0]
    slots = send_cell.shape[-1]
    n_rows = n_span * slots
    shape = sensitivity.shape
    n_wall = lax.axis_size("wall")
    wall_me = lax.axis_index("wall").astype(jnp.int32).reshape(1)
    blk = (upper_blocks, lower_blocks, iface_blocks, wall_me)
    send_row = send_cell.reshape(n_span, slots)
    orient_row = orient.reshape(n_span, slots)
    weight_row = iface_weight.reshape(n_span, slots)
    target_row = target_cell.reshape(n_span, slots)

    vmem = pl.BlockSpec(memory_space=pltpu.VMEM)
    smem = pl.BlockSpec(memory_space=pltpu.SMEM)
    adj_sds = jax.ShapeDtypeStruct(shape, F32)
    tgt_sds = jax.ShapeDtypeStruct((1, n_rows), jnp.int32)
    first_rows = jax.ShapeDtypeStruct((n_span, 1, (n_var + 1) * slots), F32)
    rows_sds = jax.ShapeDtypeStruct((n_span, 1, n_var * slots), F32)

    init = pl.pallas_call(
        init_kernel,
        out_shape=[adj_sds, first_rows] + face_shapes(shape, n_wall),
        in_specs=[smem] * 4 + [vmem] * 6,
        out_specs=[vmem] * 7,
    )
    adj, rows, *faces = init(*blk, sensitivity, diagonal, send_row, orient_row, weight_row, target_row)

    part_a = pl.pallas_call(
        make_part_a(slots),
        out_shape=adj_sds,
        in_specs=[smem] * 4 + [vmem] * 7,
        out_specs=vmem,
    )
    b_first = pl.pallas_call(
        make_part_b(True, False, slots),
        out_shape=[adj_sds, rows_sds] + face_shapes(shape, n_wall) + [tgt_sds],
        in_specs=[smem] * 3 + [vmem] * 9 + [smem],
        out_specs=[vmem] * 8,
    )
    b_step = pl.pallas_call(
        make_part_b(False, False, slots),
        out_shape=[adj_sds, rows_sds] + face_shapes(shape, n_wall),
        in_specs=[smem] * 3 + [vmem] * 10 + [smem],
        out_specs=[vmem] * 7,
    )
    b_last = pl.pallas_call(
        make_part_b(False, True, slots),
        out_shape=[adj_sds, jax.ShapeDtypeStruct(production.shape, F32)],
        in_specs=[smem] * 3 + [vmem] * 8,
        out_specs=[vmem] * 2,
    )
    ub, lb, ib, _ = blk
    received = None
    for sweep in range(SWEEPS):
        hcl, hch, hsl, hsh, w_inc = exchange(faces)
        incoming = lax.all_to_all(rows, "span", split_axis=0, concat_axis=0, tiled=True)
        partial = part_a(*blk, adj, sensitivity, diagonal, face_coef, hcl, hch, w_inc)
        common = (ub, lb, ib, partial, diagonal, face_coef, hsl, hsh, incoming)
        if sweep == 0:
            adj, rows, *faces, received = b_first(*common, send_row, orient_row, weight_row, wall_me)
        elif sweep < SWEEPS - 1:
            adj, rows, *faces = b_step(*common, received, send_row, orient_row, weight_row, wall_me)
        else:
            adj, gradient = b_last(*common, received, production)
    return (adj, gradient)


def solution(mesh):
    placed = (
        P(None, "chord", "span", "wall"),
        P(None, "chord", "span", "wall"),
        P(None, "chord", "span", "wall"),
        P(),
        P(),
        P(),
        P("chord", "span", "wall"),
        P("chord", "span", "wall", None, None),
        P("chord", "span", "wall", None, None),
        P("chord", "span", "wall", None, None),
        P("chord", "span", "wall", None, None),
    )
    return jax.shard_map(
        local,
        mesh=mesh,
        in_specs=placed,
        out_specs=(P(None, "chord", "span", "wall"), P("chord", "span", "wall")),
        check_vma=False,
    )
```

```python
import jax
import jax.numpy as jnp
from jax import lax
from jax.experimental import pallas as pl
from jax.experimental.pallas import tpu as pltpu
from jax.sharding import PartitionSpec as P

SWEEPS = 3
F32 = jnp.float32
BF16 = jnp.bfloat16


def split3(x):
    p1 = x.astype(BF16)
    p2 = (x - p1.astype(F32)).astype(BF16)
    return p1, p2


def gather_rows(adj, send_ref, orient_ref, weight_ref, blk, n_var, lanes):
    rows = adj.shape[1] * adj.shape[2]
    cell = flat_row(send_ref[...])
    n_rows = cell.shape[1]
    row_of = cell // lanes
    lane_of = cell % lanes
    lane_hot = (lax.broadcasted_iota(jnp.int32, (lanes, n_rows), 0) == lane_of).astype(BF16)
    row_hot = (lax.broadcasted_iota(jnp.int32, (rows, n_rows), 0) == row_of).astype(F32)
    flat = adj.reshape(n_var * rows, lanes)
    picked = jnp.dot(jnp.concatenate(split3(flat), axis=1),
                     jnp.concatenate([lane_hot] * 2, axis=0), preferred_element_type=F32)
    src = jnp.sum(picked.reshape(n_var, rows, n_rows) * row_hot[None], axis=1)
    orient = flat_row(orient_ref[...])
    weight = flat_row(weight_ref[...])
    out = []
    for i in range(n_var):
        first = None
        second = None
        for j in range(n_var):
            a = blk[2][j, 0, i] * src[j:j + 1]
            b = blk[2][j, 1, i] * src[j:j + 1]
            first = a if first is None else first + a
            second = b if second is None else second + b
        out.append(jnp.where(orient == 1, second, first) * weight)
    return out


def flat_row(x):
    return jnp.concatenate([x[t:t + 1] for t in range(x.shape[0])], axis=1)


def to_chunks(rows_ref, pieces, slots):
    n_dest = rows_ref.shape[0]
    for t in range(n_dest):
        rows_ref[t] = jnp.concatenate([p[:, t * slots:(t + 1) * slots] for p in pieces], axis=1)


def from_chunks(inc, count, slots):
    n_src = inc.shape[0]
    return [jnp.concatenate([inc[s][:, v * slots:(v + 1) * slots] for s in range(n_src)], axis=1)
            for v in range(count)]


def wall_columns(adj):
    n_var, nx, ny, nz = adj.shape
    lo, hi = [], []
    for v in range(n_var):
        t = adj[v].reshape(nx * ny, nz).T
        lo.append(t[0:1])
        hi.append(t[nz - 1:nz])
    return jnp.concatenate(lo, axis=0), jnp.concatenate(hi, axis=0)


def write_faces(adj, faces):
    c_lo, c_hi, s_lo, s_hi, w_buf, wall_me = faces
    nx, ny, nz = adj.shape[1], adj.shape[2], adj.shape[3]
    j_idx = lax.broadcasted_iota(jnp.int32, adj.shape, 2)
    c_lo[...] = adj[:, 0:1]
    c_hi[...] = adj[:, nx - 1:nx]
    s_lo[...] = jnp.sum(jnp.where(j_idx == 0, adj, 0.0), axis=2)
    s_hi[...] = jnp.sum(jnp.where(j_idx == ny - 1, adj, 0.0), axis=2)
    lo, hi = wall_columns(adj)
    me = wall_me[0]
    n_wall = w_buf.shape[0]
    lo = jnp.concatenate([lo[v:v + 1] for v in range(lo.shape[0])], axis=1)
    hi = jnp.concatenate([hi[v:v + 1] for v in range(hi.shape[0])], axis=1)
    for t in range(n_wall):
        w_buf[t] = jnp.where(me + 1 == t, hi, jnp.where(me - 1 == t, lo, 0.0))


def wall_halos(w_inc, wall_me, n_var):
    me = wall_me[0]
    n_wall, _, width = w_inc.shape
    below = None
    above = None
    for t in range(n_wall):
        b = jnp.where(me - 1 == t, w_inc[t], 0.0)
        a = jnp.where(me + 1 == t, w_inc[t], 0.0)
        below = b if below is None else below + b
        above = a if above is None else above + a
    rows = width // n_var
    unflat = lambda x: jnp.concatenate([x[:, v * rows:(v + 1) * rows] for v in range(n_var)], axis=0)
    return unflat(below), unflat(above)


def init_kernel(ub_ref, lb_ref, ib_ref, wall_me, sens_ref, diag_ref, send_ref, orient_ref, weight_ref, tgt_ref,
                adj_ref, rows_ref, c_lo, c_hi, s_lo, s_hi, w_buf):
    n_var = sens_ref.shape[0]
    lanes = sens_ref.shape[3]
    slots = send_ref.shape[1]
    blk_ref = (ub_ref, lb_ref, ib_ref)
    adj = sens_ref[...] / diag_ref[...]
    adj_ref[...] = adj
    write_faces(adj, (c_lo, c_hi, s_lo, s_hi, w_buf, wall_me))
    pieces = gather_rows(adj, send_ref, orient_ref, weight_ref, blk_ref, n_var, lanes)
    to_chunks(rows_ref, pieces + [flat_row(tgt_ref[...]).astype(F32)], slots)


def scatter_rows(incoming, cell, shape):
    n_var, nx, ny, nz = shape
    rows = nx * ny
    n_rows = incoming.shape[1]
    row_of = cell // nz
    lane_of = cell % nz
    row_hot = (lax.broadcasted_iota(jnp.int32, (rows, n_rows), 0) == row_of).astype(BF16)
    lane_hot = (lax.broadcasted_iota(jnp.int32, (nz, n_rows), 0) == lane_of).astype(BF16)
    lhs = jnp.concatenate([(row_hot[None] * part[:, None, :]).reshape(n_var * rows, n_rows)
                           for part in split3(incoming)], axis=1)
    coupled = lax.dot_general(lhs, jnp.concatenate([lane_hot] * 2, axis=1), (((1,), (1,)), ((), ())),
                              preferred_element_type=F32)
    return coupled.reshape(n_var, nx, ny, nz)


def sweep_body(blk, adj, sens, diag, face, halos):
    n_var, nx, ny, nz = adj.shape
    rows = nx * ny
    h_c_lo, h_c_hi, h_s_lo, h_s_hi, h_w_lo, h_w_hi = halos
    j_idx = lax.broadcasted_iota(jnp.int32, adj.shape, 2)
    k_idx = lax.broadcasted_iota(jnp.int32, adj.shape, 3)
    kk = lax.broadcasted_iota(jnp.int32, (nz, rows), 0)
    wall = []
    for v in range(n_var):
        z = jnp.where(kk == 0, h_w_lo[v:v + 1], jnp.where(kk == nz - 1, h_w_hi[v:v + 1], 0.0))
        wall.append(z.T.reshape(nx, ny, nz))
    wall = jnp.stack(wall, axis=0)
    up = [
        jnp.concatenate([adj[:, 1:], h_c_hi], axis=1),
        jnp.where(j_idx == ny - 1, h_s_hi[:, :, None, :], pltpu.roll(adj, ny - 1, 2)),
        jnp.where(k_idx == nz - 1, wall, pltpu.roll(adj, nz - 1, 3)),
    ]
    lo = [
        jnp.concatenate([h_c_lo, adj[:, :-1]], axis=1),
        jnp.where(j_idx == 0, h_s_lo[:, :, None, :], pltpu.roll(adj, 1, 2)),
        jnp.where(k_idx == 0, wall, pltpu.roll(adj, 1, 3)),
    ]
    new = []
    for i in range(n_var):
        applied = diag[i] * adj[i]
        for d in range(3):
            acc = None
            for j in range(n_var):
                t = blk[0][d, j, i] * up[d][j] + blk[1][d, j, i] * lo[d][j]
                acc = t if acc is None else acc + t
            applied = applied + face[d] * acc
        new.append(adj[i] + (sens[i] - applied) / diag[i])
    return jnp.stack(new, axis=0)


def make_part_a(slots):
    def kernel(ub_ref, lb_ref, ib_ref, wall_me, adj_ref, sens_ref, diag_ref, face_ref, hcl, hch, w_inc, out_ref):
        n_var, nx, ny, nz = adj_ref.shape
        blk_ref = (ub_ref, lb_ref, ib_ref)
        none = jnp.zeros((n_var, nx, nz), F32)
        halos = (hcl[...], hch[...], none, none) + wall_halos(w_inc[...], wall_me, n_var)
        out_ref[...] = sweep_body(blk_ref, adj_ref[...], sens_ref[...], diag_ref[...], face_ref[...], halos)
    return kernel


def make_part_b(first, last, slots):
    def kernel(ub_ref, lb_ref, ib_ref, part_ref, diag_ref, face_ref, hsl, hsh, inc_ref, *rest):
        n_var, nx, ny, nz = part_ref.shape
        inc = inc_ref[...]
        if first:
            tgt_out, rest = rest[-1], rest[:-1]
            got = from_chunks(inc, n_var + 1, slots)
            cell = got[n_var].astype(jnp.int32)
            tgt_out[...] = cell
        else:
            tgt_ref, rest = rest[0], rest[1:]
            got = from_chunks(inc, n_var, slots)
            cell = tgt_ref[...]
        coupled = scatter_rows(jnp.concatenate(got[:n_var], axis=0), cell, part_ref.shape)
        part = part_ref[...]
        diag = diag_ref[...]
        face_y = face_ref[1]
        h_lo = hsl[...]
        h_hi = hsh[...]
        j_idx = lax.broadcasted_iota(jnp.int32, (nx, ny, nz), 1)
        new = []
        for i in range(n_var):
            above = None
            below = None
            for j in range(n_var):
                a = ub_ref[1, j, i] * h_hi[j]
                b = lb_ref[1, j, i] * h_lo[j]
                above = a if above is None else above + a
                below = b if below is None else below + b
            edge = (jnp.where(j_idx == ny - 1, above[:, None, :], 0.0)
                    + jnp.where(j_idx == 0, below[:, None, :], 0.0))
            new.append(part[i] - (face_y * edge + coupled[i]) / diag[i])
        new = jnp.stack(new, axis=0)
        if last:
            prod_ref, out_ref, grad_ref = rest
            out_ref[...] = new
            grad_ref[...] = prod_ref[...] * new[n_var - 1]
        else:
            send_ref, orient_ref, weight_ref, wall_me, out_ref, rows_ref, c_lo, c_hi, s_lo, s_hi, w_buf = rest
            out_ref[...] = new
            write_faces(new, (c_lo, c_hi, s_lo, s_hi, w_buf, wall_me))
            blk_ref = (ub_ref, lb_ref, ib_ref)
            to_chunks(rows_ref, gather_rows(new, send_ref, orient_ref, weight_ref, blk_ref, n_var, nz), slots)
    return kernel


def face_shapes(shape, n_wall):
    n_var, nx, ny, nz = shape
    c = jax.ShapeDtypeStruct((n_var, 1, ny, nz), F32)
    s = jax.ShapeDtypeStruct((n_var, nx, nz), F32)
    w = jax.ShapeDtypeStruct((n_wall, 1, n_var * nx * ny), F32)
    return [c, c, s, s, w]


def exchange(faces):
    c_lo, c_hi, s_lo, s_hi, w_buf = faces
    out = []
    for axis, lo_face, hi_face in (("chord", c_lo, c_hi), ("span", s_lo, s_hi)):
        count = lax.axis_size(axis)
        forward = [(i, i + 1) for i in range(count - 1)]
        backward = [(i + 1, i) for i in range(count - 1)]
        out.append(lax.ppermute(hi_face, axis, forward))
        out.append(lax.ppermute(lo_face, axis, backward))
    out.append(lax.all_to_all(w_buf, "wall", split_axis=0, concat_axis=0, tiled=True))
    return out


def local(sensitivity, diagonal, face_coef, upper_blocks, lower_blocks, iface_blocks, production,
          send_cell, target_cell, orient, iface_weight):
    n_span = lax.axis_size("span")
    n_var = sensitivity.shape[0]
    slots = send_cell.shape[-1]
    n_rows = n_span * slots
    shape = sensitivity.shape
    n_wall = lax.axis_size("wall")
    wall_me = lax.axis_index("wall").astype(jnp.int32).reshape(1)
    blk = (upper_blocks, lower_blocks, jnp.transpose(iface_blocks, (1, 0, 2)), wall_me)
    send_row = send_cell.reshape(n_span, slots)
    orient_row = orient.reshape(n_span, slots)
    weight_row = iface_weight.reshape(n_span, slots)
    target_row = target_cell.reshape(n_span, slots)

    vmem = pl.BlockSpec(memory_space=pltpu.VMEM)
    smem = pl.BlockSpec(memory_space=pltpu.SMEM)
    adj_sds = jax.ShapeDtypeStruct(shape, F32)
    tgt_sds = jax.ShapeDtypeStruct((1, n_rows), jnp.int32)
    first_rows = jax.ShapeDtypeStruct((n_span, 1, (n_var + 1) * slots), F32)
    rows_sds = jax.ShapeDtypeStruct((n_span, 1, n_var * slots), F32)

    init = pl.pallas_call(
        init_kernel,
        out_shape=[adj_sds, first_rows] + face_shapes(shape, n_wall),
        in_specs=[smem] * 4 + [vmem] * 6,
        out_specs=[vmem] * 7,
    )
    adj, rows, *faces = init(*blk, sensitivity, diagonal, send_row, orient_row, weight_row, target_row)

    part_a = pl.pallas_call(
        make_part_a(slots),
        out_shape=adj_sds,
        in_specs=[smem] * 4 + [vmem] * 7,
        out_specs=vmem,
    )
    b_first = pl.pallas_call(
        make_part_b(True, False, slots),
        out_shape=[adj_sds, rows_sds] + face_shapes(shape, n_wall) + [tgt_sds],
        in_specs=[smem] * 3 + [vmem] * 9 + [smem],
        out_specs=[vmem] * 8,
    )
    b_step = pl.pallas_call(
        make_part_b(False, False, slots),
        out_shape=[adj_sds, rows_sds] + face_shapes(shape, n_wall),
        in_specs=[smem] * 3 + [vmem] * 10 + [smem],
        out_specs=[vmem] * 7,
    )
    b_last = pl.pallas_call(
        make_part_b(False, True, slots),
        out_shape=[adj_sds, jax.ShapeDtypeStruct(production.shape, F32)],
        in_specs=[smem] * 3 + [vmem] * 8,
        out_specs=[vmem] * 2,
    )
    ub, lb, ib, _ = blk
    received = None
    for sweep in range(SWEEPS):
        hcl, hch, hsl, hsh, w_inc = exchange(faces)
        incoming = lax.all_to_all(rows, "span", split_axis=0, concat_axis=0, tiled=True)
        partial = part_a(*blk, adj, sensitivity, diagonal, face_coef, hcl, hch, w_inc)
        common = (ub, lb, ib, partial, diagonal, face_coef, hsl, hsh, incoming)
        if sweep == 0:
            adj, rows, *faces, received = b_first(*common, send_row, orient_row, weight_row, wall_me)
        elif sweep < SWEEPS - 1:
            adj, rows, *faces = b_step(*common, received, send_row, orient_row, weight_row, wall_me)
        else:
            adj, gradient = b_last(*common, received, production)
    return (adj, gradient)


def solution(mesh):
    placed = (
        P(None, "chord", "span", "wall"),
        P(None, "chord", "span", "wall"),
        P(None, "chord", "span", "wall"),
        P(),
        P(),
        P(),
        P("chord", "span", "wall"),
        P("chord", "span", "wall", None, None),
        P("chord", "span", "wall", None, None),
        P("chord", "span", "wall", None, None),
        P("chord", "span", "wall", None, None),
    )
    return jax.shard_map(
        local,
        mesh=mesh,
        in_specs=placed,
        out_specs=(P(None, "chord", "span", "wall"), P("chord", "span", "wall")),
        check_vma=False,
    )
```

```python
import jax
import jax.numpy as jnp
from jax import lax
from jax.experimental import pallas as pl
from jax.experimental.pallas import tpu as pltpu
from jax.sharding import PartitionSpec as P

SWEEPS = 3
F32 = jnp.float32
BF16 = jnp.bfloat16


def split3(x):
    p1 = x.astype(BF16)
    p2 = (x - p1.astype(F32)).astype(BF16)
    return p1, p2


def gather_rows(adj, send_ref, orient_ref, weight_ref, blk, n_var, lanes):
    rows = adj.shape[1] * adj.shape[2]
    cell = flat_row(send_ref[...])
    n_rows = cell.shape[1]
    row_of = cell // lanes
    lane_of = cell % lanes
    lane_hot = (lax.broadcasted_iota(jnp.int32, (lanes, n_rows), 0) == lane_of).astype(BF16)
    row_hot = (lax.broadcasted_iota(jnp.int32, (rows, n_rows), 0) == row_of).astype(F32)
    flat = adj.reshape(n_var * rows, lanes)
    picked = jnp.dot(jnp.concatenate(split3(flat), axis=1),
                     jnp.concatenate([lane_hot] * 2, axis=0), preferred_element_type=F32)
    src = jnp.sum(picked.reshape(n_var, rows, n_rows) * row_hot[None], axis=1)
    orient = flat_row(orient_ref[...])
    weight = flat_row(weight_ref[...])
    out = []
    for i in range(n_var):
        first = None
        second = None
        for j in range(n_var):
            a = blk[2][j, 0, i] * src[j:j + 1]
            b = blk[2][j, 1, i] * src[j:j + 1]
            first = a if first is None else first + a
            second = b if second is None else second + b
        out.append(jnp.where(orient == 1, second, first) * weight)
    return out


def flat_row(x):
    return jnp.concatenate([x[t:t + 1] for t in range(x.shape[0])], axis=1)


def to_chunks(rows_ref, pieces, slots):
    n_dest, n_sub, lanes = rows_ref.shape
    pad = n_sub * lanes - len(pieces) * slots
    for t in range(n_dest):
        flat = [p[:, t * slots:(t + 1) * slots] for p in pieces]
        if pad:
            flat.append(jnp.zeros((1, pad), F32))
        flat = jnp.concatenate(flat, axis=1)
        rows_ref[t] = jnp.concatenate([flat[:, r * lanes:(r + 1) * lanes] for r in range(n_sub)], axis=0)


def from_chunks(inc, count, slots):
    n_src, _, lanes = inc.shape

    def piece(s, v):
        r, c = divmod(v * slots, lanes)
        return inc[s][r:r + 1, c:c + slots]
    return [jnp.concatenate([piece(s, v) for s in range(n_src)], axis=1) for v in range(count)]


def wall_columns(adj):
    n_var, nx, ny, nz = adj.shape
    lo, hi = [], []
    for v in range(n_var):
        t = adj[v].reshape(nx * ny, nz).T
        lo.append(t[0:1])
        hi.append(t[nz - 1:nz])
    return jnp.concatenate(lo, axis=0), jnp.concatenate(hi, axis=0)


def write_faces(adj, faces):
    c_lo, c_hi, s_lo, s_hi, w_buf, wall_me = faces
    nx, ny, nz = adj.shape[1], adj.shape[2], adj.shape[3]
    j_idx = lax.broadcasted_iota(jnp.int32, adj.shape, 2)
    c_lo[...] = adj[:, 0:1]
    c_hi[...] = adj[:, nx - 1:nx]
    s_lo[...] = jnp.sum(jnp.where(j_idx == 0, adj, 0.0), axis=2)
    s_hi[...] = jnp.sum(jnp.where(j_idx == ny - 1, adj, 0.0), axis=2)
    lo, hi = wall_columns(adj)
    me = wall_me[0]
    n_wall = w_buf.shape[0]
    lo = jnp.concatenate([lo[v:v + 1] for v in range(lo.shape[0])], axis=1)
    hi = jnp.concatenate([hi[v:v + 1] for v in range(hi.shape[0])], axis=1)
    for t in range(n_wall):
        w_buf[t] = jnp.where(me + 1 == t, hi, jnp.where(me - 1 == t, lo, 0.0))


def wall_halos(w_inc, wall_me, n_var):
    me = wall_me[0]
    n_wall, _, width = w_inc.shape
    below = None
    above = None
    for t in range(n_wall):
        b = jnp.where(me - 1 == t, w_inc[t], 0.0)
        a = jnp.where(me + 1 == t, w_inc[t], 0.0)
        below = b if below is None else below + b
        above = a if above is None else above + a
    rows = width // n_var
    unflat = lambda x: jnp.concatenate([x[:, v * rows:(v + 1) * rows] for v in range(n_var)], axis=0)
    return unflat(below), unflat(above)


def init_kernel(ub_ref, lb_ref, ib_ref, wall_me, sens_ref, diag_ref, send_ref, orient_ref, weight_ref, tgt_ref,
                adj_ref, rows_ref, c_lo, c_hi, s_lo, s_hi, w_buf):
    n_var = sens_ref.shape[0]
    lanes = sens_ref.shape[3]
    slots = send_ref.shape[1]
    blk_ref = (ub_ref, lb_ref, ib_ref)
    adj = sens_ref[...] / diag_ref[...]
    adj_ref[...] = adj
    write_faces(adj, (c_lo, c_hi, s_lo, s_hi, w_buf, wall_me))
    pieces = gather_rows(adj, send_ref, orient_ref, weight_ref, blk_ref, n_var, lanes)
    to_chunks(rows_ref, pieces + [flat_row(tgt_ref[...]).astype(F32)], slots)


def scatter_rows(incoming, cell, shape):
    n_var, nx, ny, nz = shape
    rows = nx * ny
    n_rows = incoming.shape[1]
    row_of = cell // nz
    lane_of = cell % nz
    row_hot = (lax.broadcasted_iota(jnp.int32, (rows, n_rows), 0) == row_of).astype(BF16)
    lane_hot = (lax.broadcasted_iota(jnp.int32, (nz, n_rows), 0) == lane_of).astype(BF16)
    lhs = jnp.concatenate([(row_hot[None] * part[:, None, :]).reshape(n_var * rows, n_rows)
                           for part in split3(incoming)], axis=1)
    coupled = lax.dot_general(lhs, jnp.concatenate([lane_hot] * 2, axis=1), (((1,), (1,)), ((), ())),
                              preferred_element_type=F32)
    return coupled.reshape(n_var, nx, ny, nz)


def sweep_body(blk, adj, sens, diag, face, halos):
    n_var, nx, ny, nz = adj.shape
    rows = nx * ny
    h_c_lo, h_c_hi, h_s_lo, h_s_hi, h_w_lo, h_w_hi = halos
    j_idx = lax.broadcasted_iota(jnp.int32, adj.shape, 2)
    k_idx = lax.broadcasted_iota(jnp.int32, adj.shape, 3)
    kk = lax.broadcasted_iota(jnp.int32, (nz, rows), 0)
    wall = []
    for v in range(n_var):
        z = jnp.where(kk == 0, h_w_lo[v:v + 1], jnp.where(kk == nz - 1, h_w_hi[v:v + 1], 0.0))
        wall.append(z.T.reshape(nx, ny, nz))
    wall = jnp.stack(wall, axis=0)
    up = [
        jnp.concatenate([adj[:, 1:], h_c_hi], axis=1),
        jnp.where(j_idx == ny - 1, h_s_hi[:, :, None, :], pltpu.roll(adj, ny - 1, 2)),
        jnp.where(k_idx == nz - 1, wall, pltpu.roll(adj, nz - 1, 3)),
    ]
    lo = [
        jnp.concatenate([h_c_lo, adj[:, :-1]], axis=1),
        jnp.where(j_idx == 0, h_s_lo[:, :, None, :], pltpu.roll(adj, 1, 2)),
        jnp.where(k_idx == 0, wall, pltpu.roll(adj, 1, 3)),
    ]
    new = []
    for i in range(n_var):
        applied = diag[i] * adj[i]
        for d in range(3):
            acc = None
            for j in range(n_var):
                t = blk[0][d, j, i] * up[d][j] + blk[1][d, j, i] * lo[d][j]
                acc = t if acc is None else acc + t
            applied = applied + face[d] * acc
        new.append(adj[i] + (sens[i] - applied) / diag[i])
    return jnp.stack(new, axis=0)


def make_part_a(slots):
    def kernel(ub_ref, lb_ref, ib_ref, wall_me, adj_ref, sens_ref, diag_ref, face_ref, hcl, hch, w_inc, out_ref):
        n_var, nx, ny, nz = adj_ref.shape
        blk_ref = (ub_ref, lb_ref, ib_ref)
        none = jnp.zeros((n_var, nx, nz), F32)
        halos = (hcl[...], hch[...], none, none) + wall_halos(w_inc[...], wall_me, n_var)
        out_ref[...] = sweep_body(blk_ref, adj_ref[...], sens_ref[...], diag_ref[...], face_ref[...], halos)
    return kernel


def make_part_b(first, last, slots):
    def kernel(ub_ref, lb_ref, ib_ref, part_ref, diag_ref, face_ref, hsl, hsh, inc_ref, *rest):
        n_var, nx, ny, nz = part_ref.shape
        inc = inc_ref[...]
        if first:
            tgt_out, rest = rest[-1], rest[:-1]
            got = from_chunks(inc, n_var + 1, slots)
            cell = got[n_var].astype(jnp.int32)
            tgt_out[...] = cell
        else:
            tgt_ref, rest = rest[0], rest[1:]
            got = from_chunks(inc, n_var, slots)
            cell = tgt_ref[...]
        coupled = scatter_rows(jnp.concatenate(got[:n_var], axis=0), cell, part_ref.shape)
        part = part_ref[...]
        diag = diag_ref[...]
        face_y = face_ref[1]
        h_lo = hsl[...]
        h_hi = hsh[...]
        j_idx = lax.broadcasted_iota(jnp.int32, (nx, ny, nz), 1)
        new = []
        for i in range(n_var):
            above = None
            below = None
            for j in range(n_var):
                a = ub_ref[1, j, i] * h_hi[j]
                b = lb_ref[1, j, i] * h_lo[j]
                above = a if above is None else above + a
                below = b if below is None else below + b
            edge = (jnp.where(j_idx == ny - 1, above[:, None, :], 0.0)
                    + jnp.where(j_idx == 0, below[:, None, :], 0.0))
            new.append(part[i] - (face_y * edge + coupled[i]) / diag[i])
        new = jnp.stack(new, axis=0)
        if last:
            prod_ref, out_ref, grad_ref = rest
            out_ref[...] = new
            grad_ref[...] = prod_ref[...] * new[n_var - 1]
        else:
            send_ref, orient_ref, weight_ref, wall_me, out_ref, rows_ref, c_lo, c_hi, s_lo, s_hi, w_buf = rest
            out_ref[...] = new
            write_faces(new, (c_lo, c_hi, s_lo, s_hi, w_buf, wall_me))
            blk_ref = (ub_ref, lb_ref, ib_ref)
            to_chunks(rows_ref, gather_rows(new, send_ref, orient_ref, weight_ref, blk_ref, n_var, nz), slots)
    return kernel


def face_shapes(shape, n_wall):
    n_var, nx, ny, nz = shape
    c = jax.ShapeDtypeStruct((n_var, 1, ny, nz), F32)
    s = jax.ShapeDtypeStruct((n_var, nx, nz), F32)
    w = jax.ShapeDtypeStruct((n_wall, 1, n_var * nx * ny), F32)
    return [c, c, s, s, w]


def exchange(faces):
    c_lo, c_hi, s_lo, s_hi, w_buf = faces
    out = []
    for axis, lo_face, hi_face in (("chord", c_lo, c_hi), ("span", s_lo, s_hi)):
        count = lax.axis_size(axis)
        forward = [(i, i + 1) for i in range(count - 1)]
        backward = [(i + 1, i) for i in range(count - 1)]
        out.append(lax.ppermute(hi_face, axis, forward))
        out.append(lax.ppermute(lo_face, axis, backward))
    out.append(lax.all_to_all(w_buf, "wall", split_axis=0, concat_axis=0, tiled=True))
    return out


def local(sensitivity, diagonal, face_coef, upper_blocks, lower_blocks, iface_blocks, production,
          send_cell, target_cell, orient, iface_weight):
    n_span = lax.axis_size("span")
    n_var = sensitivity.shape[0]
    slots = send_cell.shape[-1]
    n_rows = n_span * slots
    shape = sensitivity.shape
    n_wall = lax.axis_size("wall")
    wall_me = lax.axis_index("wall").astype(jnp.int32).reshape(1)
    blk = (upper_blocks, lower_blocks, jnp.transpose(iface_blocks, (1, 0, 2)), wall_me)
    send_row = send_cell.reshape(n_span, slots)
    orient_row = orient.reshape(n_span, slots)
    weight_row = iface_weight.reshape(n_span, slots)
    target_row = target_cell.reshape(n_span, slots)

    vmem = pl.BlockSpec(memory_space=pltpu.VMEM)
    smem = pl.BlockSpec(memory_space=pltpu.SMEM)
    adj_sds = jax.ShapeDtypeStruct(shape, F32)
    tgt_sds = jax.ShapeDtypeStruct((1, n_rows), jnp.int32)
    lanes = shape[3]
    first_rows = jax.ShapeDtypeStruct((n_span, -(-(n_var + 1) * slots // lanes), lanes), F32)
    rows_sds = jax.ShapeDtypeStruct((n_span, -(-n_var * slots // lanes), lanes), F32)

    init = pl.pallas_call(
        init_kernel,
        out_shape=[adj_sds, first_rows] + face_shapes(shape, n_wall),
        in_specs=[smem] * 4 + [vmem] * 6,
        out_specs=[vmem] * 7,
    )
    adj, rows, *faces = init(*blk, sensitivity, diagonal, send_row, orient_row, weight_row, target_row)

    part_a = pl.pallas_call(
        make_part_a(slots),
        out_shape=adj_sds,
        in_specs=[smem] * 4 + [vmem] * 7,
        out_specs=vmem,
    )
    b_first = pl.pallas_call(
        make_part_b(True, False, slots),
        out_shape=[adj_sds, rows_sds] + face_shapes(shape, n_wall) + [tgt_sds],
        in_specs=[smem] * 3 + [vmem] * 9 + [smem],
        out_specs=[vmem] * 8,
    )
    b_step = pl.pallas_call(
        make_part_b(False, False, slots),
        out_shape=[adj_sds, rows_sds] + face_shapes(shape, n_wall),
        in_specs=[smem] * 3 + [vmem] * 10 + [smem],
        out_specs=[vmem] * 7,
    )
    b_last = pl.pallas_call(
        make_part_b(False, True, slots),
        out_shape=[adj_sds, jax.ShapeDtypeStruct(production.shape, F32)],
        in_specs=[smem] * 3 + [vmem] * 8,
        out_specs=[vmem] * 2,
    )
    ub, lb, ib, _ = blk
    received = None
    for sweep in range(SWEEPS):
        hcl, hch, hsl, hsh, w_inc = exchange(faces)
        incoming = lax.all_to_all(rows, "span", split_axis=0, concat_axis=0, tiled=True)
        partial = part_a(*blk, adj, sensitivity, diagonal, face_coef, hcl, hch, w_inc)
        common = (ub, lb, ib, partial, diagonal, face_coef, hsl, hsh, incoming)
        if sweep == 0:
            adj, rows, *faces, received = b_first(*common, send_row, orient_row, weight_row, wall_me)
        elif sweep < SWEEPS - 1:
            adj, rows, *faces = b_step(*common, received, send_row, orient_row, weight_row, wall_me)
        else:
            adj, gradient = b_last(*common, received, production)
    return (adj, gradient)


def solution(mesh):
    placed = (
        P(None, "chord", "span", "wall"),
        P(None, "chord", "span", "wall"),
        P(None, "chord", "span", "wall"),
        P(),
        P(),
        P(),
        P("chord", "span", "wall"),
        P("chord", "span", "wall", None, None),
        P("chord", "span", "wall", None, None),
        P("chord", "span", "wall", None, None),
        P("chord", "span", "wall", None, None),
    )
    return jax.shard_map(
        local,
        mesh=mesh,
        in_specs=placed,
        out_specs=(P(None, "chord", "span", "wall"), P("chord", "span", "wall")),
        check_vma=False,
    )
```

```python
import jax
import jax.numpy as jnp
from jax import lax
from jax.experimental import pallas as pl
from jax.experimental.pallas import tpu as pltpu
from jax.sharding import PartitionSpec as P

SWEEPS = 3
F32 = jnp.float32
BF16 = jnp.bfloat16


def split3(x):
    p1 = x.astype(BF16)
    p2 = (x - p1.astype(F32)).astype(BF16)
    return p1, p2


def gather_rows(adj, send_ref, orient_ref, weight_ref, blk, n_var, lanes):
    rows = adj.shape[1] * adj.shape[2]
    cell = flat_row(send_ref[...])
    n_rows = cell.shape[1]
    row_of = cell // lanes
    lane_of = cell % lanes
    lane_hot = (lax.broadcasted_iota(jnp.int32, (lanes, n_rows), 0) == lane_of).astype(BF16)
    row_hot = (lax.broadcasted_iota(jnp.int32, (rows, n_rows), 0) == row_of).astype(F32)
    flat = adj.reshape(n_var * rows, lanes)
    picked = jnp.dot(jnp.concatenate(split3(flat), axis=1),
                     jnp.concatenate([lane_hot] * 2, axis=0), preferred_element_type=F32)
    src = jnp.sum(picked.reshape(n_var, rows, n_rows) * row_hot[None], axis=1)
    orient = flat_row(orient_ref[...])
    weight = flat_row(weight_ref[...])
    out = []
    for i in range(n_var):
        first = None
        second = None
        for j in range(n_var):
            a = blk[2][j, 0, i] * src[j:j + 1]
            b = blk[2][j, 1, i] * src[j:j + 1]
            first = a if first is None else first + a
            second = b if second is None else second + b
        out.append(jnp.where(orient == 1, second, first) * weight)
    return out


def flat_row(x):
    return jnp.concatenate([x[t:t + 1] for t in range(x.shape[0])], axis=1)


def to_chunks(rows_ref, pieces, slots):
    n_dest, n_sub, lanes = rows_ref.shape
    pad = n_sub * lanes - len(pieces) * slots
    for t in range(n_dest):
        flat = [p[:, t * slots:(t + 1) * slots] for p in pieces]
        if pad:
            flat.append(jnp.zeros((1, pad), F32))
        flat = jnp.concatenate(flat, axis=1)
        rows_ref[t] = jnp.concatenate([flat[:, r * lanes:(r + 1) * lanes] for r in range(n_sub)], axis=0)


def from_chunks(inc, count, slots):
    n_src, _, lanes = inc.shape

    def piece(s, v):
        r, c = divmod(v * slots, lanes)
        return inc[s][r:r + 1, c:c + slots]
    return [jnp.concatenate([piece(s, v) for s in range(n_src)], axis=1) for v in range(count)]


def wall_columns(adj):
    n_var, nx, ny, nz = adj.shape
    lo, hi = [], []
    for v in range(n_var):
        t = adj[v].reshape(nx * ny, nz).T
        lo.append(t[0:1])
        hi.append(t[nz - 1:nz])
    return jnp.concatenate(lo, axis=0), jnp.concatenate(hi, axis=0)


def write_faces(adj, faces):
    c_lo, c_hi, s_lo, s_hi, w_buf, wall_me = faces
    nx, ny, nz = adj.shape[1], adj.shape[2], adj.shape[3]
    j_idx = lax.broadcasted_iota(jnp.int32, adj.shape, 2)
    c_lo[...] = adj[:, 0:1]
    c_hi[...] = adj[:, nx - 1:nx]
    s_lo[...] = jnp.sum(jnp.where(j_idx == 0, adj, 0.0), axis=2)
    s_hi[...] = jnp.sum(jnp.where(j_idx == ny - 1, adj, 0.0), axis=2)
    lo, hi = wall_columns(adj)
    me = wall_me[0]
    n_wall = w_buf.shape[0]
    for t in range(n_wall):
        w_buf[t] = jnp.where(me + 1 == t, hi, jnp.where(me - 1 == t, lo, 0.0))


def wall_halos(w_inc, wall_me, n_var):
    me = wall_me[0]
    n_wall = w_inc.shape[0]
    below = None
    above = None
    for t in range(n_wall):
        b = jnp.where(me - 1 == t, w_inc[t], 0.0)
        a = jnp.where(me + 1 == t, w_inc[t], 0.0)
        below = b if below is None else below + b
        above = a if above is None else above + a
    return below, above


def init_kernel(ub_ref, lb_ref, ib_ref, wall_me, sens_ref, diag_ref, send_ref, orient_ref, weight_ref, tgt_ref,
                adj_ref, rows_ref, c_lo, c_hi, s_lo, s_hi, w_buf):
    n_var = sens_ref.shape[0]
    lanes = sens_ref.shape[3]
    slots = send_ref.shape[1]
    blk_ref = (ub_ref, lb_ref, ib_ref)
    adj = sens_ref[...] / diag_ref[...]
    adj_ref[...] = adj
    write_faces(adj, (c_lo, c_hi, s_lo, s_hi, w_buf, wall_me))
    pieces = gather_rows(adj, send_ref, orient_ref, weight_ref, blk_ref, n_var, lanes)
    to_chunks(rows_ref, pieces + [flat_row(tgt_ref[...]).astype(F32)], slots)


def scatter_rows(incoming, cell, shape):
    n_var, nx, ny, nz = shape
    rows = nx * ny
    n_rows = incoming.shape[1]
    row_of = cell // nz
    lane_of = cell % nz
    row_hot = (lax.broadcasted_iota(jnp.int32, (rows, n_rows), 0) == row_of).astype(BF16)
    lane_hot = (lax.broadcasted_iota(jnp.int32, (nz, n_rows), 0) == lane_of).astype(BF16)
    lhs = jnp.concatenate([(row_hot[None] * part[:, None, :]).reshape(n_var * rows, n_rows)
                           for part in split3(incoming)], axis=1)
    coupled = lax.dot_general(lhs, jnp.concatenate([lane_hot] * 2, axis=1), (((1,), (1,)), ((), ())),
                              preferred_element_type=F32)
    return coupled.reshape(n_var, nx, ny, nz)


def sweep_body(blk, adj, sens, diag, face, halos):
    n_var, nx, ny, nz = adj.shape
    rows = nx * ny
    h_c_lo, h_c_hi, h_s_lo, h_s_hi, h_w_lo, h_w_hi = halos
    j_idx = lax.broadcasted_iota(jnp.int32, adj.shape, 2)
    k_idx = lax.broadcasted_iota(jnp.int32, adj.shape, 3)
    kk = lax.broadcasted_iota(jnp.int32, (nz, rows), 0)
    wall = []
    for v in range(n_var):
        z = jnp.where(kk == 0, h_w_lo[v:v + 1], jnp.where(kk == nz - 1, h_w_hi[v:v + 1], 0.0))
        wall.append(z.T.reshape(nx, ny, nz))
    wall = jnp.stack(wall, axis=0)
    up = [
        jnp.concatenate([adj[:, 1:], h_c_hi], axis=1),
        jnp.where(j_idx == ny - 1, h_s_hi[:, :, None, :], pltpu.roll(adj, ny - 1, 2)),
        jnp.where(k_idx == nz - 1, wall, pltpu.roll(adj, nz - 1, 3)),
    ]
    lo = [
        jnp.concatenate([h_c_lo, adj[:, :-1]], axis=1),
        jnp.where(j_idx == 0, h_s_lo[:, :, None, :], pltpu.roll(adj, 1, 2)),
        jnp.where(k_idx == 0, wall, pltpu.roll(adj, 1, 3)),
    ]
    new = []
    for i in range(n_var):
        applied = diag[i] * adj[i]
        for d in range(3):
            acc = None
            for j in range(n_var):
                t = blk[0][d, j, i] * up[d][j] + blk[1][d, j, i] * lo[d][j]
                acc = t if acc is None else acc + t
            applied = applied + face[d] * acc
        new.append(adj[i] + (sens[i] - applied) / diag[i])
    return jnp.stack(new, axis=0)


def make_part_a(slots):
    def kernel(ub_ref, lb_ref, ib_ref, wall_me, adj_ref, sens_ref, diag_ref, face_ref, hcl, hch, w_inc, out_ref):
        n_var, nx, ny, nz = adj_ref.shape
        blk_ref = (ub_ref, lb_ref, ib_ref)
        none = jnp.zeros((n_var, nx, nz), F32)
        halos = (hcl[...], hch[...], none, none) + wall_halos(w_inc[...], wall_me, n_var)
        out_ref[...] = sweep_body(blk_ref, adj_ref[...], sens_ref[...], diag_ref[...], face_ref[...], halos)
    return kernel


def make_part_b(first, last, slots):
    def kernel(ub_ref, lb_ref, ib_ref, part_ref, diag_ref, face_ref, hsl, hsh, inc_ref, *rest):
        n_var, nx, ny, nz = part_ref.shape
        inc = inc_ref[...]
        if first:
            tgt_out, rest = rest[-1], rest[:-1]
            got = from_chunks(inc, n_var + 1, slots)
            cell = got[n_var].astype(jnp.int32)
            tgt_out[...] = cell
        else:
            tgt_ref, rest = rest[0], rest[1:]
            got = from_chunks(inc, n_var, slots)
            cell = tgt_ref[...]
        coupled = scatter_rows(jnp.concatenate(got[:n_var], axis=0), cell, part_ref.shape)
        part = part_ref[...]
        diag = diag_ref[...]
        face_y = face_ref[1]
        h_lo = hsl[...]
        h_hi = hsh[...]
        j_idx = lax.broadcasted_iota(jnp.int32, (nx, ny, nz), 1)
        new = []
        for i in range(n_var):
            above = None
            below = None
            for j in range(n_var):
                a = ub_ref[1, j, i] * h_hi[j]
                b = lb_ref[1, j, i] * h_lo[j]
                above = a if above is None else above + a
                below = b if below is None else below + b
            edge = (jnp.where(j_idx == ny - 1, above[:, None, :], 0.0)
                    + jnp.where(j_idx == 0, below[:, None, :], 0.0))
            new.append(part[i] - (face_y * edge + coupled[i]) / diag[i])
        new = jnp.stack(new, axis=0)
        if last:
            prod_ref, out_ref, grad_ref = rest
            out_ref[...] = new
            grad_ref[...] = prod_ref[...] * new[n_var - 1]
        else:
            send_ref, orient_ref, weight_ref, wall_me, out_ref, rows_ref, c_lo, c_hi, s_lo, s_hi, w_buf = rest
            out_ref[...] = new
            write_faces(new, (c_lo, c_hi, s_lo, s_hi, w_buf, wall_me))
            blk_ref = (ub_ref, lb_ref, ib_ref)
            to_chunks(rows_ref, gather_rows(new, send_ref, orient_ref, weight_ref, blk_ref, n_var, nz), slots)
    return kernel


def face_shapes(shape, n_wall):
    n_var, nx, ny, nz = shape
    c = jax.ShapeDtypeStruct((n_var, 1, ny, nz), F32)
    s = jax.ShapeDtypeStruct((n_var, nx, nz), F32)
    w = jax.ShapeDtypeStruct((n_wall, n_var, nx * ny), F32)
    return [c, c, s, s, w]


def exchange(faces):
    c_lo, c_hi, s_lo, s_hi, w_buf = faces
    out = []
    for axis, lo_face, hi_face in (("chord", c_lo, c_hi), ("span", s_lo, s_hi)):
        count = lax.axis_size(axis)
        forward = [(i, i + 1) for i in range(count - 1)]
        backward = [(i + 1, i) for i in range(count - 1)]
        out.append(lax.ppermute(hi_face, axis, forward))
        out.append(lax.ppermute(lo_face, axis, backward))
    out.append(lax.all_to_all(w_buf, "wall", split_axis=0, concat_axis=0, tiled=True))
    return out


def local(sensitivity, diagonal, face_coef, upper_blocks, lower_blocks, iface_blocks, production,
          send_cell, target_cell, orient, iface_weight):
    n_span = lax.axis_size("span")
    n_var = sensitivity.shape[0]
    slots = send_cell.shape[-1]
    n_rows = n_span * slots
    shape = sensitivity.shape
    n_wall = lax.axis_size("wall")
    wall_me = lax.axis_index("wall").astype(jnp.int32).reshape(1)
    blk = (upper_blocks, lower_blocks, jnp.transpose(iface_blocks, (1, 0, 2)), wall_me)
    send_row = send_cell.reshape(n_span, slots)
    orient_row = orient.reshape(n_span, slots)
    weight_row = iface_weight.reshape(n_span, slots)
    target_row = target_cell.reshape(n_span, slots)

    vmem = pl.BlockSpec(memory_space=pltpu.VMEM)
    smem = pl.BlockSpec(memory_space=pltpu.SMEM)
    adj_sds = jax.ShapeDtypeStruct(shape, F32)
    tgt_sds = jax.ShapeDtypeStruct((1, n_rows), jnp.int32)
    lanes = shape[3]
    first_rows = jax.ShapeDtypeStruct((n_span, -(-(n_var + 1) * slots // lanes), lanes), F32)
    rows_sds = jax.ShapeDtypeStruct((n_span, -(-n_var * slots // lanes), lanes), F32)

    init = pl.pallas_call(
        init_kernel,
        out_shape=[adj_sds, first_rows] + face_shapes(shape, n_wall),
        in_specs=[smem] * 4 + [vmem] * 6,
        out_specs=[vmem] * 7,
    )
    adj, rows, *faces = init(*blk, sensitivity, diagonal, send_row, orient_row, weight_row, target_row)

    part_a = pl.pallas_call(
        make_part_a(slots),
        out_shape=adj_sds,
        in_specs=[smem] * 4 + [vmem] * 7,
        out_specs=vmem,
    )
    b_first = pl.pallas_call(
        make_part_b(True, False, slots),
        out_shape=[adj_sds, rows_sds] + face_shapes(shape, n_wall) + [tgt_sds],
        in_specs=[smem] * 3 + [vmem] * 9 + [smem],
        out_specs=[vmem] * 8,
    )
    b_step = pl.pallas_call(
        make_part_b(False, False, slots),
        out_shape=[adj_sds, rows_sds] + face_shapes(shape, n_wall),
        in_specs=[smem] * 3 + [vmem] * 10 + [smem],
        out_specs=[vmem] * 7,
    )
    b_last = pl.pallas_call(
        make_part_b(False, True, slots),
        out_shape=[adj_sds, jax.ShapeDtypeStruct(production.shape, F32)],
        in_specs=[smem] * 3 + [vmem] * 8,
        out_specs=[vmem] * 2,
    )
    ub, lb, ib, _ = blk
    received = None
    for sweep in range(SWEEPS):
        hcl, hch, hsl, hsh, w_inc = exchange(faces)
        incoming = lax.all_to_all(rows, "span", split_axis=0, concat_axis=0, tiled=True)
        partial = part_a(*blk, adj, sensitivity, diagonal, face_coef, hcl, hch, w_inc)
        common = (ub, lb, ib, partial, diagonal, face_coef, hsl, hsh, incoming)
        if sweep == 0:
            adj, rows, *faces, received = b_first(*common, send_row, orient_row, weight_row, wall_me)
        elif sweep < SWEEPS - 1:
            adj, rows, *faces = b_step(*common, received, send_row, orient_row, weight_row, wall_me)
        else:
            adj, gradient = b_last(*common, received, production)
    return (adj, gradient)


def solution(mesh):
    placed = (
        P(None, "chord", "span", "wall"),
        P(None, "chord", "span", "wall"),
        P(None, "chord", "span", "wall"),
        P(),
        P(),
        P(),
        P("chord", "span", "wall"),
        P("chord", "span", "wall", None, None),
        P("chord", "span", "wall", None, None),
        P("chord", "span", "wall", None, None),
        P("chord", "span", "wall", None, None),
    )
    return jax.shard_map(
        local,
        mesh=mesh,
        in_specs=placed,
        out_specs=(P(None, "chord", "span", "wall"), P("chord", "span", "wall")),
        check_vma=False,
    )
```

```python
import jax
import jax.numpy as jnp
from jax import lax
from jax.experimental import pallas as pl
from jax.experimental.pallas import tpu as pltpu
from jax.sharding import PartitionSpec as P

SWEEPS = 3
F32 = jnp.float32
BF16 = jnp.bfloat16


def split3(x):
    p1 = x.astype(BF16)
    p2 = (x - p1.astype(F32)).astype(BF16)
    return p1, p2


def gather_rows(adj, send_ref, orient_ref, weight_ref, blk, n_var, lanes):
    rows = adj.shape[1] * adj.shape[2]
    cell = flat_row(send_ref[...])
    n_rows = cell.shape[1]
    row_of = cell // lanes
    lane_of = cell % lanes
    lane_hot = (lax.broadcasted_iota(jnp.int32, (lanes, n_rows), 0) == lane_of).astype(BF16)
    row_hot = (lax.broadcasted_iota(jnp.int32, (rows, n_rows), 0) == row_of).astype(F32)
    flat = adj.reshape(n_var * rows, lanes)
    picked = jnp.dot(jnp.concatenate(split3(flat), axis=1),
                     jnp.concatenate([lane_hot] * 2, axis=0), preferred_element_type=F32)
    src = jnp.sum(picked.reshape(n_var, rows, n_rows) * row_hot[None], axis=1)
    orient = flat_row(orient_ref[...])
    weight = flat_row(weight_ref[...])
    out = []
    for i in range(n_var):
        first = None
        second = None
        for j in range(n_var):
            a = blk[2][j, 0, i] * src[j:j + 1]
            b = blk[2][j, 1, i] * src[j:j + 1]
            first = a if first is None else first + a
            second = b if second is None else second + b
        out.append(jnp.where(orient == 1, second, first) * weight)
    return out


def flat_row(x):
    return jnp.concatenate([x[t:t + 1] for t in range(x.shape[0])], axis=1)


def to_chunks(rows_ref, pieces, slots):
    n_dest, n_sub, lanes = rows_ref.shape
    pad = n_sub * lanes - len(pieces) * slots
    for t in range(n_dest):
        flat = [p[:, t * slots:(t + 1) * slots] for p in pieces]
        if pad:
            flat.append(jnp.zeros((1, pad), F32))
        flat = jnp.concatenate(flat, axis=1)
        rows_ref[t] = jnp.concatenate([flat[:, r * lanes:(r + 1) * lanes] for r in range(n_sub)], axis=0)


def from_chunks(inc, count, slots):
    n_src, _, lanes = inc.shape

    def piece(s, v):
        r, c = divmod(v * slots, lanes)
        return inc[s][r:r + 1, c:c + slots]
    return [jnp.concatenate([piece(s, v) for s in range(n_src)], axis=1) for v in range(count)]


def wall_columns(adj):
    n_var, nx, ny, nz = adj.shape
    lo, hi = [], []
    for v in range(n_var):
        t = adj[v].reshape(nx * ny, nz).T
        lo.append(t[0:1])
        hi.append(t[nz - 1:nz])
    return jnp.concatenate(lo, axis=0), jnp.concatenate(hi, axis=0)


def write_faces(adj, faces):
    c_lo, c_hi, s_lo, s_hi, w_buf, wall_me = faces
    nx, ny, nz = adj.shape[1], adj.shape[2], adj.shape[3]
    c_lo[...] = adj[:, 0:1]
    c_hi[...] = adj[:, nx - 1:nx]
    s_lo[...] = adj[:, :, 0, :]
    s_hi[...] = adj[:, :, ny - 1, :]
    lo, hi = wall_columns(adj)
    me = wall_me[0]
    n_wall = w_buf.shape[0]
    lo = jnp.concatenate([lo[v:v + 1] for v in range(lo.shape[0])], axis=1)
    hi = jnp.concatenate([hi[v:v + 1] for v in range(hi.shape[0])], axis=1)
    for t in range(n_wall):
        w_buf[t] = jnp.where(me + 1 == t, hi, jnp.where(me - 1 == t, lo, 0.0))


def wall_halos(w_inc, wall_me, n_var):
    me = wall_me[0]
    n_wall, _, width = w_inc.shape
    below = None
    above = None
    for t in range(n_wall):
        b = jnp.where(me - 1 == t, w_inc[t], 0.0)
        a = jnp.where(me + 1 == t, w_inc[t], 0.0)
        below = b if below is None else below + b
        above = a if above is None else above + a
    rows = width // n_var
    unflat = lambda x: jnp.concatenate([x[:, v * rows:(v + 1) * rows] for v in range(n_var)], axis=0)
    return unflat(below), unflat(above)


def init_kernel(ub_ref, lb_ref, ib_ref, wall_me, sens_ref, diag_ref, send_ref, orient_ref, weight_ref, tgt_ref,
                adj_ref, rows_ref, c_lo, c_hi, s_lo, s_hi, w_buf):
    n_var = sens_ref.shape[0]
    lanes = sens_ref.shape[3]
    slots = send_ref.shape[1]
    blk_ref = (ub_ref, lb_ref, ib_ref)
    adj = sens_ref[...] / diag_ref[...]
    adj_ref[...] = adj
    write_faces(adj, (c_lo, c_hi, s_lo, s_hi, w_buf, wall_me))
    pieces = gather_rows(adj, send_ref, orient_ref, weight_ref, blk_ref, n_var, lanes)
    to_chunks(rows_ref, pieces + [flat_row(tgt_ref[...]).astype(F32)], slots)


def scatter_rows(incoming, cell, shape):
    n_var, nx, ny, nz = shape
    rows = nx * ny
    n_rows = incoming.shape[1]
    row_of = cell // nz
    lane_of = cell % nz
    row_hot = (lax.broadcasted_iota(jnp.int32, (rows, n_rows), 0) == row_of).astype(BF16)
    lane_hot = (lax.broadcasted_iota(jnp.int32, (nz, n_rows), 0) == lane_of).astype(BF16)
    lhs = jnp.concatenate([(row_hot[None] * part[:, None, :]).reshape(n_var * rows, n_rows)
                           for part in split3(incoming)], axis=1)
    coupled = lax.dot_general(lhs, jnp.concatenate([lane_hot] * 2, axis=1), (((1,), (1,)), ((), ())),
                              preferred_element_type=F32)
    return coupled.reshape(n_var, nx, ny, nz)


def sweep_body(blk, adj, sens, diag, face, halos):
    n_var, nx, ny, nz = adj.shape
    rows = nx * ny
    h_c_lo, h_c_hi, h_s_lo, h_s_hi, h_w_lo, h_w_hi = halos
    j_idx = lax.broadcasted_iota(jnp.int32, adj.shape, 2)
    k_idx = lax.broadcasted_iota(jnp.int32, adj.shape, 3)
    kk = lax.broadcasted_iota(jnp.int32, (nz, rows), 0)
    wall = []
    for v in range(n_var):
        z = jnp.where(kk == 0, h_w_lo[v:v + 1], jnp.where(kk == nz - 1, h_w_hi[v:v + 1], 0.0))
        wall.append(z.T.reshape(nx, ny, nz))
    wall = jnp.stack(wall, axis=0)
    up = [
        jnp.concatenate([adj[:, 1:], h_c_hi], axis=1),
        jnp.where(j_idx == ny - 1, h_s_hi[:, :, None, :], pltpu.roll(adj, ny - 1, 2)),
        jnp.where(k_idx == nz - 1, wall, pltpu.roll(adj, nz - 1, 3)),
    ]
    lo = [
        jnp.concatenate([h_c_lo, adj[:, :-1]], axis=1),
        jnp.where(j_idx == 0, h_s_lo[:, :, None, :], pltpu.roll(adj, 1, 2)),
        jnp.where(k_idx == 0, wall, pltpu.roll(adj, 1, 3)),
    ]
    new = []
    for i in range(n_var):
        applied = diag[i] * adj[i]
        for d in range(3):
            acc = None
            for j in range(n_var):
                t = blk[0][d, j, i] * up[d][j] + blk[1][d, j, i] * lo[d][j]
                acc = t if acc is None else acc + t
            applied = applied + face[d] * acc
        new.append(adj[i] + (sens[i] - applied) / diag[i])
    return jnp.stack(new, axis=0)


def make_part_a(slots):
    def kernel(ub_ref, lb_ref, ib_ref, wall_me, adj_ref, sens_ref, diag_ref, face_ref, hcl, hch, w_inc, out_ref):
        n_var, nx, ny, nz = adj_ref.shape
        blk_ref = (ub_ref, lb_ref, ib_ref)
        none = jnp.zeros((n_var, nx, nz), F32)
        halos = (hcl[...], hch[...], none, none) + wall_halos(w_inc[...], wall_me, n_var)
        out_ref[...] = sweep_body(blk_ref, adj_ref[...], sens_ref[...], diag_ref[...], face_ref[...], halos)
    return kernel


def make_part_b(first, last, slots):
    def kernel(ub_ref, lb_ref, ib_ref, part_ref, diag_ref, face_ref, hsl, hsh, inc_ref, *rest):
        n_var, nx, ny, nz = part_ref.shape
        inc = inc_ref[...]
        if first:
            tgt_out, rest = rest[-1], rest[:-1]
            got = from_chunks(inc, n_var + 1, slots)
            cell = got[n_var].astype(jnp.int32)
            tgt_out[...] = cell
        else:
            tgt_ref, rest = rest[0], rest[1:]
            got = from_chunks(inc, n_var, slots)
            cell = tgt_ref[...]
        coupled = scatter_rows(jnp.concatenate(got[:n_var], axis=0), cell, part_ref.shape)
        part = part_ref[...]
        diag = diag_ref[...]
        face_y = face_ref[1]
        h_lo = hsl[...]
        h_hi = hsh[...]
        j_idx = lax.broadcasted_iota(jnp.int32, (nx, ny, nz), 1)
        new = []
        for i in range(n_var):
            above = None
            below = None
            for j in range(n_var):
                a = ub_ref[1, j, i] * h_hi[j]
                b = lb_ref[1, j, i] * h_lo[j]
                above = a if above is None else above + a
                below = b if below is None else below + b
            edge = (jnp.where(j_idx == ny - 1, above[:, None, :], 0.0)
                    + jnp.where(j_idx == 0, below[:, None, :], 0.0))
            new.append(part[i] - (face_y * edge + coupled[i]) / diag[i])
        new = jnp.stack(new, axis=0)
        if last:
            prod_ref, out_ref, grad_ref = rest
            out_ref[...] = new
            grad_ref[...] = prod_ref[...] * new[n_var - 1]
        else:
            send_ref, orient_ref, weight_ref, wall_me, out_ref, rows_ref, c_lo, c_hi, s_lo, s_hi, w_buf = rest
            out_ref[...] = new
            write_faces(new, (c_lo, c_hi, s_lo, s_hi, w_buf, wall_me))
            blk_ref = (ub_ref, lb_ref, ib_ref)
            to_chunks(rows_ref, gather_rows(new, send_ref, orient_ref, weight_ref, blk_ref, n_var, nz), slots)
    return kernel


def face_shapes(shape, n_wall):
    n_var, nx, ny, nz = shape
    c = jax.ShapeDtypeStruct((n_var, 1, ny, nz), F32)
    s = jax.ShapeDtypeStruct((n_var, nx, nz), F32)
    w = jax.ShapeDtypeStruct((n_wall, 1, n_var * nx * ny), F32)
    return [c, c, s, s, w]


def exchange(faces):
    c_lo, c_hi, s_lo, s_hi, w_buf = faces
    out = []
    for axis, lo_face, hi_face in (("chord", c_lo, c_hi), ("span", s_lo, s_hi)):
        count = lax.axis_size(axis)
        forward = [(i, i + 1) for i in range(count - 1)]
        backward = [(i + 1, i) for i in range(count - 1)]
        out.append(lax.ppermute(hi_face, axis, forward))
        out.append(lax.ppermute(lo_face, axis, backward))
    out.append(lax.all_to_all(w_buf, "wall", split_axis=0, concat_axis=0, tiled=True))
    return out


def local(sensitivity, diagonal, face_coef, upper_blocks, lower_blocks, iface_blocks, production,
          send_cell, target_cell, orient, iface_weight):
    n_span = lax.axis_size("span")
    n_var = sensitivity.shape[0]
    slots = send_cell.shape[-1]
    n_rows = n_span * slots
    shape = sensitivity.shape
    n_wall = lax.axis_size("wall")
    wall_me = lax.axis_index("wall").astype(jnp.int32).reshape(1)
    blk = (upper_blocks, lower_blocks, jnp.transpose(iface_blocks, (1, 0, 2)), wall_me)
    send_row = send_cell.reshape(n_span, slots)
    orient_row = orient.reshape(n_span, slots)
    weight_row = iface_weight.reshape(n_span, slots)
    target_row = target_cell.reshape(n_span, slots)

    vmem = pl.BlockSpec(memory_space=pltpu.VMEM)
    smem = pl.BlockSpec(memory_space=pltpu.SMEM)
    adj_sds = jax.ShapeDtypeStruct(shape, F32)
    tgt_sds = jax.ShapeDtypeStruct((1, n_rows), jnp.int32)
    lanes = shape[3]
    first_rows = jax.ShapeDtypeStruct((n_span, -(-(n_var + 1) * slots // lanes), lanes), F32)
    rows_sds = jax.ShapeDtypeStruct((n_span, -(-n_var * slots // lanes), lanes), F32)

    init = pl.pallas_call(
        init_kernel,
        out_shape=[adj_sds, first_rows] + face_shapes(shape, n_wall),
        in_specs=[smem] * 4 + [vmem] * 6,
        out_specs=[vmem] * 7,
    )
    adj, rows, *faces = init(*blk, sensitivity, diagonal, send_row, orient_row, weight_row, target_row)

    part_a = pl.pallas_call(
        make_part_a(slots),
        out_shape=adj_sds,
        in_specs=[smem] * 4 + [vmem] * 7,
        out_specs=vmem,
    )
    b_first = pl.pallas_call(
        make_part_b(True, False, slots),
        out_shape=[adj_sds, rows_sds] + face_shapes(shape, n_wall) + [tgt_sds],
        in_specs=[smem] * 3 + [vmem] * 9 + [smem],
        out_specs=[vmem] * 8,
    )
    b_step = pl.pallas_call(
        make_part_b(False, False, slots),
        out_shape=[adj_sds, rows_sds] + face_shapes(shape, n_wall),
        in_specs=[smem] * 3 + [vmem] * 10 + [smem],
        out_specs=[vmem] * 7,
    )
    b_last = pl.pallas_call(
        make_part_b(False, True, slots),
        out_shape=[adj_sds, jax.ShapeDtypeStruct(production.shape, F32)],
        in_specs=[smem] * 3 + [vmem] * 8,
        out_specs=[vmem] * 2,
    )
    ub, lb, ib, _ = blk
    received = None
    for sweep in range(SWEEPS):
        hcl, hch, hsl, hsh, w_inc = exchange(faces)
        incoming = lax.all_to_all(rows, "span", split_axis=0, concat_axis=0, tiled=True)
        partial = part_a(*blk, adj, sensitivity, diagonal, face_coef, hcl, hch, w_inc)
        common = (ub, lb, ib, partial, diagonal, face_coef, hsl, hsh, incoming)
        if sweep == 0:
            adj, rows, *faces, received = b_first(*common, send_row, orient_row, weight_row, wall_me)
        elif sweep < SWEEPS - 1:
            adj, rows, *faces = b_step(*common, received, send_row, orient_row, weight_row, wall_me)
        else:
            adj, gradient = b_last(*common, received, production)
    return (adj, gradient)


def solution(mesh):
    placed = (
        P(None, "chord", "span", "wall"),
        P(None, "chord", "span", "wall"),
        P(None, "chord", "span", "wall"),
        P(),
        P(),
        P(),
        P("chord", "span", "wall"),
        P("chord", "span", "wall", None, None),
        P("chord", "span", "wall", None, None),
        P("chord", "span", "wall", None, None),
        P("chord", "span", "wall", None, None),
    )
    return jax.shard_map(
        local,
        mesh=mesh,
        in_specs=placed,
        out_specs=(P(None, "chord", "span", "wall"), P("chord", "span", "wall")),
        check_vma=False,
    )
```
